32 devices in a mesh: seq: 8 (over y, x, core), tp: 4 (over z).
Axes of the slice: x: 2, y: 2, z: 4, core: 2. Of those that a mesh axis runs over, the one named last changes fastest.
Arguments:
- hidden: bfloat16 [4096, 2560], P('seq', 'tp'), may hold values from -6 to 6
- norm_gain: float32 [2560], replicated, may hold values from 0.25 to 1.75
- query_weight: float32 [2560, 4096], P('seq', 'tp'), may hold values from -0.125 to 0.125
- key_weight: float32 [2560, 1024], P('seq', 'tp'), may hold values from -0.125 to 0.125
- value_weight: float32 [2560, 1024], P('seq', 'tp'), may hold values from -0.125 to 0.125
- query_gain: float32 [128], replicated, may hold values from 0.5 to 8
- key_gain: float32 [128], replicated, may hold values from 0.5 to 8
- lengths: int32 [8], replicated, may hold values from 1 to 2048, 4096 in all
- page_table: int32 [32], replicated, may hold values from 0 to 31, each once
Outputs:
- attention: bfloat16 [4096, 4096], P('seq', 'tp')
- key_cache: bfloat16 [32, 8, 128, 128], P('seq', 'tp')
- value_cache: bfloat16 [32, 8, 128, 128], P('seq', 'tp')
The draws below stay inside these ranges and needn't reach their ends.
Inputs may be any that keep to these rules, and one draw needn't show every extreme that they name: 8 positive lengths summing to 4096; the longest is exactly 2048. `page_table`: every page is named by exactly one block.
All inputs are finite; a program needn't handle non-finite values.
Results may differ from the reference program's by a relative error of at most 0.0085.
The reference program's roundings to bfloat16 on the way count: a program that leaves them out, or rounds other values in their place, can miss the bound.
Values may be sent and summed in bfloat16 or wider, within the bound.
No kernel may reach another device: no remote copies, remote signals or barrier semaphores. Data moves between devices by JAX's collectives and lax.ppermute only.
A program may use at most 128 MiB of HBM per device.

```python
import math
import jax
import jax.numpy as jnp
import numpy as np
from jax import lax

D = 2560
QH = 32
KVH = 8
HD = 128
PAGE = 128
NSEG = 8
TOKENS = 4096
PAGES = 32
MOST = 2048


def gain_values(key):
    return jnp.exp(jax.random.uniform(key, (HD,), jnp.float32, math.log(0.5), math.log(2.0)))


def draw_query_gain(key, part):
    return gain_values(jax.random.fold_in(key, 11))


def draw_key_gain(key, part):
    return gain_values(jax.random.fold_in(key, 23))


def block_scale(rng, extent, pieces, smallest, top_value):
    level = 1.0
    for dim, blocks in pieces:
        heights = jax.random.uniform(jax.random.fold_in(jax.random.fold_in(rng, 6), dim), (blocks,), jnp.float32, smallest / len(pieces), top_value / len(pieces))
        level = level * jnp.repeat(jnp.exp(heights), extent[dim] // blocks).reshape((-1,) + (1,) * (len(extent) - 1 - dim))
    return level


def split_up(amount, total, most, slope):
    loads = [(1 << 20) // math.isqrt(standing ** slope) + 1 for standing in range(2, amount + 1)]
    surplus, counts = total - most - (amount - 1), [1] * (amount - 1)
    while surplus > 0:
        free = [i for i in range(amount - 1) if counts[i] < most]
        pool, left = sum([loads[i] for i in free]), surplus
        for i in free:
            extra = min(most - counts[i], max(1, left * loads[i] // pool), surplus)
            counts[i] = counts[i] + extra
            surplus = surplus - extra
    return np.array([most] + counts)


def ragged(own_key, number_of, total, most, slope):
    if number_of == 2:
        one = jax.random.randint(own_key, (), max(1, total - most), min(most, total - 1) + 1)
        return jnp.stack([one, total - one])
    sizes = jnp.asarray(split_up(number_of, total, most, slope), jnp.int32)
    pairs = (number_of - 1) // 2
    donor, taker = sizes[1:1 + 2 * pairs:2], sizes[2:2 + 2 * pairs:2]
    margin = jnp.minimum(donor - 1, most - taker)
    passed = jax.random.randint(jax.random.fold_in(own_key, 1), (pairs,), 0, 1 << 20) % (margin + 1)
    sizes = sizes.at[1:1 + 2 * pairs:2].set(donor - passed).at[2:2 + 2 * pairs:2].set(taker + passed)
    return sizes[jax.random.permutation(jax.random.fold_in(own_key, 2), number_of)]


def bell_draw(key, shape, scale, limit, cuts=(), kind=jnp.bfloat16):
    loudness = block_scale(key, shape, cuts, -0.22, 0.18) if cuts else 1.0
    drawn = jax.random.normal(key, shape, jnp.float32) * scale * loudness
    return jnp.minimum(jnp.maximum(drawn, -limit), limit).astype(kind)


def setup_inputs(seed: int = 0) -> dict:
    keys = jax.random.split(jax.random.key(seed), 10)
    hidden = bell_draw(keys[0], (TOKENS, D), 1.0, 6.0, ((0, 8), (1, 4)))
    norm_gain = jnp.clip(1.0 + 0.15 * jax.random.normal(keys[1], (D,), jnp.float32), 0.25, 1.75)
    query_weight = bell_draw(keys[2], (D, QH * HD), D ** -0.5, 0.125, ((0, 8), (1, 4)), jnp.float32)
    key_weight = bell_draw(keys[3], (D, KVH * HD), D ** -0.5, 0.125, ((0, 8), (1, 4)), jnp.float32)
    value_weight = bell_draw(keys[4], (D, KVH * HD), D ** -0.5, 0.125, ((0, 8), (1, 4)), jnp.float32)
    query_gain = draw_query_gain(jax.random.fold_in(keys[9], 71), 0)
    key_gain = draw_key_gain(jax.random.fold_in(keys[9], 71), 0)
    lengths = ragged(keys[7], NSEG, TOKENS, MOST, 2).astype(jnp.int32)
    page_table = jax.random.permutation(keys[8], PAGES).astype(jnp.int32)
    return {"hidden": hidden, "norm_gain": norm_gain, "query_weight": query_weight, "key_weight": key_weight, "value_weight": value_weight, "query_gain": query_gain, "key_gain": key_gain, "lengths": lengths, "page_table": page_table}


epsilon = 1e-06
excluded = -1e+30

def segment_of(slot_index, prompt_ends):
    return lax.optimization_barrier(jnp.sum((slot_index[..., None] >= prompt_ends).astype(jnp.int32), axis=-1))

def position_of(slot_index, prompt_ends, lengths):
    segment_id = segment_of(slot_index, prompt_ends)
    prompt_starts = prompt_ends - lengths
    labels = jnp.arange(lengths.shape[0], dtype=jnp.int32)
    picked = lax.optimization_barrier(jnp.sum(jnp.where(segment_id[..., None] == labels, prompt_starts, 0), axis=-1))
    return (segment_id, slot_index - picked)

def head_norm(vectors, gain):
    mean_sq = lax.optimization_barrier(jnp.mean(vectors * vectors, axis=-1, keepdims=True))
    return vectors * lax.rsqrt(mean_sq + epsilon) * gain

def rotate(vectors, position):
    head_dim = vectors.shape[-1]
    half_dim = head_dim // 2
    frequency = 1000000.0 ** (-(jnp.arange(half_dim, dtype=jnp.float32) * 2.0 / head_dim))
    angles = position.astype(jnp.float32)[:, None] * frequency[None, :]
    cosine = jnp.cos(angles)[:, None, :]
    sine_part = jnp.sin(angles)[:, None, :]
    front = vectors[..., :half_dim]
    back_half = vectors[..., half_dim:]
    return jnp.concatenate([front * cosine - back_half * sine_part, back_half * cosine + front * sine_part], axis=-1)

def reference(hidden, norm_gain, query_weight, key_weight, value_weight, query_gain, key_gain, lengths, page_table):
    widened = hidden.astype(jnp.float32)
    normed = (widened * lax.rsqrt(lax.optimization_barrier(jnp.mean(widened * widened, axis=-1, keepdims=True)) + epsilon) * norm_gain).astype(jnp.bfloat16)
    server_block = jnp.concatenate([query_weight, key_weight, value_weight], axis=1).astype(jnp.bfloat16)
    projected = jnp.dot(normed, server_block, preferred_element_type=jnp.float32)
    query_cols = QH * HD
    key_cols = KVH * HD
    slot_index = jnp.arange(TOKENS, dtype=jnp.int32)
    prompt_ends = jnp.cumsum(lengths).astype(jnp.int32)
    segment_id, position = position_of(slot_index, prompt_ends, lengths)
    queries = rotate(head_norm(projected[:, :query_cols].reshape(TOKENS, QH, HD), query_gain), position).astype(jnp.bfloat16)
    key_rows = rotate(head_norm(projected[:, query_cols:query_cols + key_cols].reshape(TOKENS, KVH, HD), key_gain), position).astype(jnp.bfloat16)
    values = projected[:, query_cols + key_cols:].reshape(TOKENS, KVH, HD).astype(jnp.bfloat16)
    group_size = QH // KVH
    row_block = math.gcd(TOKENS, 2048)
    block_count = TOKENS // row_block

    def one_block(index):
        head = index // block_count
        first = index % block_count * row_block
        query_block = lax.dynamic_slice_in_dim(queries[:, head, :], first, row_block, 0)
        row_slots = lax.dynamic_slice_in_dim(slot_index, first, row_block, 0)
        row_segments = lax.dynamic_slice_in_dim(segment_id, first, row_block, 0)
        key_block = key_rows[:, head // group_size, :]
        value_block = values[:, head // group_size, :]
        allowed = (segment_id[None, :] == row_segments[:, None]) & (slot_index[None, :] <= row_slots[:, None])
        scores = jnp.dot(query_block, key_block.T, preferred_element_type=jnp.float32) * HD ** (-0.5)
        running_max = lax.optimization_barrier(jnp.max(jnp.where(allowed, scores, excluded), axis=1, keepdims=True))
        weights = jnp.where(allowed, jnp.exp(scores - running_max), 0.0)
        summed = jnp.dot(weights.astype(jnp.bfloat16), value_block, preferred_element_type=jnp.float32)
        return summed / lax.optimization_barrier(jnp.sum(weights, axis=1, keepdims=True))
    blocks = lax.map(one_block, jnp.arange(QH * block_count, dtype=jnp.int32))
    heads = blocks.reshape(QH, TOKENS, HD)
    attention = heads.transpose(1, 0, 2).reshape(TOKENS, query_cols).astype(jnp.bfloat16)
    key_blocks = key_rows.reshape(PAGES, PAGE, KVH, HD).transpose(0, 2, 1, 3)
    value_blocks = values.reshape(PAGES, PAGE, KVH, HD).transpose(0, 2, 1, 3)
    key_cache = jnp.zeros_like(key_blocks).at[page_table].set(key_blocks)
    value_cache = jnp.zeros_like(value_blocks).at[page_table].set(value_blocks)
    return (attention, key_cache, value_cache)
```

```python
from functools import partial

import jax
import jax.numpy as jnp
from jax import lax
from jax.sharding import PartitionSpec as P

PAGE = 128


epsilon = 1e-06
excluded = -1e30


def segment_of(slot_index, prompt_ends):
    return jnp.sum((slot_index[..., None] >= prompt_ends).astype(jnp.int32), axis=-1)


def position_of(slot_index, prompt_ends, lengths):
    segment_id = segment_of(slot_index, prompt_ends)
    prompt_starts = prompt_ends - lengths
    labels = jnp.arange(lengths.shape[0], dtype=jnp.int32)
    picked = jnp.sum(jnp.where(segment_id[..., None] == labels, prompt_starts, 0), axis=-1)
    return (segment_id, slot_index - picked)


def head_norm(vectors, gain):
    mean_sq = jnp.mean(vectors * vectors, axis=-1, keepdims=True)
    return vectors * lax.rsqrt(mean_sq + epsilon) * gain


def rotate(vectors, position):
    head_dim = vectors.shape[-1]
    half_dim = head_dim // 2
    frequency = 1000000.0 ** (-(jnp.arange(half_dim, dtype=jnp.float32) * 2.0 / head_dim))
    angles = position.astype(jnp.float32)[:, None] * frequency[None, :]
    cosine = jnp.cos(angles)[:, None, :]
    sine_part = jnp.sin(angles)[:, None, :]
    front = vectors[..., :half_dim]
    back_half = vectors[..., half_dim:]
    return jnp.concatenate(
        [front * cosine - back_half * sine_part, back_half * cosine + front * sine_part], axis=-1
    )


def attend(
    query_block,
    query_slots,
    query_segments,
    key_piece,
    value_piece,
    key_slots,
    key_segments,
    kv_heads,
    group_size,
    head_dim,
    running,
):
    running_max, denominator, accumulator = running
    half_rows = query_block.shape[0]
    key_count = key_piece.shape[0]
    scores = jnp.einsum(
        "qkgd,nkd->kgqn",
        query_block.reshape(half_rows, kv_heads, group_size, head_dim),
        key_piece.reshape(key_count, kv_heads, head_dim),
        preferred_element_type=jnp.float32,
    ) * head_dim ** (-0.5)
    allowed = (key_segments[None, :] == query_segments[:, None]) & (
        key_slots[None, :] <= query_slots[:, None]
    )
    masked = jnp.where(allowed, scores, excluded)
    new_max = jnp.maximum(running_max, jnp.max(masked, axis=-1))
    weights = jnp.where(allowed, jnp.exp(scores - new_max[..., None]), 0.0)
    denominator = jnp.sum(weights, axis=-1)
    probs = weights.astype(jnp.bfloat16)
    accumulator = jnp.einsum(
        "kgqn,nkd->kgqd",
        probs,
        value_piece.reshape(key_count, kv_heads, head_dim),
        preferred_element_type=jnp.float32,
    )
    return (new_max, denominator, accumulator)


def keep_state(running):
    return running


def shards(
    hidden_parts,
    hidden,
    norm_gain,
    query_weight,
    key_weight,
    value_weight,
    query_gain,
    key_gain,
    lengths,
    page_table,
):
    row_count = hidden.shape[0]
    half_rows = row_count // 2
    head_dim = query_gain.shape[0]
    query_cols = query_weight.shape[1]
    key_cols = key_weight.shape[1]
    kv_heads = key_cols // head_dim
    group_size = query_cols // key_cols
    seq_rank = lax.axis_index("seq")
    prompt_ends = jnp.cumsum(lengths)
    tp_size = hidden_parts
    tp_rank = lax.axis_index("tp")
    pieces = [hidden]
    for shift in range(1, tp_size):
        pairs = [(i, (i + shift) % tp_size) for i in range(tp_size)]
        pieces.append(lax.ppermute(hidden, "tp", pairs))
    stacked = jnp.stack(pieces)
    order = (tp_rank - jnp.arange(tp_size, dtype=jnp.int32)) % tp_size
    gathered = jnp.take(stacked, order, axis=0).transpose(1, 0, 2).reshape(row_count, -1)
    widened = gathered.astype(jnp.float32)
    normed = (
        widened
        * lax.rsqrt(jnp.mean(widened * widened, axis=-1, keepdims=True) + epsilon)
        * norm_gain
    ).astype(jnp.bfloat16)
    server_block = jnp.concatenate([query_weight, key_weight, value_weight], axis=1).astype(
        jnp.bfloat16
    )
    projected = jnp.dot(
        normed,
        lax.all_gather(server_block, "seq", axis=0, tiled=True),
        preferred_element_type=jnp.float32,
    )
    slot_index = seq_rank * row_count + jnp.arange(row_count, dtype=jnp.int32)
    segment_id, position = position_of(slot_index, prompt_ends, lengths)
    queries = rotate(
        head_norm(
            projected[:, :query_cols].reshape(row_count, query_cols // head_dim, head_dim),
            query_gain,
        ),
        position,
    )
    queries = queries.reshape(row_count, query_cols).astype(jnp.bfloat16)
    key_rows = rotate(
        head_norm(
            projected[:, query_cols : query_cols + key_cols].reshape(row_count, kv_heads, head_dim),
            key_gain,
        ),
        position,
    )
    key_rows = key_rows.reshape(row_count, key_cols).astype(jnp.bfloat16)
    values = projected[:, query_cols + key_cols :].astype(jnp.bfloat16)
    shipped = queries[half_rows:]
    other_slots = slot_index[half_rows:]
    query_blocks = (queries[:half_rows], shipped)
    block_slots = (slot_index[:half_rows], other_slots)
    block_segments = (
        segment_of(block_slots[0], prompt_ends),
        segment_of(block_slots[1], prompt_ends),
    )
    pages_dev = row_count // PAGE
    owned_pages = seq_rank * pages_dev + jnp.arange(pages_dev, dtype=jnp.int32)
    page_count = page_table.shape[0]
    source_block = jnp.sum(
        jnp.where(
            page_table[None, :] == owned_pages[:, None],
            jnp.arange(page_count, dtype=jnp.int32)[None, :],
            0,
        ),
        axis=1,
    )

    def empty_state():
        return (
            jnp.full((kv_heads, group_size, half_rows), excluded, jnp.float32),
            jnp.zeros((kv_heads, group_size, half_rows), jnp.float32),
            jnp.zeros((kv_heads, group_size, half_rows, head_dim), jnp.float32),
        )

    empty_pages = jnp.zeros((pages_dev, PAGE, key_cols), jnp.bfloat16)
    initial = (empty_state(), empty_state(), empty_pages, empty_pages)
    first_row = jnp.int32(0)
    both_piece = lax.all_gather(jnp.concatenate([key_rows, values], axis=1), "seq", axis=0, tiled=True)
    key_piece = both_piece[:, :key_cols]
    value_piece = both_piece[:, key_cols:]
    key_count = key_piece.shape[0]
    key_slots = jnp.arange(key_count, dtype=jnp.int32)
    key_segments = segment_of(key_slots, prompt_ends)
    states = []
    for fold_half_number in range(2):
        query_slots = block_slots[fold_half_number]
        query_segments = block_segments[fold_half_number]
        last_query = query_slots[-1]
        clipped = jnp.minimum(first_row + key_count - 1, last_query)
        is_live = (first_row <= last_query) & (
            segment_of(clipped, prompt_ends) >= query_segments[0]
        )
        update = partial(
            attend,
            query_blocks[fold_half_number],
            query_slots,
            query_segments,
            key_piece,
            value_piece,
            key_slots,
            key_segments,
            kv_heads,
            group_size,
            head_dim,
        )
        states.append(lax.cond(is_live, update, keep_state, initial[fold_half_number]))
    blocks_in = key_count // PAGE
    block_number = jnp.arange(blocks_in, dtype=jnp.int32)
    matches = source_block[:, None] == block_number[None, :]
    selector = matches.astype(jnp.bfloat16)
    has_page = jnp.any(matches, axis=1)[:, None, None]
    new_keys = jnp.einsum(
        "pj,jtc->ptc",
        selector,
        key_piece.reshape(blocks_in, PAGE, key_cols),
        preferred_element_type=jnp.float32,
    ).astype(jnp.bfloat16)
    new_values = jnp.einsum(
        "pj,jtc->ptc",
        selector,
        value_piece.reshape(blocks_in, PAGE, key_cols),
        preferred_element_type=jnp.float32,
    ).astype(jnp.bfloat16)
    key_pages = jnp.where(has_page, new_keys, initial[2])
    value_pages = jnp.where(has_page, new_values, initial[3])
    result = (states[0], states[1], key_pages, value_pages)
    outputs = []
    for half_number in range(2):
        running_max, denominator, accumulator = result[half_number]
        result_block = accumulator / denominator[..., None]
        outputs.append(
            result_block.transpose(2, 0, 1, 3).reshape(half_rows, query_cols).astype(jnp.bfloat16)
        )
    returned = outputs[1]
    attention = jnp.concatenate([outputs[0], returned], axis=0)
    key_cache = result[2].reshape(pages_dev, PAGE, kv_heads, head_dim).transpose(0, 2, 1, 3)
    value_cache = result[3].reshape(pages_dev, PAGE, kv_heads, head_dim).transpose(0, 2, 1, 3)
    return (attention, key_cache, value_cache)


def solution(mesh):
    return jax.shard_map(
        partial(shards, mesh.shape["tp"]),
        mesh=mesh,
        in_specs=(
            P("seq", "tp"),
            P(),
            P("seq", "tp"),
            P("seq", "tp"),
            P("seq", "tp"),
            P(),
            P(),
            P(),
            P(),
        ),
        out_specs=(P("seq", "tp"), P("seq", "tp", None, None), P("seq", "tp", None, None)),
        check_vma=False,
    )
```

```python
from functools import partial

import jax
import jax.numpy as jnp
from jax import lax
from jax.sharding import PartitionSpec as P
from jax.experimental import pallas as pl
from jax.experimental.pallas import tpu as pltpu

PAGE = 128


epsilon = 1e-06
excluded = -1e30


def segment_of(slot_index, prompt_ends):
    return jnp.sum((slot_index[..., None] >= prompt_ends).astype(jnp.int32), axis=-1)


def position_of(slot_index, prompt_ends, lengths):
    segment_id = segment_of(slot_index, prompt_ends)
    prompt_starts = prompt_ends - lengths
    labels = jnp.arange(lengths.shape[0], dtype=jnp.int32)
    picked = jnp.sum(jnp.where(segment_id[..., None] == labels, prompt_starts, 0), axis=-1)
    return (segment_id, slot_index - picked)


def head_norm(vectors, gain):
    mean_sq = jnp.mean(vectors * vectors, axis=-1, keepdims=True)
    return vectors * lax.rsqrt(mean_sq + epsilon) * gain


def rotate(vectors, position):
    head_dim = vectors.shape[-1]
    half_dim = head_dim // 2
    frequency = 1000000.0 ** (-(jnp.arange(half_dim, dtype=jnp.float32) * 2.0 / head_dim))
    angles = position.astype(jnp.float32)[:, None] * frequency[None, :]
    cosine = jnp.cos(angles)[:, None, :]
    sine_part = jnp.sin(angles)[:, None, :]
    front = vectors[..., :half_dim]
    back_half = vectors[..., half_dim:]
    return jnp.concatenate(
        [front * cosine - back_half * sine_part, back_half * cosine + front * sine_part], axis=-1
    )


def attend(
    query_block,
    query_slots,
    query_segments,
    key_piece,
    value_piece,
    key_slots,
    key_segments,
    kv_heads,
    group_size,
    head_dim,
    running,
):
    running_max, denominator, accumulator = running
    half_rows = query_block.shape[0]
    key_count = key_piece.shape[0]
    scores = jnp.einsum(
        "qkgd,nkd->kgqn",
        query_block.reshape(half_rows, kv_heads, group_size, head_dim),
        key_piece.reshape(key_count, kv_heads, head_dim),
        preferred_element_type=jnp.float32,
    ) * head_dim ** (-0.5)
    allowed = (key_segments[None, :] == query_segments[:, None]) & (
        key_slots[None, :] <= query_slots[:, None]
    )
    masked = jnp.where(allowed, scores, excluded)
    new_max = jnp.maximum(running_max, jnp.max(masked, axis=-1))
    weights = jnp.where(allowed, jnp.exp(scores - new_max[..., None]), 0.0)
    denominator = jnp.sum(weights, axis=-1)
    probs = weights.astype(jnp.bfloat16)
    accumulator = jnp.einsum(
        "kgqn,nkd->kgqd",
        probs,
        value_piece.reshape(key_count, kv_heads, head_dim),
        preferred_element_type=jnp.float32,
    )
    return (new_max, denominator, accumulator)


def flash_kernel(group_size, block_q, block_k, head_dim, meta_ref, q_ref, k_ref, v_ref, rs_ref, o_ref, m_sc, l_sc, acc_sc):
    i = pl.program_id(1)
    r0 = meta_ref[3 * i]
    s_first = meta_ref[3 * i + 1]
    s_last = meta_ref[3 * i + 2]
    rows = group_size * block_q
    q = q_ref[...]
    qs = jnp.concatenate([q[:, g * head_dim : (g + 1) * head_dim] for g in range(group_size)], axis=0)
    rstart = jnp.concatenate([rs_ref[...]] * group_size, axis=0)
    row_slot = r0 + lax.broadcasted_iota(jnp.int32, (group_size, block_q, 1), 1).reshape(rows, 1)
    m_sc[...] = jnp.full(m_sc.shape, excluded, jnp.float32)
    l_sc[...] = jnp.zeros(l_sc.shape, jnp.float32)
    acc_sc[...] = jnp.zeros(acc_sc.shape, jnp.float32)
    scale = head_dim ** (-0.5)

    def update(kb, masked):
        first = pl.multiple_of(kb * block_k, block_k)
        k = k_ref[pl.ds(first, block_k), :]
        v = v_ref[pl.ds(first, block_k), :]
        s = lax.dot_general(qs, k, (((1,), (1,)), ((), ())), preferred_element_type=jnp.float32) * scale
        if masked:
            cols = first + lax.broadcasted_iota(jnp.int32, (rows, block_k), 1)
            allowed = (cols >= rstart) & (cols <= row_slot)
            s_max = jnp.max(jnp.where(allowed, s, excluded), axis=1, keepdims=True)
        else:
            s_max = jnp.max(s, axis=1, keepdims=True)
        m_prev = m_sc[...]
        m_next = jnp.maximum(m_prev, s_max)
        alpha = jnp.exp(m_prev - m_next)
        p = jnp.exp(s - m_next[:, :1])
        if masked:
            p = jnp.where(allowed, p, 0.0)
        l_sc[...] = alpha * l_sc[...] + jnp.sum(p, axis=1, keepdims=True)
        pv = jnp.dot(p.astype(jnp.bfloat16), v, preferred_element_type=jnp.float32)
        acc_sc[...] = acc_sc[...] * alpha + pv
        m_sc[...] = m_next

    def body(kb, carry):
        lo = kb * block_k
        full = (lo >= s_last) & (lo + block_k - 1 <= r0)

        @pl.when(full)
        def _():
            update(kb, False)

        @pl.when(jnp.logical_not(full))
        def _():
            update(kb, True)

        return carry

    lax.fori_loop(s_first // block_k, (r0 + block_q - 1) // block_k + 1, body, 0)
    res = acc_sc[...] / l_sc[...]
    o_ref[...] = jnp.concatenate(
        [res[g * block_q : (g + 1) * block_q] for g in range(group_size)], axis=1
    ).astype(o_ref.dtype)


def flash(meta, queries, both, row_start, kv_heads, group_size, head_dim, block_q, block_k):
    row_count = queries.shape[0]
    key_count = both.shape[0]
    n_qb = row_count // block_q
    rows = group_size * block_q
    kernel = partial(flash_kernel, group_size, block_q, block_k, head_dim)
    grid_spec = pltpu.PrefetchScalarGridSpec(
        num_scalar_prefetch=1,
        grid=(kv_heads, n_qb),
        in_specs=[
            pl.BlockSpec((block_q, group_size * head_dim), lambda h, i, meta: (i, h)),
            pl.BlockSpec((key_count, head_dim), lambda h, i, meta: (0, h)),
            pl.BlockSpec((key_count, head_dim), lambda h, i, meta: (0, kv_heads + h)),
            pl.BlockSpec((block_q, 1), lambda h, i, meta: (i, 0)),
        ],
        out_specs=pl.BlockSpec((block_q, group_size * head_dim), lambda h, i, meta: (i, h)),
        scratch_shapes=[
            pltpu.VMEM((rows, head_dim), jnp.float32),
            pltpu.VMEM((rows, head_dim), jnp.float32),
            pltpu.VMEM((rows, head_dim), jnp.float32),
        ],
    )
    flops = 4 * kv_heads * rows * n_qb * 1536 * head_dim
    return pl.pallas_call(
        kernel,
        grid_spec=grid_spec,
        out_shape=jax.ShapeDtypeStruct(queries.shape, queries.dtype),
        compiler_params=pltpu.CompilerParams(dimension_semantics=("arbitrary", "arbitrary")),
        cost_estimate=pl.CostEstimate(
            flops=flops, transcendentals=flops // (4 * head_dim), bytes_accessed=2 * queries.size * 2 + both.size * 2
        ),
    )(meta, queries, both, both, row_start)


def keep_state(running):
    return running


def shards(
    hidden_parts,
    hidden,
    norm_gain,
    query_weight,
    key_weight,
    value_weight,
    query_gain,
    key_gain,
    lengths,
    page_table,
):
    row_count = hidden.shape[0]
    half_rows = row_count // 2
    head_dim = query_gain.shape[0]
    query_cols = query_weight.shape[1]
    key_cols = key_weight.shape[1]
    kv_heads = key_cols // head_dim
    group_size = query_cols // key_cols
    seq_rank = lax.axis_index("seq")
    prompt_ends = jnp.cumsum(lengths)
    tp_size = hidden_parts
    tp_rank = lax.axis_index("tp")
    pieces = [hidden]
    for shift in range(1, tp_size):
        pairs = [(i, (i + shift) % tp_size) for i in range(tp_size)]
        pieces.append(lax.ppermute(hidden, "tp", pairs))
    stacked = jnp.stack(pieces)
    order = (tp_rank - jnp.arange(tp_size, dtype=jnp.int32)) % tp_size
    gathered = jnp.take(stacked, order, axis=0).transpose(1, 0, 2).reshape(row_count, -1)
    widened = gathered.astype(jnp.float32)
    normed = (
        widened
        * lax.rsqrt(jnp.mean(widened * widened, axis=-1, keepdims=True) + epsilon)
        * norm_gain
    ).astype(jnp.bfloat16)
    server_block = jnp.concatenate([query_weight, key_weight, value_weight], axis=1).astype(
        jnp.bfloat16
    )
    projected = jnp.dot(
        normed,
        lax.all_gather(server_block, "seq", axis=0, tiled=True),
        preferred_element_type=jnp.float32,
    )
    slot_index = seq_rank * row_count + jnp.arange(row_count, dtype=jnp.int32)
    segment_id, position = position_of(slot_index, prompt_ends, lengths)
    queries = rotate(
        head_norm(
            projected[:, :query_cols].reshape(row_count, query_cols // head_dim, head_dim),
            query_gain,
        ),
        position,
    )
    queries = queries.reshape(row_count, query_cols).astype(jnp.bfloat16)
    key_rows = rotate(
        head_norm(
            projected[:, query_cols : query_cols + key_cols].reshape(row_count, kv_heads, head_dim),
            key_gain,
        ),
        position,
    )
    key_rows = key_rows.reshape(row_count, key_cols).astype(jnp.bfloat16)
    values = projected[:, query_cols + key_cols :].astype(jnp.bfloat16)
    pages_dev = row_count // PAGE
    owned_pages = seq_rank * pages_dev + jnp.arange(pages_dev, dtype=jnp.int32)
    page_count = page_table.shape[0]
    source_block = jnp.sum(
        jnp.where(
            page_table[None, :] == owned_pages[:, None],
            jnp.arange(page_count, dtype=jnp.int32)[None, :],
            0,
        ),
        axis=1,
    )
    empty_pages = jnp.zeros((pages_dev, PAGE, key_cols), jnp.bfloat16)
    both_piece = lax.all_gather(jnp.concatenate([key_rows, values], axis=1), "seq", axis=0, tiled=True)
    key_piece = both_piece[:, :key_cols]
    value_piece = both_piece[:, key_cols:]
    key_count = key_piece.shape[0]
    block_q = 128
    block_k = 256
    row_start = slot_index - position
    firsts = row_start[::block_q]
    lasts = row_start[block_q - 1 :: block_q]
    meta = jnp.stack([slot_index[::block_q], firsts, lasts], axis=1).reshape(-1).astype(jnp.int32)
    attention = flash(
        meta, queries, both_piece, row_start.reshape(row_count, 1).astype(jnp.int32),
        kv_heads, group_size, head_dim, block_q, block_k,
    )
    blocks_in = key_count // PAGE
    block_number = jnp.arange(blocks_in, dtype=jnp.int32)
    matches = source_block[:, None] == block_number[None, :]
    selector = matches.astype(jnp.bfloat16)
    has_page = jnp.any(matches, axis=1)[:, None, None]
    new_keys = jnp.einsum(
        "pj,jtc->ptc",
        selector,
        key_piece.reshape(blocks_in, PAGE, key_cols),
        preferred_element_type=jnp.float32,
    ).astype(jnp.bfloat16)
    new_values = jnp.einsum(
        "pj,jtc->ptc",
        selector,
        value_piece.reshape(blocks_in, PAGE, key_cols),
        preferred_element_type=jnp.float32,
    ).astype(jnp.bfloat16)
    key_pages = jnp.where(has_page, new_keys, empty_pages)
    value_pages = jnp.where(has_page, new_values, empty_pages)
    result = (None, None, key_pages, value_pages)
    key_cache = result[2].reshape(pages_dev, PAGE, kv_heads, head_dim).transpose(0, 2, 1, 3)
    value_cache = result[3].reshape(pages_dev, PAGE, kv_heads, head_dim).transpose(0, 2, 1, 3)
    return (attention, key_cache, value_cache)


def solution(mesh):
    return jax.shard_map(
        partial(shards, mesh.shape["tp"]),
        mesh=mesh,
        in_specs=(
            P("seq", "tp"),
            P(),
            P("seq", "tp"),
            P("seq", "tp"),
            P("seq", "tp"),
            P(),
            P(),
            P(),
            P(),
        ),
        out_specs=(P("seq", "tp"), P("seq", "tp", None, None), P("seq", "tp", None, None)),
        check_vma=False,
    )
```

```python
from functools import partial

import jax
import jax.numpy as jnp
from jax import lax
from jax.sharding import Mesh, PartitionSpec as P
from jax.experimental import pallas as pl
from jax.experimental.pallas import tpu as pltpu

PAGE = 128


epsilon = 1e-06
excluded = -1e30


def segment_of(slot_index, prompt_ends):
    return jnp.sum((slot_index[..., None] >= prompt_ends).astype(jnp.int32), axis=-1)


def position_of(slot_index, prompt_ends, lengths):
    segment_id = segment_of(slot_index, prompt_ends)
    prompt_starts = prompt_ends - lengths
    labels = jnp.arange(lengths.shape[0], dtype=jnp.int32)
    picked = jnp.sum(jnp.where(segment_id[..., None] == labels, prompt_starts, 0), axis=-1)
    return (segment_id, slot_index - picked)


def head_norm(vectors, gain):
    mean_sq = jnp.mean(vectors * vectors, axis=-1, keepdims=True)
    return vectors * lax.rsqrt(mean_sq + epsilon) * gain


def rotate(vectors, position):
    head_dim = vectors.shape[-1]
    half_dim = head_dim // 2
    frequency = 1000000.0 ** (-(jnp.arange(half_dim, dtype=jnp.float32) * 2.0 / head_dim))
    angles = position.astype(jnp.float32)[:, None] * frequency[None, :]
    cosine = jnp.cos(angles)[:, None, :]
    sine_part = jnp.sin(angles)[:, None, :]
    front = vectors[..., :half_dim]
    back_half = vectors[..., half_dim:]
    return jnp.concatenate(
        [front * cosine - back_half * sine_part, back_half * cosine + front * sine_part], axis=-1
    )


def attend(
    query_block,
    query_slots,
    query_segments,
    key_piece,
    value_piece,
    key_slots,
    key_segments,
    kv_heads,
    group_size,
    head_dim,
    running,
):
    running_max, denominator, accumulator = running
    half_rows = query_block.shape[0]
    key_count = key_piece.shape[0]
    scores = jnp.einsum(
        "qkgd,nkd->kgqn",
        query_block.reshape(half_rows, kv_heads, group_size, head_dim),
        key_piece.reshape(key_count, kv_heads, head_dim),
        preferred_element_type=jnp.float32,
    ) * head_dim ** (-0.5)
    allowed = (key_segments[None, :] == query_segments[:, None]) & (
        key_slots[None, :] <= query_slots[:, None]
    )
    masked = jnp.where(allowed, scores, excluded)
    new_max = jnp.maximum(running_max, jnp.max(masked, axis=-1))
    weights = jnp.where(allowed, jnp.exp(scores - new_max[..., None]), 0.0)
    denominator = jnp.sum(weights, axis=-1)
    probs = weights.astype(jnp.bfloat16)
    accumulator = jnp.einsum(
        "kgqn,nkd->kgqd",
        probs,
        value_piece.reshape(key_count, kv_heads, head_dim),
        preferred_element_type=jnp.float32,
    )
    return (new_max, denominator, accumulator)


def flash_kernel(group_size, block_q, block_k, head_dim, chips, rank_rows, meta_ref, q_ref, k_ref, v_ref, rs_ref, o_ref, m_sc, l_sc, acc_sc):
    i = pl.program_id(1)
    r0 = meta_ref[3 * i]
    s_first = meta_ref[3 * i + 1]
    s_last = meta_ref[3 * i + 2]
    rows = group_size * block_q
    q = q_ref[...]
    qs = jnp.concatenate([q[:, g * head_dim : (g + 1) * head_dim] for g in range(group_size)], axis=0)
    rstart = jnp.concatenate([rs_ref[...]] * group_size, axis=0)
    row_slot = r0 + lax.broadcasted_iota(jnp.int32, (group_size, block_q, 1), 1).reshape(rows, 1)
    m_sc[...] = jnp.full(m_sc.shape, excluded, jnp.float32)
    l_sc[...] = jnp.zeros(l_sc.shape, jnp.float32)
    acc_sc[...] = jnp.zeros(acc_sc.shape, jnp.float32)
    scale = head_dim ** (-0.5)

    def update(kb, masked):
        first = kb * block_k
        rank = first // rank_rows
        stored = pl.multiple_of(((rank % 2) * chips + rank // 2) * rank_rows + first % rank_rows, block_k)
        k = k_ref[pl.ds(stored, block_k), :]
        v = v_ref[pl.ds(stored, block_k), :]
        s = lax.dot_general(qs, k, (((1,), (1,)), ((), ())), preferred_element_type=jnp.float32) * scale
        if masked:
            cols = first + lax.broadcasted_iota(jnp.int32, (rows, block_k), 1)
            allowed = (cols >= rstart) & (cols <= row_slot)
            s_max = jnp.max(jnp.where(allowed, s, excluded), axis=1, keepdims=True)
        else:
            s_max = jnp.max(s, axis=1, keepdims=True)
        m_prev = m_sc[...]
        m_next = jnp.maximum(m_prev, s_max)
        alpha = jnp.exp(m_prev - m_next)
        p = jnp.exp(s - m_next[:, :1])
        if masked:
            p = jnp.where(allowed, p, 0.0)
        l_sc[...] = alpha * l_sc[...] + jnp.sum(p, axis=1, keepdims=True)
        pv = jnp.dot(p.astype(jnp.bfloat16), v, preferred_element_type=jnp.float32)
        acc_sc[...] = acc_sc[...] * alpha + pv
        m_sc[...] = m_next

    def body(kb, carry):
        lo = kb * block_k
        full = (lo >= s_last) & (lo + block_k - 1 <= r0)

        @pl.when(full)
        def _():
            update(kb, False)

        @pl.when(jnp.logical_not(full))
        def _():
            update(kb, True)

        return carry

    lax.fori_loop(s_first // block_k, (r0 + block_q - 1) // block_k + 1, body, 0)
    res = acc_sc[...] / l_sc[...]
    o_ref[...] = jnp.concatenate(
        [res[g * block_q : (g + 1) * block_q] for g in range(group_size)], axis=1
    ).astype(o_ref.dtype)


def flash(meta, queries, both, row_start, kv_heads, group_size, head_dim, block_q, block_k, chips):
    row_count = queries.shape[0]
    key_count = both.shape[0]
    n_qb = row_count // block_q
    rows = group_size * block_q
    kernel = partial(flash_kernel, group_size, block_q, block_k, head_dim, chips, row_count)
    grid_spec = pltpu.PrefetchScalarGridSpec(
        num_scalar_prefetch=1,
        grid=(kv_heads, n_qb),
        in_specs=[
            pl.BlockSpec((block_q, group_size * head_dim), lambda h, i, meta: (i, h)),
            pl.BlockSpec((key_count, head_dim), lambda h, i, meta: (0, h)),
            pl.BlockSpec((key_count, head_dim), lambda h, i, meta: (0, kv_heads + h)),
            pl.BlockSpec((block_q, 1), lambda h, i, meta: (i, 0)),
        ],
        out_specs=pl.BlockSpec((block_q, group_size * head_dim), lambda h, i, meta: (i, h)),
        scratch_shapes=[
            pltpu.VMEM((rows, head_dim), jnp.float32),
            pltpu.VMEM((rows, head_dim), jnp.float32),
            pltpu.VMEM((rows, head_dim), jnp.float32),
        ],
    )
    flops = 4 * kv_heads * rows * n_qb * 1536 * head_dim
    return pl.pallas_call(
        kernel,
        grid_spec=grid_spec,
        out_shape=jax.ShapeDtypeStruct(queries.shape, queries.dtype),
        compiler_params=pltpu.CompilerParams(dimension_semantics=("arbitrary", "arbitrary")),
        cost_estimate=pl.CostEstimate(
            flops=flops, transcendentals=flops // (4 * head_dim), bytes_accessed=2 * queries.size * 2 + both.size * 2
        ),
    )(meta, queries, both, both, row_start)


def shards(
    chips,
    tp_size,
    hidden,
    norm_gain,
    query_weight,
    key_weight,
    value_weight,
    query_gain,
    key_gain,
    lengths,
    page_table,
):
    row_count = hidden.shape[0]
    head_dim = query_gain.shape[0]
    query_cols = query_weight.shape[1]
    key_cols = key_weight.shape[1]
    kv_heads = key_cols // head_dim
    group_size = query_cols // key_cols
    seq_rank = lax.axis_index("chip") * 2 + lax.axis_index("core")
    prompt_ends = jnp.cumsum(lengths)
    tp_rank = lax.axis_index("tp")
    pieces = [hidden]
    for shift in range(1, tp_size):
        pairs = [(i, (i + shift) % tp_size) for i in range(tp_size)]
        pieces.append(lax.ppermute(hidden, "tp", pairs))
    gathered = jnp.concatenate(
        [lax.select_n((tp_rank - u) % tp_size, *pieces) for u in range(tp_size)], axis=1
    )
    widened = gathered.astype(jnp.float32)
    normed = (
        widened
        * lax.rsqrt(jnp.mean(widened * widened, axis=-1, keepdims=True) + epsilon)
        * norm_gain
    ).astype(jnp.bfloat16)
    server_block = jnp.concatenate([query_weight, key_weight, value_weight], axis=1).astype(
        jnp.bfloat16
    )
    by_chip = lax.all_gather(server_block, "chip", axis=0, tiled=True)
    full_block = lax.all_gather(by_chip, "core", axis=0, tiled=True)
    weight_rows = server_block.shape[0]
    order = [2 * k + c for c in range(2) for k in range(chips)]
    normed_perm = normed.reshape(row_count, 2 * chips, weight_rows)[:, jnp.array(order), :].reshape(row_count, -1)
    projected_kv = jnp.dot(normed_perm, full_block[:, query_cols:], preferred_element_type=jnp.float32)
    slot_index = seq_rank * row_count + jnp.arange(row_count, dtype=jnp.int32)
    segment_id, position = position_of(slot_index, prompt_ends, lengths)
    key_rows = rotate(
        head_norm(projected_kv[:, :key_cols].reshape(row_count, kv_heads, head_dim), key_gain),
        position,
    )
    key_rows = key_rows.reshape(row_count, key_cols).astype(jnp.bfloat16)
    values = projected_kv[:, key_cols:].astype(jnp.bfloat16)
    local_kv = jnp.concatenate([key_rows, values], axis=1)
    both_piece = lax.all_gather(
        lax.all_gather(local_kv, "chip", axis=0, tiled=True), "core", axis=0, tiled=True
    )
    projected_q = jnp.dot(normed_perm, full_block[:, :query_cols], preferred_element_type=jnp.float32)
    queries = rotate(
        head_norm(projected_q.reshape(row_count, query_cols // head_dim, head_dim), query_gain),
        position,
    )
    queries = queries.reshape(row_count, query_cols).astype(jnp.bfloat16)
    block_q = 128
    block_k = 256
    row_start = slot_index - position
    firsts = row_start[::block_q]
    lasts = row_start[block_q - 1 :: block_q]
    meta = jnp.stack([slot_index[::block_q], firsts, lasts], axis=1).reshape(-1).astype(jnp.int32)
    attention = flash(
        meta, queries, both_piece, row_start.reshape(row_count, 1).astype(jnp.int32),
        kv_heads, group_size, head_dim, block_q, block_k, chips,
    )
    pages_dev = row_count // PAGE
    owned_pages = seq_rank * pages_dev + jnp.arange(pages_dev, dtype=jnp.int32)
    page_count = page_table.shape[0]
    source_block = jnp.sum(
        jnp.where(
            page_table[None, :] == owned_pages[:, None],
            jnp.arange(page_count, dtype=jnp.int32)[None, :],
            0,
        ),
        axis=1,
    )
    source_rank = source_block // pages_dev
    stored = ((source_rank % 2) * chips + source_rank // 2) * row_count + (source_block % pages_dev) * PAGE
    pages = jnp.stack([lax.dynamic_slice_in_dim(both_piece, stored[p], PAGE, 0) for p in range(pages_dev)])
    key_cache = pages[:, :, :key_cols].reshape(pages_dev, PAGE, kv_heads, head_dim).transpose(0, 2, 1, 3)
    value_cache = pages[:, :, key_cols:].reshape(pages_dev, PAGE, kv_heads, head_dim).transpose(0, 2, 1, 3)
    return (attention, key_cache, value_cache)


def solution(mesh):
    seq_size = mesh.shape["seq"]
    tp_size = mesh.shape["tp"]
    chips = seq_size // 2
    split = Mesh(mesh.devices.reshape(chips, 2, tp_size), ("chip", "core", "tp"))
    rows = ("chip", "core")
    return jax.shard_map(
        partial(shards, chips, tp_size),
        mesh=split,
        in_specs=(
            P(rows, "tp"),
            P(),
            P(rows, "tp"),
            P(rows, "tp"),
            P(rows, "tp"),
            P(),
            P(),
            P(),
            P(),
        ),
        out_specs=(P(rows, "tp"), P(rows, "tp", None, None), P(rows, "tp", None, None)),
        check_vma=False,
    )
```

```python
from functools import partial

import jax
import jax.numpy as jnp
from jax import lax
from jax.sharding import Mesh, PartitionSpec as P
from jax.experimental import pallas as pl
from jax.experimental.pallas import tpu as pltpu

PAGE = 128


epsilon = 1e-06
excluded = -1e30


def segment_of(slot_index, prompt_ends):
    return jnp.sum((slot_index[..., None] >= prompt_ends).astype(jnp.int32), axis=-1)


def position_of(slot_index, prompt_ends, lengths):
    segment_id = segment_of(slot_index, prompt_ends)
    prompt_starts = prompt_ends - lengths
    labels = jnp.arange(lengths.shape[0], dtype=jnp.int32)
    picked = jnp.sum(jnp.where(segment_id[..., None] == labels, prompt_starts, 0), axis=-1)
    return (segment_id, slot_index - picked)


def head_norm(vectors, gain):
    mean_sq = jnp.mean(vectors * vectors, axis=-1, keepdims=True)
    return vectors * lax.rsqrt(mean_sq + epsilon) * gain


def rotate(vectors, position):
    head_dim = vectors.shape[-1]
    half_dim = head_dim // 2
    frequency = 1000000.0 ** (-(jnp.arange(half_dim, dtype=jnp.float32) * 2.0 / head_dim))
    angles = position.astype(jnp.float32)[:, None] * frequency[None, :]
    cosine = jnp.cos(angles)[:, None, :]
    sine_part = jnp.sin(angles)[:, None, :]
    front = vectors[..., :half_dim]
    back_half = vectors[..., half_dim:]
    return jnp.concatenate(
        [front * cosine - back_half * sine_part, back_half * cosine + front * sine_part], axis=-1
    )


def attend(
    query_block,
    query_slots,
    query_segments,
    key_piece,
    value_piece,
    key_slots,
    key_segments,
    kv_heads,
    group_size,
    head_dim,
    running,
):
    running_max, denominator, accumulator = running
    half_rows = query_block.shape[0]
    key_count = key_piece.shape[0]
    scores = jnp.einsum(
        "qkgd,nkd->kgqn",
        query_block.reshape(half_rows, kv_heads, group_size, head_dim),
        key_piece.reshape(key_count, kv_heads, head_dim),
        preferred_element_type=jnp.float32,
    ) * head_dim ** (-0.5)
    allowed = (key_segments[None, :] == query_segments[:, None]) & (
        key_slots[None, :] <= query_slots[:, None]
    )
    masked = jnp.where(allowed, scores, excluded)
    new_max = jnp.maximum(running_max, jnp.max(masked, axis=-1))
    weights = jnp.where(allowed, jnp.exp(scores - new_max[..., None]), 0.0)
    denominator = jnp.sum(weights, axis=-1)
    probs = weights.astype(jnp.bfloat16)
    accumulator = jnp.einsum(
        "kgqn,nkd->kgqd",
        probs,
        value_piece.reshape(key_count, kv_heads, head_dim),
        preferred_element_type=jnp.float32,
    )
    return (new_max, denominator, accumulator)


def flash_kernel(group_size, block_q, block_k, head_dim, chips, rank_rows, meta_ref, q_ref, k_ref, v_ref, rs_ref, o_ref, m_sc, l_sc, acc_sc):
    i = pl.program_id(1)
    r0 = meta_ref[3 * i]
    s_first = meta_ref[3 * i + 1]
    s_last = meta_ref[3 * i + 2]
    rows = group_size * block_q
    q = q_ref[...]
    qs = jnp.concatenate([q[:, g * head_dim : (g + 1) * head_dim] for g in range(group_size)], axis=0)
    rstart = jnp.concatenate([rs_ref[...]] * group_size, axis=0)
    row_slot = r0 + lax.broadcasted_iota(jnp.int32, (group_size, block_q, 1), 1).reshape(rows, 1)
    m_sc[...] = jnp.full(m_sc.shape, excluded, jnp.float32)
    l_sc[...] = jnp.zeros(l_sc.shape, jnp.float32)
    acc_sc[...] = jnp.zeros(acc_sc.shape, jnp.float32)
    scale = head_dim ** (-0.5)

    def update(kb, masked):
        first = kb * block_k
        rank = first // rank_rows
        stored = pl.multiple_of(first, block_k)
        k = k_ref[pl.ds(stored, block_k), :]
        v = v_ref[pl.ds(stored, block_k), :]
        s = lax.dot_general(qs, k, (((1,), (1,)), ((), ())), preferred_element_type=jnp.float32) * scale
        if masked:
            cols = first + lax.broadcasted_iota(jnp.int32, (rows, block_k), 1)
            allowed = (cols >= rstart) & (cols <= row_slot)
            s_max = jnp.max(jnp.where(allowed, s, excluded), axis=1, keepdims=True)
        else:
            s_max = jnp.max(s, axis=1, keepdims=True)
        m_prev = m_sc[...]
        m_next = jnp.maximum(m_prev, s_max)
        alpha = jnp.exp(m_prev - m_next)
        p = jnp.exp(s - m_next[:, :1])
        if masked:
            p = jnp.where(allowed, p, 0.0)
        l_sc[...] = alpha * l_sc[...] + jnp.sum(p, axis=1, keepdims=True)
        pv = jnp.dot(p.astype(jnp.bfloat16), v, preferred_element_type=jnp.float32)
        acc_sc[...] = acc_sc[...] * alpha + pv
        m_sc[...] = m_next

    def body(kb, carry):
        lo = kb * block_k
        full = (lo >= s_last) & (lo + block_k - 1 <= r0)

        @pl.when(full)
        def _():
            update(kb, False)

        @pl.when(jnp.logical_not(full))
        def _():
            update(kb, True)

        return carry

    lax.fori_loop(s_first // block_k, (r0 + block_q - 1) // block_k + 1, body, 0)
    res = acc_sc[...] / l_sc[...]
    o_ref[...] = jnp.concatenate(
        [res[g * block_q : (g + 1) * block_q] for g in range(group_size)], axis=1
    ).astype(o_ref.dtype)


def flash(meta, queries, both, row_start, kv_heads, group_size, head_dim, block_q, block_k, chips):
    row_count = queries.shape[0]
    key_count = both.shape[0]
    n_qb = row_count // block_q
    rows = group_size * block_q
    kernel = partial(flash_kernel, group_size, block_q, block_k, head_dim, chips, row_count)
    grid_spec = pltpu.PrefetchScalarGridSpec(
        num_scalar_prefetch=1,
        grid=(kv_heads, n_qb),
        in_specs=[
            pl.BlockSpec((block_q, group_size * head_dim), lambda h, i, meta: (i, h)),
            pl.BlockSpec((key_count, head_dim), lambda h, i, meta: (0, h)),
            pl.BlockSpec((key_count, head_dim), lambda h, i, meta: (0, kv_heads + h)),
            pl.BlockSpec((block_q, 1), lambda h, i, meta: (i, 0)),
        ],
        out_specs=pl.BlockSpec((block_q, group_size * head_dim), lambda h, i, meta: (i, h)),
        scratch_shapes=[
            pltpu.VMEM((rows, head_dim), jnp.float32),
            pltpu.VMEM((rows, head_dim), jnp.float32),
            pltpu.VMEM((rows, head_dim), jnp.float32),
        ],
    )
    flops = 4 * kv_heads * rows * n_qb * 1536 * head_dim
    return pl.pallas_call(
        kernel,
        grid_spec=grid_spec,
        out_shape=jax.ShapeDtypeStruct(queries.shape, queries.dtype),
        compiler_params=pltpu.CompilerParams(dimension_semantics=("arbitrary", "arbitrary")),
        cost_estimate=pl.CostEstimate(
            flops=flops, transcendentals=flops // (4 * head_dim), bytes_accessed=2 * queries.size * 2 + both.size * 2
        ),
    )(meta, queries, both, both, row_start)


def shards(
    chips,
    tp_size,
    hidden,
    norm_gain,
    query_weight,
    key_weight,
    value_weight,
    query_gain,
    key_gain,
    lengths,
    page_table,
):
    row_count = hidden.shape[0]
    head_dim = query_gain.shape[0]
    query_cols = query_weight.shape[1]
    key_cols = key_weight.shape[1]
    kv_heads = key_cols // head_dim
    group_size = query_cols // key_cols
    seq_rank = lax.axis_index("seq")
    prompt_ends = jnp.cumsum(lengths)
    tp_rank = lax.axis_index("tp")
    pieces = [hidden]
    for shift in range(1, tp_size):
        pairs = [(i, (i + shift) % tp_size) for i in range(tp_size)]
        pieces.append(lax.ppermute(hidden, "tp", pairs))
    gathered = jnp.concatenate(
        [lax.select_n((tp_rank - u) % tp_size, *pieces) for u in range(tp_size)], axis=1
    )
    widened = gathered.astype(jnp.float32)
    normed = (
        widened
        * lax.rsqrt(jnp.mean(widened * widened, axis=-1, keepdims=True) + epsilon)
        * norm_gain
    ).astype(jnp.bfloat16)
    server_block = jnp.concatenate([query_weight, key_weight, value_weight], axis=1).astype(
        jnp.bfloat16
    )
    full_block = lax.all_gather(server_block, "seq", axis=0, tiled=True)
    normed_perm = normed
    projected_kv = jnp.dot(normed_perm, full_block[:, query_cols:], preferred_element_type=jnp.float32)
    slot_index = seq_rank * row_count + jnp.arange(row_count, dtype=jnp.int32)
    segment_id, position = position_of(slot_index, prompt_ends, lengths)
    key_rows = rotate(
        head_norm(projected_kv[:, :key_cols].reshape(row_count, kv_heads, head_dim), key_gain),
        position,
    )
    key_rows = key_rows.reshape(row_count, key_cols).astype(jnp.bfloat16)
    values = projected_kv[:, key_cols:].astype(jnp.bfloat16)
    local_kv = jnp.concatenate([key_rows, values], axis=1)
    both_piece = lax.all_gather(local_kv, "seq", axis=0, tiled=True)
    projected_q = jnp.dot(normed_perm, full_block[:, :query_cols], preferred_element_type=jnp.float32)
    queries = rotate(
        head_norm(projected_q.reshape(row_count, query_cols // head_dim, head_dim), query_gain),
        position,
    )
    queries = queries.reshape(row_count, query_cols).astype(jnp.bfloat16)
    block_q = 128
    block_k = 256
    row_start = slot_index - position
    firsts = row_start[::block_q]
    lasts = row_start[block_q - 1 :: block_q]
    meta = jnp.stack([slot_index[::block_q], firsts, lasts], axis=1).reshape(-1).astype(jnp.int32)
    attention = flash(
        meta, queries, both_piece, row_start.reshape(row_count, 1).astype(jnp.int32),
        kv_heads, group_size, head_dim, block_q, block_k, chips,
    )
    pages_dev = row_count // PAGE
    owned_pages = seq_rank * pages_dev + jnp.arange(pages_dev, dtype=jnp.int32)
    page_count = page_table.shape[0]
    source_block = jnp.sum(
        jnp.where(
            page_table[None, :] == owned_pages[:, None],
            jnp.arange(page_count, dtype=jnp.int32)[None, :],
            0,
        ),
        axis=1,
    )
    stored = source_block * PAGE
    pages = jnp.stack([lax.dynamic_slice_in_dim(both_piece, stored[p], PAGE, 0) for p in range(pages_dev)])
    key_cache = pages[:, :, :key_cols].reshape(pages_dev, PAGE, kv_heads, head_dim).transpose(0, 2, 1, 3)
    value_cache = pages[:, :, key_cols:].reshape(pages_dev, PAGE, kv_heads, head_dim).transpose(0, 2, 1, 3)
    return (attention, key_cache, value_cache)


def solution(mesh):
    seq_size = mesh.shape["seq"]
    tp_size = mesh.shape["tp"]
    chips = seq_size // 2
    return jax.shard_map(
        partial(shards, chips, tp_size),
        mesh=mesh,
        in_specs=(
            P("seq", "tp"),
            P(),
            P("seq", "tp"),
            P("seq", "tp"),
            P("seq", "tp"),
            P(),
            P(),
            P(),
            P(),
        ),
        out_specs=(P("seq", "tp"), P("seq", "tp", None, None), P("seq", "tp", None, None)),
        check_vma=False,
    )
```

```python
import math
from functools import partial

import jax
import jax.numpy as jnp
from jax import lax
from jax.sharding import Mesh, PartitionSpec as P
from jax.experimental import pallas as pl
from jax.experimental.pallas import tpu as pltpu

PAGE = 128


epsilon = 1e-06
excluded = -1e30


def segment_of(slot_index, prompt_ends):
    return jnp.sum((slot_index[..., None] >= prompt_ends).astype(jnp.int32), axis=-1)


def position_of(slot_index, prompt_ends, lengths):
    segment_id = segment_of(slot_index, prompt_ends)
    prompt_starts = prompt_ends - lengths
    labels = jnp.arange(lengths.shape[0], dtype=jnp.int32)
    picked = jnp.sum(jnp.where(segment_id[..., None] == labels, prompt_starts, 0), axis=-1)
    return (segment_id, slot_index - picked)


def head_norm(vectors, gain):
    mean_sq = jnp.mean(vectors * vectors, axis=-1, keepdims=True)
    return vectors * lax.rsqrt(mean_sq + epsilon) * gain


def rotate(vectors, position):
    head_dim = vectors.shape[-1]
    half_dim = head_dim // 2
    frequency = 1000000.0 ** (-(jnp.arange(half_dim, dtype=jnp.float32) * 2.0 / head_dim))
    angles = position.astype(jnp.float32)[:, None] * frequency[None, :]
    cosine = jnp.cos(angles)[:, None, :]
    sine_part = jnp.sin(angles)[:, None, :]
    front = vectors[..., :half_dim]
    back_half = vectors[..., half_dim:]
    return jnp.concatenate(
        [front * cosine - back_half * sine_part, back_half * cosine + front * sine_part], axis=-1
    )


def attend(
    query_block,
    query_slots,
    query_segments,
    key_piece,
    value_piece,
    key_slots,
    key_segments,
    kv_heads,
    group_size,
    head_dim,
    running,
):
    running_max, denominator, accumulator = running
    half_rows = query_block.shape[0]
    key_count = key_piece.shape[0]
    scores = jnp.einsum(
        "qkgd,nkd->kgqn",
        query_block.reshape(half_rows, kv_heads, group_size, head_dim),
        key_piece.reshape(key_count, kv_heads, head_dim),
        preferred_element_type=jnp.float32,
    ) * head_dim ** (-0.5)
    allowed = (key_segments[None, :] == query_segments[:, None]) & (
        key_slots[None, :] <= query_slots[:, None]
    )
    masked = jnp.where(allowed, scores, excluded)
    new_max = jnp.maximum(running_max, jnp.max(masked, axis=-1))
    weights = jnp.where(allowed, jnp.exp(scores - new_max[..., None]), 0.0)
    denominator = jnp.sum(weights, axis=-1)
    probs = weights.astype(jnp.bfloat16)
    accumulator = jnp.einsum(
        "kgqn,nkd->kgqd",
        probs,
        value_piece.reshape(key_count, kv_heads, head_dim),
        preferred_element_type=jnp.float32,
    )
    return (new_max, denominator, accumulator)


def flash_kernel(group_size, block_q, block_k, head_dim, chips, rank_rows, meta_ref, q_ref, k_ref, v_ref, rs_ref, o_ref, m_sc, l_sc, acc_sc):
    i = pl.program_id(1)
    r0 = meta_ref[3 * i]
    s_first = meta_ref[3 * i + 1]
    s_last = meta_ref[3 * i + 2]
    rows = group_size * block_q
    q = q_ref[...]
    qs = jnp.concatenate([q[:, g * head_dim : (g + 1) * head_dim] for g in range(group_size)], axis=0)
    rstart = jnp.concatenate([rs_ref[...]] * group_size, axis=0)
    row_slot = r0 + lax.broadcasted_iota(jnp.int32, (group_size, block_q, 1), 1).reshape(rows, 1)
    m_sc[...] = jnp.full(m_sc.shape, excluded, jnp.float32)
    l_sc[...] = jnp.zeros(l_sc.shape, jnp.float32)
    acc_sc[...] = jnp.zeros(acc_sc.shape, jnp.float32)
    scale = head_dim ** (-0.5) * math.log2(math.e)

    def update(kb, masked):
        first = kb * block_k
        rank = first // rank_rows
        stored = pl.multiple_of(first, block_k)
        k = k_ref[pl.ds(stored, block_k), :]
        v = v_ref[pl.ds(stored, block_k), :]
        s = lax.dot_general(qs, k, (((1,), (1,)), ((), ())), preferred_element_type=jnp.float32)
        if masked:
            cols = first + lax.broadcasted_iota(jnp.int32, (rows, block_k), 1)
            allowed = (cols >= rstart) & (cols <= row_slot)
            s_max = jnp.max(jnp.where(allowed, s, excluded), axis=1, keepdims=True)
        else:
            s_max = jnp.max(s, axis=1, keepdims=True)
        m_prev = m_sc[...]
        m_next = jnp.maximum(m_prev, s_max)
        alpha = jnp.exp2((m_prev - m_next) * scale)
        p = jnp.exp2((s - m_next[:, :1]) * scale)
        if masked:
            p = jnp.where(allowed, p, 0.0)
        l_sc[...] = alpha * l_sc[...] + jnp.sum(p, axis=1, keepdims=True)
        pv = jnp.dot(p.astype(jnp.bfloat16), v, preferred_element_type=jnp.float32)
        acc_sc[...] = acc_sc[...] * alpha + pv
        m_sc[...] = m_next

    def body(kb, carry):
        lo = kb * block_k
        full = (lo >= s_last) & (lo + block_k - 1 <= r0)

        @pl.when(full)
        def _():
            update(kb, False)

        @pl.when(jnp.logical_not(full))
        def _():
            update(kb, True)

        return carry

    lax.fori_loop(s_first // block_k, (r0 + block_q - 1) // block_k + 1, body, 0)
    res = acc_sc[...] / l_sc[...]
    o_ref[...] = jnp.concatenate(
        [res[g * block_q : (g + 1) * block_q] for g in range(group_size)], axis=1
    ).astype(o_ref.dtype)


def flash(meta, queries, both, row_start, kv_heads, group_size, head_dim, block_q, block_k, chips):
    row_count = queries.shape[0]
    key_count = both.shape[0]
    n_qb = row_count // block_q
    rows = group_size * block_q
    kernel = partial(flash_kernel, group_size, block_q, block_k, head_dim, chips, row_count)
    grid_spec = pltpu.PrefetchScalarGridSpec(
        num_scalar_prefetch=1,
        grid=(kv_heads, n_qb),
        in_specs=[
            pl.BlockSpec((block_q, group_size * head_dim), lambda h, i, meta: (i, h)),
            pl.BlockSpec((key_count, head_dim), lambda h, i, meta: (0, h)),
            pl.BlockSpec((key_count, head_dim), lambda h, i, meta: (0, kv_heads + h)),
            pl.BlockSpec((block_q, 1), lambda h, i, meta: (i, 0)),
        ],
        out_specs=pl.BlockSpec((block_q, group_size * head_dim), lambda h, i, meta: (i, h)),
        scratch_shapes=[
            pltpu.VMEM((rows, head_dim), jnp.float32),
            pltpu.VMEM((rows, head_dim), jnp.float32),
            pltpu.VMEM((rows, head_dim), jnp.float32),
        ],
    )
    flops = 4 * kv_heads * rows * n_qb * 1536 * head_dim
    return pl.pallas_call(
        kernel,
        grid_spec=grid_spec,
        out_shape=jax.ShapeDtypeStruct(queries.shape, queries.dtype),
        compiler_params=pltpu.CompilerParams(dimension_semantics=("arbitrary", "arbitrary")),
        cost_estimate=pl.CostEstimate(
            flops=flops, transcendentals=flops // (4 * head_dim), bytes_accessed=2 * queries.size * 2 + both.size * 2
        ),
    )(meta, queries, both, both, row_start)


def shards(
    chips,
    tp_size,
    hidden,
    norm_gain,
    query_weight,
    key_weight,
    value_weight,
    query_gain,
    key_gain,
    lengths,
    page_table,
):
    row_count = hidden.shape[0]
    head_dim = query_gain.shape[0]
    query_cols = query_weight.shape[1]
    key_cols = key_weight.shape[1]
    kv_heads = key_cols // head_dim
    group_size = query_cols // key_cols
    seq_rank = lax.axis_index("seq")
    prompt_ends = jnp.cumsum(lengths)
    tp_rank = lax.axis_index("tp")
    pieces = [hidden]
    for shift in range(1, tp_size):
        pairs = [(i, (i + shift) % tp_size) for i in range(tp_size)]
        pieces.append(lax.ppermute(hidden, "tp", pairs))
    gathered = jnp.concatenate(
        [lax.select_n((tp_rank - u) % tp_size, *pieces) for u in range(tp_size)], axis=1
    )
    widened = gathered.astype(jnp.float32)
    normed = (
        widened
        * lax.rsqrt(jnp.mean(widened * widened, axis=-1, keepdims=True) + epsilon)
        * norm_gain
    ).astype(jnp.bfloat16)
    server_block = jnp.concatenate([query_weight, key_weight, value_weight], axis=1).astype(
        jnp.bfloat16
    )
    full_block = lax.all_gather(server_block, "seq", axis=0, tiled=True)
    normed_perm = normed
    projected_kv = jnp.dot(normed_perm, full_block[:, query_cols:], preferred_element_type=jnp.float32)
    slot_index = seq_rank * row_count + jnp.arange(row_count, dtype=jnp.int32)
    segment_id, position = position_of(slot_index, prompt_ends, lengths)
    key_rows = rotate(
        head_norm(projected_kv[:, :key_cols].reshape(row_count, kv_heads, head_dim), key_gain),
        position,
    )
    key_rows = key_rows.reshape(row_count, key_cols).astype(jnp.bfloat16)
    values = projected_kv[:, key_cols:].astype(jnp.bfloat16)
    local_kv = jnp.concatenate([key_rows, values], axis=1)
    both_piece = lax.all_gather(local_kv, "seq", axis=0, tiled=True)
    projected_q = jnp.dot(normed_perm, full_block[:, :query_cols], preferred_element_type=jnp.float32)
    queries = rotate(
        head_norm(projected_q.reshape(row_count, query_cols // head_dim, head_dim), query_gain),
        position,
    )
    queries = queries.reshape(row_count, query_cols).astype(jnp.bfloat16)
    block_q = 128
    block_k = 512
    row_start = slot_index - position
    firsts = row_start[::block_q]
    lasts = row_start[block_q - 1 :: block_q]
    meta = jnp.stack([slot_index[::block_q], firsts, lasts], axis=1).reshape(-1).astype(jnp.int32)
    attention = flash(
        meta, queries, both_piece, row_start.reshape(row_count, 1).astype(jnp.int32),
        kv_heads, group_size, head_dim, block_q, block_k, chips,
    )
    pages_dev = row_count // PAGE
    owned_pages = seq_rank * pages_dev + jnp.arange(pages_dev, dtype=jnp.int32)
    page_count = page_table.shape[0]
    source_block = jnp.sum(
        jnp.where(
            page_table[None, :] == owned_pages[:, None],
            jnp.arange(page_count, dtype=jnp.int32)[None, :],
            0,
        ),
        axis=1,
    )
    stored = source_block * PAGE
    pages = jnp.stack([lax.dynamic_slice_in_dim(both_piece, stored[p], PAGE, 0) for p in range(pages_dev)])
    key_cache = pages[:, :, :key_cols].reshape(pages_dev, PAGE, kv_heads, head_dim).transpose(0, 2, 1, 3)
    value_cache = pages[:, :, key_cols:].reshape(pages_dev, PAGE, kv_heads, head_dim).transpose(0, 2, 1, 3)
    return (attention, key_cache, value_cache)


def solution(mesh):
    seq_size = mesh.shape["seq"]
    tp_size = mesh.shape["tp"]
    chips = seq_size // 2
    return jax.shard_map(
        partial(shards, chips, tp_size),
        mesh=mesh,
        in_specs=(
            P("seq", "tp"),
            P(),
            P("seq", "tp"),
            P("seq", "tp"),
            P("seq", "tp"),
            P(),
            P(),
            P(),
            P(),
        ),
        out_specs=(P("seq", "tp"), P("seq", "tp", None, None), P("seq", "tp", None, None)),
        check_vma=False,
    )
```

```python
import math
from functools import partial

import jax
import jax.numpy as jnp
from jax import lax
from jax.sharding import Mesh, PartitionSpec as P
from jax.experimental import pallas as pl
from jax.experimental.pallas import tpu as pltpu

PAGE = 128


epsilon = 1e-06
excluded = -1e30


def segment_of(slot_index, prompt_ends):
    return jnp.sum((slot_index[..., None] >= prompt_ends).astype(jnp.int32), axis=-1)


def position_of(slot_index, prompt_ends, lengths):
    segment_id = segment_of(slot_index, prompt_ends)
    prompt_starts = prompt_ends - lengths
    labels = jnp.arange(lengths.shape[0], dtype=jnp.int32)
    picked = jnp.sum(jnp.where(segment_id[..., None] == labels, prompt_starts, 0), axis=-1)
    return (segment_id, slot_index - picked)


def head_norm(vectors, gain):
    mean_sq = jnp.mean(vectors * vectors, axis=-1, keepdims=True)
    return vectors * lax.rsqrt(mean_sq + epsilon) * gain


def rotate(vectors, position):
    head_dim = vectors.shape[-1]
    half_dim = head_dim // 2
    frequency = 1000000.0 ** (-(jnp.arange(half_dim, dtype=jnp.float32) * 2.0 / head_dim))
    angles = position.astype(jnp.float32)[:, None] * frequency[None, :]
    cosine = jnp.cos(angles)[:, None, :]
    sine_part = jnp.sin(angles)[:, None, :]
    front = vectors[..., :half_dim]
    back_half = vectors[..., half_dim:]
    return jnp.concatenate(
        [front * cosine - back_half * sine_part, back_half * cosine + front * sine_part], axis=-1
    )


def attend(
    query_block,
    query_slots,
    query_segments,
    key_piece,
    value_piece,
    key_slots,
    key_segments,
    kv_heads,
    group_size,
    head_dim,
    running,
):
    running_max, denominator, accumulator = running
    half_rows = query_block.shape[0]
    key_count = key_piece.shape[0]
    scores = jnp.einsum(
        "qkgd,nkd->kgqn",
        query_block.reshape(half_rows, kv_heads, group_size, head_dim),
        key_piece.reshape(key_count, kv_heads, head_dim),
        preferred_element_type=jnp.float32,
    ) * head_dim ** (-0.5)
    allowed = (key_segments[None, :] == query_segments[:, None]) & (
        key_slots[None, :] <= query_slots[:, None]
    )
    masked = jnp.where(allowed, scores, excluded)
    new_max = jnp.maximum(running_max, jnp.max(masked, axis=-1))
    weights = jnp.where(allowed, jnp.exp(scores - new_max[..., None]), 0.0)
    denominator = jnp.sum(weights, axis=-1)
    probs = weights.astype(jnp.bfloat16)
    accumulator = jnp.einsum(
        "kgqn,nkd->kgqd",
        probs,
        value_piece.reshape(key_count, kv_heads, head_dim),
        preferred_element_type=jnp.float32,
    )
    return (new_max, denominator, accumulator)


def flash_kernel(group_size, block_q, block_k, head_dim, chips, rank_rows, meta_ref, q_ref, k_ref, v_ref, rs_ref, o_ref, m_sc, l_sc, acc_sc):
    i = pl.program_id(1)
    r0 = meta_ref[4 * i]
    s_first = meta_ref[4 * i + 1]
    s_last = meta_ref[4 * i + 2]
    origin = meta_ref[4 * i + 3]
    rows = group_size * block_q
    q = q_ref[...]
    qs = jnp.concatenate([q[:, g * head_dim : (g + 1) * head_dim] for g in range(group_size)], axis=0)
    rstart = jnp.concatenate([rs_ref[...]] * group_size, axis=0)
    row_slot = r0 + lax.broadcasted_iota(jnp.int32, (group_size, block_q, 1), 1).reshape(rows, 1)
    m_sc[...] = jnp.full(m_sc.shape, excluded, jnp.float32)
    l_sc[...] = jnp.zeros(l_sc.shape, jnp.float32)
    acc_sc[...] = jnp.zeros(acc_sc.shape, jnp.float32)
    scale = head_dim ** (-0.5) * math.log2(math.e)

    def update(kb, masked):
        first = kb * block_k
        stored = pl.multiple_of(first - origin, block_k)
        k = k_ref[pl.ds(stored, block_k), :]
        v = v_ref[pl.ds(stored, block_k), :]
        s = lax.dot_general(qs, k, (((1,), (1,)), ((), ())), preferred_element_type=jnp.float32)
        if masked:
            cols = first + lax.broadcasted_iota(jnp.int32, (rows, block_k), 1)
            allowed = (cols >= rstart) & (cols <= row_slot)
            s_max = jnp.max(jnp.where(allowed, s, excluded), axis=1, keepdims=True)
        else:
            s_max = jnp.max(s, axis=1, keepdims=True)
        m_prev = m_sc[...]
        m_next = jnp.maximum(m_prev, s_max)
        alpha = jnp.exp2((m_prev - m_next) * scale)
        p = jnp.exp2((s - m_next[:, :1]) * scale)
        if masked:
            p = jnp.where(allowed, p, 0.0)
        l_sc[...] = alpha * l_sc[...] + jnp.sum(p, axis=1, keepdims=True)
        pv = jnp.dot(p.astype(jnp.bfloat16), v, preferred_element_type=jnp.float32)
        acc_sc[...] = acc_sc[...] * alpha + pv
        m_sc[...] = m_next

    def body(kb, carry):
        lo = kb * block_k
        full = (lo >= s_last) & (lo + block_k - 1 <= r0)

        @pl.when(full)
        def _():
            update(kb, False)

        @pl.when(jnp.logical_not(full))
        def _():
            update(kb, True)

        return carry

    lax.fori_loop(s_first // block_k, (r0 + block_q - 1) // block_k + 1, body, 0)
    res = acc_sc[...] / l_sc[...]
    o_ref[...] = jnp.concatenate(
        [res[g * block_q : (g + 1) * block_q] for g in range(group_size)], axis=1
    ).astype(o_ref.dtype)


def flash(meta, queries, both, row_start, kv_heads, group_size, head_dim, block_q, block_k, chips):
    row_count = queries.shape[0]
    key_count = both.shape[0]
    n_qb = row_count // block_q
    rows = group_size * block_q
    kernel = partial(flash_kernel, group_size, block_q, block_k, head_dim, chips, row_count)
    grid_spec = pltpu.PrefetchScalarGridSpec(
        num_scalar_prefetch=1,
        grid=(kv_heads, n_qb),
        in_specs=[
            pl.BlockSpec((block_q, group_size * head_dim), lambda h, i, meta: (i, h)),
            pl.BlockSpec((key_count, head_dim), lambda h, i, meta: (0, h)),
            pl.BlockSpec((key_count, head_dim), lambda h, i, meta: (0, kv_heads + h)),
            pl.BlockSpec((block_q, 1), lambda h, i, meta: (i, 0)),
        ],
        out_specs=pl.BlockSpec((block_q, group_size * head_dim), lambda h, i, meta: (i, h)),
        scratch_shapes=[
            pltpu.VMEM((rows, head_dim), jnp.float32),
            pltpu.VMEM((rows, head_dim), jnp.float32),
            pltpu.VMEM((rows, head_dim), jnp.float32),
        ],
    )
    flops = 4 * kv_heads * rows * n_qb * 1536 * head_dim
    return pl.pallas_call(
        kernel,
        grid_spec=grid_spec,
        out_shape=jax.ShapeDtypeStruct(queries.shape, queries.dtype),
        compiler_params=pltpu.CompilerParams(dimension_semantics=("arbitrary", "arbitrary")),
        cost_estimate=pl.CostEstimate(
            flops=flops, transcendentals=flops // (4 * head_dim), bytes_accessed=2 * queries.size * 2 + both.size * 2
        ),
    )(meta, queries, both, both, row_start)


def shards(
    chips,
    tp_size,
    hidden,
    norm_gain,
    query_weight,
    key_weight,
    value_weight,
    query_gain,
    key_gain,
    lengths,
    page_table,
):
    row_count = hidden.shape[0]
    head_dim = query_gain.shape[0]
    query_cols = query_weight.shape[1]
    key_cols = key_weight.shape[1]
    kv_heads = key_cols // head_dim
    group_size = query_cols // key_cols
    seq_rank = lax.axis_index("seq")
    prompt_ends = jnp.cumsum(lengths)
    tp_rank = lax.axis_index("tp")
    pieces = [hidden]
    for shift in range(1, tp_size):
        pairs = [(i, (i + shift) % tp_size) for i in range(tp_size)]
        pieces.append(lax.ppermute(hidden, "tp", pairs))
    gathered = jnp.concatenate(
        [lax.select_n((tp_rank - u) % tp_size, *pieces) for u in range(tp_size)], axis=1
    )
    widened = gathered.astype(jnp.float32)
    normed = (
        widened
        * lax.rsqrt(jnp.mean(widened * widened, axis=-1, keepdims=True) + epsilon)
        * norm_gain
    ).astype(jnp.bfloat16)
    server_block = jnp.concatenate([query_weight, key_weight, value_weight], axis=1).astype(
        jnp.bfloat16
    )
    full_block = lax.all_gather(server_block, "seq", axis=0, tiled=True)
    normed_perm = normed
    projected_kv = jnp.dot(normed_perm, full_block[:, query_cols:], preferred_element_type=jnp.float32)
    slot_index = seq_rank * row_count + jnp.arange(row_count, dtype=jnp.int32)
    segment_id, position = position_of(slot_index, prompt_ends, lengths)
    key_rows = rotate(
        head_norm(projected_kv[:, :key_cols].reshape(row_count, kv_heads, head_dim), key_gain),
        position,
    )
    key_rows = key_rows.reshape(row_count, key_cols).astype(jnp.bfloat16)
    values = projected_kv[:, key_cols:].astype(jnp.bfloat16)
    local_kv = jnp.concatenate([key_rows, values], axis=1)
    seq_size = 2 * chips
    most = row_count * seq_size // 2
    back = min((most - 1 + row_count - 1) // row_count, seq_size - 1)
    received = [
        lax.ppermute(local_kv, "seq", [(i, i + shift) for i in range(seq_size - shift)])
        for shift in range(back, 0, -1)
    ]
    window = jnp.concatenate(received + [local_kv], axis=0)
    both_piece = lax.all_gather(local_kv, "seq", axis=0, tiled=True)
    projected_q = jnp.dot(normed_perm, full_block[:, :query_cols], preferred_element_type=jnp.float32)
    queries = rotate(
        head_norm(projected_q.reshape(row_count, query_cols // head_dim, head_dim), query_gain),
        position,
    )
    queries = queries.reshape(row_count, query_cols).astype(jnp.bfloat16)
    block_q = 128
    block_k = 512
    row_start = slot_index - position
    firsts = row_start[::block_q]
    lasts = row_start[block_q - 1 :: block_q]
    origins = jnp.full(firsts.shape, (seq_rank - back) * row_count, jnp.int32)
    meta = jnp.stack([slot_index[::block_q], firsts, lasts, origins], axis=1).reshape(-1).astype(jnp.int32)
    attention = flash(
        meta, queries, window, row_start.reshape(row_count, 1).astype(jnp.int32),
        kv_heads, group_size, head_dim, block_q, block_k, chips,
    )
    pages_dev = row_count // PAGE
    owned_pages = seq_rank * pages_dev + jnp.arange(pages_dev, dtype=jnp.int32)
    page_count = page_table.shape[0]
    source_block = jnp.sum(
        jnp.where(
            page_table[None, :] == owned_pages[:, None],
            jnp.arange(page_count, dtype=jnp.int32)[None, :],
            0,
        ),
        axis=1,
    )
    stored = source_block * PAGE
    pages = jnp.stack([lax.dynamic_slice_in_dim(both_piece, stored[p], PAGE, 0) for p in range(pages_dev)])
    key_cache = pages[:, :, :key_cols].reshape(pages_dev, PAGE, kv_heads, head_dim).transpose(0, 2, 1, 3)
    value_cache = pages[:, :, key_cols:].reshape(pages_dev, PAGE, kv_heads, head_dim).transpose(0, 2, 1, 3)
    return (attention, key_cache, value_cache)


def solution(mesh):
    seq_size = mesh.shape["seq"]
    tp_size = mesh.shape["tp"]
    chips = seq_size // 2
    return jax.shard_map(
        partial(shards, chips, tp_size),
        mesh=mesh,
        in_specs=(
            P("seq", "tp"),
            P(),
            P("seq", "tp"),
            P("seq", "tp"),
            P("seq", "tp"),
            P(),
            P(),
            P(),
            P(),
        ),
        out_specs=(P("seq", "tp"), P("seq", "tp", None, None), P("seq", "tp", None, None)),
        check_vma=False,
    )
```

```python
import math
from functools import partial

import jax
import jax.numpy as jnp
from jax import lax
from jax.sharding import Mesh, PartitionSpec as P
from jax.experimental import pallas as pl
from jax.experimental.pallas import tpu as pltpu

PAGE = 128


epsilon = 1e-06
excluded = -1e30


def segment_of(slot_index, prompt_ends):
    return jnp.sum((slot_index[..., None] >= prompt_ends).astype(jnp.int32), axis=-1)


def position_of(slot_index, prompt_ends, lengths):
    segment_id = segment_of(slot_index, prompt_ends)
    prompt_starts = prompt_ends - lengths
    labels = jnp.arange(lengths.shape[0], dtype=jnp.int32)
    picked = jnp.sum(jnp.where(segment_id[..., None] == labels, prompt_starts, 0), axis=-1)
    return (segment_id, slot_index - picked)


def head_norm(vectors, gain):
    mean_sq = jnp.mean(vectors * vectors, axis=-1, keepdims=True)
    return vectors * lax.rsqrt(mean_sq + epsilon) * gain


def rotate(vectors, position):
    head_dim = vectors.shape[-1]
    half_dim = head_dim // 2
    frequency = 1000000.0 ** (-(jnp.arange(half_dim, dtype=jnp.float32) * 2.0 / head_dim))
    angles = position.astype(jnp.float32)[:, None] * frequency[None, :]
    cosine = jnp.cos(angles)[:, None, :]
    sine_part = jnp.sin(angles)[:, None, :]
    front = vectors[..., :half_dim]
    back_half = vectors[..., half_dim:]
    return jnp.concatenate(
        [front * cosine - back_half * sine_part, back_half * cosine + front * sine_part], axis=-1
    )


def attend(
    query_block,
    query_slots,
    query_segments,
    key_piece,
    value_piece,
    key_slots,
    key_segments,
    kv_heads,
    group_size,
    head_dim,
    running,
):
    running_max, denominator, accumulator = running
    half_rows = query_block.shape[0]
    key_count = key_piece.shape[0]
    scores = jnp.einsum(
        "qkgd,nkd->kgqn",
        query_block.reshape(half_rows, kv_heads, group_size, head_dim),
        key_piece.reshape(key_count, kv_heads, head_dim),
        preferred_element_type=jnp.float32,
    ) * head_dim ** (-0.5)
    allowed = (key_segments[None, :] == query_segments[:, None]) & (
        key_slots[None, :] <= query_slots[:, None]
    )
    masked = jnp.where(allowed, scores, excluded)
    new_max = jnp.maximum(running_max, jnp.max(masked, axis=-1))
    weights = jnp.where(allowed, jnp.exp(scores - new_max[..., None]), 0.0)
    denominator = jnp.sum(weights, axis=-1)
    probs = weights.astype(jnp.bfloat16)
    accumulator = jnp.einsum(
        "kgqn,nkd->kgqd",
        probs,
        value_piece.reshape(key_count, kv_heads, head_dim),
        preferred_element_type=jnp.float32,
    )
    return (new_max, denominator, accumulator)


def flash_kernel(group_size, block_q, block_k, head_dim, chips, rank_rows, meta_ref, where_ref, q_ref, k_ref, v_ref, rs_ref, o_ref, m_sc, l_sc, acc_sc):
    i = pl.program_id(1)
    r0 = meta_ref[3 * i]
    s_first = meta_ref[3 * i + 1]
    s_last = meta_ref[3 * i + 2]
    rows = group_size * block_q
    q = q_ref[...]
    qs = jnp.concatenate([q[:, g * head_dim : (g + 1) * head_dim] for g in range(group_size)], axis=0)
    rstart = jnp.concatenate([rs_ref[...]] * group_size, axis=0)
    row_slot = r0 + lax.broadcasted_iota(jnp.int32, (group_size, block_q, 1), 1).reshape(rows, 1)
    m_sc[...] = jnp.full(m_sc.shape, excluded, jnp.float32)
    l_sc[...] = jnp.zeros(l_sc.shape, jnp.float32)
    acc_sc[...] = jnp.zeros(acc_sc.shape, jnp.float32)
    scale = head_dim ** (-0.5) * math.log2(math.e)

    def update(kb, masked):
        first = kb * block_k
        stored = pl.multiple_of(where_ref[first // rank_rows] * rank_rows + first % rank_rows, block_k)
        k = k_ref[pl.ds(stored, block_k), :]
        v = v_ref[pl.ds(stored, block_k), :]
        s = lax.dot_general(qs, k, (((1,), (1,)), ((), ())), preferred_element_type=jnp.float32)
        if masked:
            cols = first + lax.broadcasted_iota(jnp.int32, (rows, block_k), 1)
            allowed = (cols >= rstart) & (cols <= row_slot)
            s_max = jnp.max(jnp.where(allowed, s, excluded), axis=1, keepdims=True)
        else:
            s_max = jnp.max(s, axis=1, keepdims=True)
        m_prev = m_sc[...]
        m_next = jnp.maximum(m_prev, s_max)
        alpha = jnp.exp2((m_prev - m_next) * scale)
        p = jnp.exp2((s - m_next[:, :1]) * scale)
        if masked:
            p = jnp.where(allowed, p, 0.0)
        l_sc[...] = alpha * l_sc[...] + jnp.sum(p, axis=1, keepdims=True)
        pv = jnp.dot(p.astype(jnp.bfloat16), v, preferred_element_type=jnp.float32)
        acc_sc[...] = acc_sc[...] * alpha + pv
        m_sc[...] = m_next

    def body(kb, carry):
        lo = kb * block_k
        full = (lo >= s_last) & (lo + block_k - 1 <= r0)

        @pl.when(full)
        def _():
            update(kb, False)

        @pl.when(jnp.logical_not(full))
        def _():
            update(kb, True)

        return carry

    lax.fori_loop(s_first // block_k, (r0 + block_q - 1) // block_k + 1, body, 0)
    res = acc_sc[...] / l_sc[...]
    o_ref[...] = jnp.concatenate(
        [res[g * block_q : (g + 1) * block_q] for g in range(group_size)], axis=1
    ).astype(o_ref.dtype)


def flash(meta, where, queries, both, row_start, kv_heads, group_size, head_dim, block_q, block_k, chips):
    row_count = queries.shape[0]
    key_count = both.shape[0]
    n_qb = row_count // block_q
    rows = group_size * block_q
    kernel = partial(flash_kernel, group_size, block_q, block_k, head_dim, chips, row_count)
    grid_spec = pltpu.PrefetchScalarGridSpec(
        num_scalar_prefetch=2,
        grid=(kv_heads, n_qb),
        in_specs=[
            pl.BlockSpec((block_q, group_size * head_dim), lambda h, i, meta, where: (i, h)),
            pl.BlockSpec((key_count, head_dim), lambda h, i, meta, where: (0, h)),
            pl.BlockSpec((key_count, head_dim), lambda h, i, meta, where: (0, kv_heads + h)),
            pl.BlockSpec((block_q, 1), lambda h, i, meta, where: (i, 0)),
        ],
        out_specs=pl.BlockSpec((block_q, group_size * head_dim), lambda h, i, meta, where: (i, h)),
        scratch_shapes=[
            pltpu.VMEM((rows, head_dim), jnp.float32),
            pltpu.VMEM((rows, head_dim), jnp.float32),
            pltpu.VMEM((rows, head_dim), jnp.float32),
        ],
    )
    flops = 4 * kv_heads * rows * n_qb * 1536 * head_dim
    return pl.pallas_call(
        kernel,
        grid_spec=grid_spec,
        out_shape=jax.ShapeDtypeStruct(queries.shape, queries.dtype),
        compiler_params=pltpu.CompilerParams(dimension_semantics=("arbitrary", "arbitrary")),
        cost_estimate=pl.CostEstimate(
            flops=flops, transcendentals=flops // (4 * head_dim), bytes_accessed=2 * queries.size * 2 + both.size * 2
        ),
    )(meta, where, queries, both, both, row_start)


def gather_rows(x, chips):
    seq_size = 2 * chips
    me = lax.axis_index("seq")
    if chips != 4:
        return lax.all_gather(x, "seq", axis=0, tiled=True), jnp.arange(seq_size, dtype=jnp.int32)

    def swap(value, bit):
        return lax.ppermute(value, "seq", [(i, i ^ bit) for i in range(seq_size)])

    from_partner = swap(x, 1)
    from_x = swap(x, 2)
    from_y = swap(x, 4)
    forward = jnp.where(me % 2 == 0, from_y, from_x)
    from_diagonal = lax.ppermute(
        forward, "seq", [(i, i ^ 2) if i % 2 == 0 else (i, i ^ 4) for i in range(seq_size)]
    )
    by_mask = [
        x,
        from_partner,
        from_x,
        swap(from_x, 1),
        from_y,
        swap(from_y, 1),
        from_diagonal,
        swap(from_diagonal, 1),
    ]
    where = jnp.bitwise_xor(jnp.arange(seq_size, dtype=jnp.int32), me)
    return jnp.concatenate(by_mask, axis=0), where


def shards(
    chips,
    tp_size,
    hidden,
    norm_gain,
    query_weight,
    key_weight,
    value_weight,
    query_gain,
    key_gain,
    lengths,
    page_table,
):
    row_count = hidden.shape[0]
    head_dim = query_gain.shape[0]
    query_cols = query_weight.shape[1]
    key_cols = key_weight.shape[1]
    kv_heads = key_cols // head_dim
    group_size = query_cols // key_cols
    seq_rank = lax.axis_index("seq")
    prompt_ends = jnp.cumsum(lengths)
    tp_rank = lax.axis_index("tp")
    pieces = [hidden]
    for shift in range(1, tp_size):
        pairs = [(i, (i + shift) % tp_size) for i in range(tp_size)]
        pieces.append(lax.ppermute(hidden, "tp", pairs))
    gathered = jnp.concatenate(
        [lax.select_n((tp_rank - u) % tp_size, *pieces) for u in range(tp_size)], axis=1
    )
    widened = gathered.astype(jnp.float32)
    normed = (
        widened
        * lax.rsqrt(jnp.mean(widened * widened, axis=-1, keepdims=True) + epsilon)
        * norm_gain
    ).astype(jnp.bfloat16)
    server_block = jnp.concatenate([query_weight, key_weight, value_weight], axis=1).astype(
        jnp.bfloat16
    )
    full_block = lax.all_gather(server_block, "seq", axis=0, tiled=True)
    normed_perm = normed
    projected_kv = jnp.dot(normed_perm, full_block[:, query_cols:], preferred_element_type=jnp.float32)
    slot_index = seq_rank * row_count + jnp.arange(row_count, dtype=jnp.int32)
    segment_id, position = position_of(slot_index, prompt_ends, lengths)
    key_rows = rotate(
        head_norm(projected_kv[:, :key_cols].reshape(row_count, kv_heads, head_dim), key_gain),
        position,
    )
    key_rows = key_rows.reshape(row_count, key_cols).astype(jnp.bfloat16)
    values = projected_kv[:, key_cols:].astype(jnp.bfloat16)
    local_kv = jnp.concatenate([key_rows, values], axis=1)
    both_piece, where = gather_rows(local_kv, chips)
    projected_q = jnp.dot(normed_perm, full_block[:, :query_cols], preferred_element_type=jnp.float32)
    queries = rotate(
        head_norm(projected_q.reshape(row_count, query_cols // head_dim, head_dim), query_gain),
        position,
    )
    queries = queries.reshape(row_count, query_cols).astype(jnp.bfloat16)
    block_q = 128
    block_k = 512
    row_start = slot_index - position
    firsts = row_start[::block_q]
    lasts = row_start[block_q - 1 :: block_q]
    meta = jnp.stack([slot_index[::block_q], firsts, lasts], axis=1).reshape(-1).astype(jnp.int32)
    attention = flash(
        meta, where, queries, both_piece, row_start.reshape(row_count, 1).astype(jnp.int32),
        kv_heads, group_size, head_dim, block_q, block_k, chips,
    )
    pages_dev = row_count // PAGE
    owned_pages = seq_rank * pages_dev + jnp.arange(pages_dev, dtype=jnp.int32)
    page_count = page_table.shape[0]
    source_block = jnp.sum(
        jnp.where(
            page_table[None, :] == owned_pages[:, None],
            jnp.arange(page_count, dtype=jnp.int32)[None, :],
            0,
        ),
        axis=1,
    )
    stored = where[source_block // pages_dev] * row_count + (source_block % pages_dev) * PAGE
    pages = jnp.stack([lax.dynamic_slice_in_dim(both_piece, stored[p], PAGE, 0) for p in range(pages_dev)])
    key_cache = pages[:, :, :key_cols].reshape(pages_dev, PAGE, kv_heads, head_dim).transpose(0, 2, 1, 3)
    value_cache = pages[:, :, key_cols:].reshape(pages_dev, PAGE, kv_heads, head_dim).transpose(0, 2, 1, 3)
    return (attention, key_cache, value_cache)


def solution(mesh):
    seq_size = mesh.shape["seq"]
    tp_size = mesh.shape["tp"]
    chips = seq_size // 2
    return jax.shard_map(
        partial(shards, chips, tp_size),
        mesh=mesh,
        in_specs=(
            P("seq", "tp"),
            P(),
            P("seq", "tp"),
            P("seq", "tp"),
            P("seq", "tp"),
            P(),
            P(),
            P(),
            P(),
        ),
        out_specs=(P("seq", "tp"), P("seq", "tp", None, None), P("seq", "tp", None, None)),
        check_vma=False,
    )
```

```python
import math
from functools import partial

import jax
import jax.numpy as jnp
from jax import lax
from jax.sharding import Mesh, PartitionSpec as P
from jax.experimental import pallas as pl
from jax.experimental.pallas import tpu as pltpu

PAGE = 128


epsilon = 1e-06
excluded = -1e30


def segment_of(slot_index, prompt_ends):
    return jnp.sum((slot_index[..., None] >= prompt_ends).astype(jnp.int32), axis=-1)


def position_of(slot_index, prompt_ends, lengths):
    segment_id = segment_of(slot_index, prompt_ends)
    prompt_starts = prompt_ends - lengths
    labels = jnp.arange(lengths.shape[0], dtype=jnp.int32)
    picked = jnp.sum(jnp.where(segment_id[..., None] == labels, prompt_starts, 0), axis=-1)
    return (segment_id, slot_index - picked)


def head_norm(vectors, gain):
    mean_sq = jnp.mean(vectors * vectors, axis=-1, keepdims=True)
    return vectors * lax.rsqrt(mean_sq + epsilon) * gain


def rotate(vectors, position):
    head_dim = vectors.shape[-1]
    half_dim = head_dim // 2
    frequency = 1000000.0 ** (-(jnp.arange(half_dim, dtype=jnp.float32) * 2.0 / head_dim))
    angles = position.astype(jnp.float32)[:, None] * frequency[None, :]
    cosine = jnp.cos(angles)[:, None, :]
    sine_part = jnp.sin(angles)[:, None, :]
    front = vectors[..., :half_dim]
    back_half = vectors[..., half_dim:]
    return jnp.concatenate(
        [front * cosine - back_half * sine_part, back_half * cosine + front * sine_part], axis=-1
    )


def attend(
    query_block,
    query_slots,
    query_segments,
    key_piece,
    value_piece,
    key_slots,
    key_segments,
    kv_heads,
    group_size,
    head_dim,
    running,
):
    running_max, denominator, accumulator = running
    half_rows = query_block.shape[0]
    key_count = key_piece.shape[0]
    scores = jnp.einsum(
        "qkgd,nkd->kgqn",
        query_block.reshape(half_rows, kv_heads, group_size, head_dim),
        key_piece.reshape(key_count, kv_heads, head_dim),
        preferred_element_type=jnp.float32,
    ) * head_dim ** (-0.5)
    allowed = (key_segments[None, :] == query_segments[:, None]) & (
        key_slots[None, :] <= query_slots[:, None]
    )
    masked = jnp.where(allowed, scores, excluded)
    new_max = jnp.maximum(running_max, jnp.max(masked, axis=-1))
    weights = jnp.where(allowed, jnp.exp(scores - new_max[..., None]), 0.0)
    denominator = jnp.sum(weights, axis=-1)
    probs = weights.astype(jnp.bfloat16)
    accumulator = jnp.einsum(
        "kgqn,nkd->kgqd",
        probs,
        value_piece.reshape(key_count, kv_heads, head_dim),
        preferred_element_type=jnp.float32,
    )
    return (new_max, denominator, accumulator)


def flash_kernel(group_size, block_q, block_k, head_dim, chips, rank_rows, meta_ref, where_ref, q_ref, k_ref, v_ref, rs_ref, o_ref, m_sc, l_sc, acc_sc):
    i = pl.program_id(1)
    r0 = meta_ref[3 * i]
    s_first = meta_ref[3 * i + 1]
    s_last = meta_ref[3 * i + 2]
    rows = group_size * block_q
    q = q_ref[...]
    qs = jnp.concatenate([q[:, g * head_dim : (g + 1) * head_dim] for g in range(group_size)], axis=0)
    rstart = jnp.concatenate([rs_ref[...]] * group_size, axis=0)
    row_slot = r0 + lax.broadcasted_iota(jnp.int32, (group_size, block_q, 1), 1).reshape(rows, 1)
    m_sc[...] = jnp.full(m_sc.shape, excluded, jnp.float32)
    l_sc[...] = jnp.zeros(l_sc.shape, jnp.float32)
    acc_sc[...] = jnp.zeros(acc_sc.shape, jnp.float32)
    scale = head_dim ** (-0.5) * math.log2(math.e)

    def update(kb, masked):
        first = kb * block_k
        stored = pl.multiple_of(where_ref[first // rank_rows] * rank_rows + first % rank_rows, block_k)
        k = k_ref[pl.ds(stored, block_k), :]
        v = v_ref[pl.ds(stored, block_k), :]
        s = lax.dot_general(qs, k, (((1,), (1,)), ((), ())), preferred_element_type=jnp.float32)
        if masked:
            cols = first + lax.broadcasted_iota(jnp.int32, (rows, block_k), 1)
            allowed = (cols >= rstart) & (cols <= row_slot)
            s_max = jnp.max(jnp.where(allowed, s, excluded), axis=1, keepdims=True)
        else:
            s_max = jnp.max(s, axis=1, keepdims=True)
        m_prev = m_sc[...]
        m_next = jnp.maximum(m_prev, s_max)
        alpha = jnp.exp2((m_prev - m_next) * scale)
        p = jnp.exp2((s - m_next[:, :1]) * scale)
        if masked:
            p = jnp.where(allowed, p, 0.0)
        l_sc[...] = alpha * l_sc[...] + jnp.sum(p, axis=1, keepdims=True)
        pv = jnp.dot(p.astype(jnp.bfloat16), v, preferred_element_type=jnp.float32)
        acc_sc[...] = acc_sc[...] * alpha + pv
        m_sc[...] = m_next

    def body(kb, carry):
        lo = kb * block_k
        full = (lo >= s_last) & (lo + block_k - 1 <= r0)

        @pl.when(full)
        def _():
            update(kb, False)

        @pl.when(jnp.logical_not(full))
        def _():
            update(kb, True)

        return carry

    lax.fori_loop(s_first // block_k, (r0 + block_q - 1) // block_k + 1, body, 0)
    res = acc_sc[...] / l_sc[...]
    o_ref[...] = jnp.concatenate(
        [res[g * block_q : (g + 1) * block_q] for g in range(group_size)], axis=1
    ).astype(o_ref.dtype)


def flash(meta, where, queries, both, row_start, kv_heads, group_size, head_dim, block_q, block_k, chips):
    row_count = queries.shape[0]
    key_count = both.shape[0]
    n_qb = row_count // block_q
    rows = group_size * block_q
    kernel = partial(flash_kernel, group_size, block_q, block_k, head_dim, chips, row_count)
    grid_spec = pltpu.PrefetchScalarGridSpec(
        num_scalar_prefetch=2,
        grid=(kv_heads, n_qb),
        in_specs=[
            pl.BlockSpec((block_q, group_size * head_dim), lambda h, i, meta, where: (i, h)),
            pl.BlockSpec((key_count, head_dim), lambda h, i, meta, where: (0, h)),
            pl.BlockSpec((key_count, head_dim), lambda h, i, meta, where: (0, kv_heads + h)),
            pl.BlockSpec((block_q, 1), lambda h, i, meta, where: (i, 0)),
        ],
        out_specs=pl.BlockSpec((block_q, group_size * head_dim), lambda h, i, meta, where: (i, h)),
        scratch_shapes=[
            pltpu.VMEM((rows, head_dim), jnp.float32),
            pltpu.VMEM((rows, head_dim), jnp.float32),
            pltpu.VMEM((rows, head_dim), jnp.float32),
        ],
    )
    flops = 4 * kv_heads * rows * n_qb * 1536 * head_dim
    return pl.pallas_call(
        kernel,
        grid_spec=grid_spec,
        out_shape=jax.ShapeDtypeStruct(queries.shape, queries.dtype),
        compiler_params=pltpu.CompilerParams(dimension_semantics=("arbitrary", "arbitrary")),
        cost_estimate=pl.CostEstimate(
            flops=flops, transcendentals=flops // (4 * head_dim), bytes_accessed=2 * queries.size * 2 + both.size * 2
        ),
    )(meta, where, queries, both, both, row_start)


def gather_rows(x, chips):
    seq_size = 2 * chips
    me = lax.axis_index("seq")
    if chips != 4:
        return lax.all_gather(x, "seq", axis=0, tiled=True), jnp.arange(seq_size, dtype=jnp.int32)

    def swap(value, bit):
        return lax.ppermute(value, "seq", [(i, i ^ bit) for i in range(seq_size)])

    from_partner = swap(x, 1)
    from_x = swap(x, 2)
    from_y = swap(x, 4)
    forward = jnp.where(me % 2 == 0, from_y, from_x)
    from_diagonal = lax.ppermute(
        forward, "seq", [(i, i ^ 2) if i % 2 == 0 else (i, i ^ 4) for i in range(seq_size)]
    )
    by_mask = [
        x,
        from_partner,
        from_x,
        swap(from_x, 1),
        from_y,
        swap(from_y, 1),
        from_diagonal,
        swap(from_diagonal, 1),
    ]
    where = jnp.bitwise_xor(jnp.arange(seq_size, dtype=jnp.int32), me)
    return jnp.concatenate(by_mask, axis=0), where


def shards(
    chips,
    tp_size,
    hidden,
    norm_gain,
    query_weight,
    key_weight,
    value_weight,
    query_gain,
    key_gain,
    lengths,
    page_table,
):
    row_count = hidden.shape[0]
    head_dim = query_gain.shape[0]
    query_cols = query_weight.shape[1]
    key_cols = key_weight.shape[1]
    kv_heads = key_cols // head_dim
    group_size = query_cols // key_cols
    seq_rank = lax.axis_index("seq")
    prompt_ends = jnp.cumsum(lengths)
    tp_rank = lax.axis_index("tp")
    pieces = [hidden]
    for shift in range(1, tp_size):
        pairs = [(i, (i + shift) % tp_size) for i in range(tp_size)]
        pieces.append(lax.ppermute(hidden, "tp", pairs))
    gathered = jnp.concatenate(
        [lax.select_n((tp_rank - u) % tp_size, *pieces) for u in range(tp_size)], axis=1
    )
    widened = gathered.astype(jnp.float32)
    normed = (
        widened
        * lax.rsqrt(jnp.mean(widened * widened, axis=-1, keepdims=True) + epsilon)
        * norm_gain
    ).astype(jnp.bfloat16)
    kv_block = lax.all_gather(
        jnp.concatenate([key_weight, value_weight], axis=1).astype(jnp.bfloat16), "seq", axis=0, tiled=True
    )
    q_block = lax.all_gather(query_weight.astype(jnp.bfloat16), "seq", axis=0, tiled=True)
    normed_perm = normed
    projected_kv = jnp.dot(normed_perm, kv_block, preferred_element_type=jnp.float32)
    slot_index = seq_rank * row_count + jnp.arange(row_count, dtype=jnp.int32)
    segment_id, position = position_of(slot_index, prompt_ends, lengths)
    key_rows = rotate(
        head_norm(projected_kv[:, :key_cols].reshape(row_count, kv_heads, head_dim), key_gain),
        position,
    )
    key_rows = key_rows.reshape(row_count, key_cols).astype(jnp.bfloat16)
    values = projected_kv[:, key_cols:].astype(jnp.bfloat16)
    local_kv = jnp.concatenate([key_rows, values], axis=1)
    both_piece, where = gather_rows(local_kv, chips)
    projected_q = jnp.dot(normed_perm, q_block, preferred_element_type=jnp.float32)
    queries = rotate(
        head_norm(projected_q.reshape(row_count, query_cols // head_dim, head_dim), query_gain),
        position,
    )
    queries = queries.reshape(row_count, query_cols).astype(jnp.bfloat16)
    block_q = 128
    block_k = 512
    row_start = slot_index - position
    firsts = row_start[::block_q]
    lasts = row_start[block_q - 1 :: block_q]
    meta = jnp.stack([slot_index[::block_q], firsts, lasts], axis=1).reshape(-1).astype(jnp.int32)
    attention = flash(
        meta, where, queries, both_piece, row_start.reshape(row_count, 1).astype(jnp.int32),
        kv_heads, group_size, head_dim, block_q, block_k, chips,
    )
    pages_dev = row_count // PAGE
    owned_pages = seq_rank * pages_dev + jnp.arange(pages_dev, dtype=jnp.int32)
    page_count = page_table.shape[0]
    source_block = jnp.sum(
        jnp.where(
            page_table[None, :] == owned_pages[:, None],
            jnp.arange(page_count, dtype=jnp.int32)[None, :],
            0,
        ),
        axis=1,
    )
    stored = where[source_block // pages_dev] * row_count + (source_block % pages_dev) * PAGE
    pages = jnp.stack([lax.dynamic_slice_in_dim(both_piece, stored[p], PAGE, 0) for p in range(pages_dev)])
    key_cache = pages[:, :, :key_cols].reshape(pages_dev, PAGE, kv_heads, head_dim).transpose(0, 2, 1, 3)
    value_cache = pages[:, :, key_cols:].reshape(pages_dev, PAGE, kv_heads, head_dim).transpose(0, 2, 1, 3)
    return (attention, key_cache, value_cache)


def solution(mesh):
    seq_size = mesh.shape["seq"]
    tp_size = mesh.shape["tp"]
    chips = seq_size // 2
    return jax.shard_map(
        partial(shards, chips, tp_size),
        mesh=mesh,
        in_specs=(
            P("seq", "tp"),
            P(),
            P("seq", "tp"),
            P("seq", "tp"),
            P("seq", "tp"),
            P(),
            P(),
            P(),
            P(),
        ),
        out_specs=(P("seq", "tp"), P("seq", "tp", None, None), P("seq", "tp", None, None)),
        check_vma=False,
    )
```

```python
import math
from functools import partial

import jax
import jax.numpy as jnp
from jax import lax
from jax.sharding import Mesh, PartitionSpec as P
from jax.experimental import pallas as pl
from jax.experimental.pallas import tpu as pltpu

PAGE = 128


epsilon = 1e-06
excluded = -1e30


def segment_of(slot_index, prompt_ends):
    return jnp.sum((slot_index[..., None] >= prompt_ends).astype(jnp.int32), axis=-1)


def position_of(slot_index, prompt_ends, lengths):
    segment_id = segment_of(slot_index, prompt_ends)
    prompt_starts = prompt_ends - lengths
    labels = jnp.arange(lengths.shape[0], dtype=jnp.int32)
    picked = jnp.sum(jnp.where(segment_id[..., None] == labels, prompt_starts, 0), axis=-1)
    return (segment_id, slot_index - picked)


def head_norm(vectors, gain):
    mean_sq = jnp.mean(vectors * vectors, axis=-1, keepdims=True)
    return vectors * lax.rsqrt(mean_sq + epsilon) * gain


def rotate(vectors, position):
    head_dim = vectors.shape[-1]
    half_dim = head_dim // 2
    frequency = 1000000.0 ** (-(jnp.arange(half_dim, dtype=jnp.float32) * 2.0 / head_dim))
    angles = position.astype(jnp.float32)[:, None] * frequency[None, :]
    cosine = jnp.cos(angles)[:, None, :]
    sine_part = jnp.sin(angles)[:, None, :]
    front = vectors[..., :half_dim]
    back_half = vectors[..., half_dim:]
    return jnp.concatenate(
        [front * cosine - back_half * sine_part, back_half * cosine + front * sine_part], axis=-1
    )


def attend(
    query_block,
    query_slots,
    query_segments,
    key_piece,
    value_piece,
    key_slots,
    key_segments,
    kv_heads,
    group_size,
    head_dim,
    running,
):
    running_max, denominator, accumulator = running
    half_rows = query_block.shape[0]
    key_count = key_piece.shape[0]
    scores = jnp.einsum(
        "qkgd,nkd->kgqn",
        query_block.reshape(half_rows, kv_heads, group_size, head_dim),
        key_piece.reshape(key_count, kv_heads, head_dim),
        preferred_element_type=jnp.float32,
    ) * head_dim ** (-0.5)
    allowed = (key_segments[None, :] == query_segments[:, None]) & (
        key_slots[None, :] <= query_slots[:, None]
    )
    masked = jnp.where(allowed, scores, excluded)
    new_max = jnp.maximum(running_max, jnp.max(masked, axis=-1))
    weights = jnp.where(allowed, jnp.exp(scores - new_max[..., None]), 0.0)
    denominator = jnp.sum(weights, axis=-1)
    probs = weights.astype(jnp.bfloat16)
    accumulator = jnp.einsum(
        "kgqn,nkd->kgqd",
        probs,
        value_piece.reshape(key_count, kv_heads, head_dim),
        preferred_element_type=jnp.float32,
    )
    return (new_max, denominator, accumulator)


def flash_kernel(group_size, block_q, block_k, head_dim, rank_rows, first_call, last_call, meta_ref, where_ref, *refs):
    if first_call:
        q_ref, k_ref, v_ref, rs_ref = refs[:4]
        refs = refs[4:]
    else:
        q_ref, k_ref, v_ref, rs_ref, m_in, l_in, acc_in = refs[:7]
        refs = refs[7:]
    if last_call:
        o_ref, m_sc, l_sc, acc_sc = refs
    else:
        m_out, l_out, acc_out, m_sc, l_sc, acc_sc = refs
    i = pl.program_id(1)
    r0 = meta_ref[3 * i]
    s_first = meta_ref[3 * i + 1]
    s_last = meta_ref[3 * i + 2]
    rows = group_size * block_q
    q = q_ref[...]
    qs = jnp.concatenate([q[:, g * head_dim : (g + 1) * head_dim] for g in range(group_size)], axis=0)
    rstart = jnp.concatenate([rs_ref[...]] * group_size, axis=0)
    row_slot = r0 + lax.broadcasted_iota(jnp.int32, (group_size, block_q, 1), 1).reshape(rows, 1)
    if first_call:
        m_sc[...] = jnp.full(m_sc.shape, excluded, jnp.float32)
        l_sc[...] = jnp.zeros(l_sc.shape, jnp.float32)
        acc_sc[...] = jnp.zeros(acc_sc.shape, jnp.float32)
    else:
        m_sc[...] = jnp.broadcast_to(m_in[...], m_sc.shape)
        l_sc[...] = jnp.broadcast_to(l_in[...], l_sc.shape)
        acc_sc[...] = acc_in[...]
    scale = head_dim ** (-0.5) * math.log2(math.e)

    def update(kb, masked):
        first = kb * block_k
        stored = pl.multiple_of(where_ref[first // rank_rows] * rank_rows + first % rank_rows, block_k)
        k = k_ref[pl.ds(stored, block_k), :]
        v = v_ref[pl.ds(stored, block_k), :]
        s = lax.dot_general(qs, k, (((1,), (1,)), ((), ())), preferred_element_type=jnp.float32)
        if masked:
            cols = first + lax.broadcasted_iota(jnp.int32, (rows, block_k), 1)
            allowed = (cols >= rstart) & (cols <= row_slot)
            s_max = jnp.max(jnp.where(allowed, s, excluded), axis=1, keepdims=True)
        else:
            s_max = jnp.max(s, axis=1, keepdims=True)
        m_prev = m_sc[...]
        m_next = jnp.maximum(m_prev, s_max)
        alpha = jnp.exp2((m_prev - m_next) * scale)
        p = jnp.exp2((s - m_next[:, :1]) * scale)
        if masked:
            p = jnp.where(allowed, p, 0.0)
        l_sc[...] = alpha * l_sc[...] + jnp.sum(p, axis=1, keepdims=True)
        pv = jnp.dot(p.astype(jnp.bfloat16), v, preferred_element_type=jnp.float32)
        acc_sc[...] = acc_sc[...] * alpha + pv
        m_sc[...] = m_next

    def body(kb, carry):
        lo = kb * block_k
        full = (lo >= s_last) & (lo + block_k - 1 <= r0)
        present = where_ref[lo // rank_rows] >= 0

        @pl.when(full & present)
        def _():
            update(kb, False)

        @pl.when(jnp.logical_not(full) & present)
        def _():
            update(kb, True)

        return carry

    lax.fori_loop(s_first // block_k, (r0 + block_q - 1) // block_k + 1, body, 0)
    if last_call:
        res = acc_sc[...] / l_sc[...]
        o_ref[...] = jnp.concatenate(
            [res[g * block_q : (g + 1) * block_q] for g in range(group_size)], axis=1
        ).astype(o_ref.dtype)
    else:
        m_out[...] = m_sc[:, :1]
        l_out[...] = l_sc[:, :1]
        acc_out[...] = acc_sc[...]


def flash(meta, where, queries, both, row_start, state, kv_heads, group_size, head_dim, block_q, block_k, last_call):
    row_count = queries.shape[0]
    key_count = both.shape[0]
    n_qb = row_count // block_q
    rows = group_size * block_q
    first_call = state is None
    kernel = partial(flash_kernel, group_size, block_q, block_k, head_dim, row_count, first_call, last_call)
    in_specs = [
        pl.BlockSpec((block_q, group_size * head_dim), lambda h, i, meta, where: (i, h)),
        pl.BlockSpec((key_count, head_dim), lambda h, i, meta, where: (0, h)),
        pl.BlockSpec((key_count, head_dim), lambda h, i, meta, where: (0, kv_heads + h)),
        pl.BlockSpec((block_q, 1), lambda h, i, meta, where: (i, 0)),
    ]
    state_specs = [
        pl.BlockSpec((rows, 1), lambda h, i, meta, where: (h * n_qb + i, 0)),
        pl.BlockSpec((rows, 1), lambda h, i, meta, where: (h * n_qb + i, 0)),
        pl.BlockSpec((rows, head_dim), lambda h, i, meta, where: (h * n_qb + i, 0)),
    ]
    state_shapes = [
        jax.ShapeDtypeStruct((kv_heads * n_qb * rows, 1), jnp.float32),
        jax.ShapeDtypeStruct((kv_heads * n_qb * rows, 1), jnp.float32),
        jax.ShapeDtypeStruct((kv_heads * n_qb * rows, head_dim), jnp.float32),
    ]
    operands = [meta, where, queries, both, both, row_start]
    if not first_call:
        in_specs = in_specs + state_specs
        operands = operands + list(state)
    if last_call:
        out_specs = pl.BlockSpec((block_q, group_size * head_dim), lambda h, i, meta, where: (i, h))
        out_shape = jax.ShapeDtypeStruct(queries.shape, queries.dtype)
    else:
        out_specs = state_specs
        out_shape = state_shapes
    grid_spec = pltpu.PrefetchScalarGridSpec(
        num_scalar_prefetch=2,
        grid=(kv_heads, n_qb),
        in_specs=in_specs,
        out_specs=out_specs,
        scratch_shapes=[
            pltpu.VMEM((rows, head_dim), jnp.float32),
            pltpu.VMEM((rows, head_dim), jnp.float32),
            pltpu.VMEM((rows, head_dim), jnp.float32),
        ],
    )
    flops = 2 * kv_heads * rows * n_qb * 1024 * head_dim
    return pl.pallas_call(
        kernel,
        grid_spec=grid_spec,
        out_shape=out_shape,
        compiler_params=pltpu.CompilerParams(dimension_semantics=("arbitrary", "arbitrary")),
        cost_estimate=pl.CostEstimate(
            flops=flops, transcendentals=flops // (4 * head_dim), bytes_accessed=2 * queries.size * 2 + both.size * 2
        ),
    )(*operands)


def gather_rows(x, chips):
    seq_size = 2 * chips
    me = lax.axis_index("seq")
    ranks = jnp.arange(seq_size, dtype=jnp.int32)
    if chips != 4:
        return [(lax.all_gather(x, "seq", axis=0, tiled=True), ranks)]

    def swap(value, bit):
        return lax.ppermute(value, "seq", [(i, i ^ bit) for i in range(seq_size)])

    from_partner = swap(x, 1)
    from_x = swap(x, 2)
    from_y = swap(x, 4)
    forward = jnp.where(me % 2 == 0, from_y, from_x)
    from_diagonal = lax.ppermute(
        forward, "seq", [(i, i ^ 2) if i % 2 == 0 else (i, i ^ 4) for i in range(seq_size)]
    )
    early = jnp.concatenate([x, from_partner, from_x, from_y], axis=0)
    late = jnp.concatenate([swap(from_x, 1), swap(from_y, 1), from_diagonal, swap(from_diagonal, 1)], axis=0)
    mask = jnp.bitwise_xor(ranks, me)
    early_at = jnp.array([0, 1, 2, -1, 3, -1, -1, -1], jnp.int32)[mask]
    late_at = jnp.array([-1, -1, -1, 0, -1, 1, 2, 3], jnp.int32)[mask]
    return [(early, early_at), (late, late_at)]


def shards(
    chips,
    tp_size,
    hidden,
    norm_gain,
    query_weight,
    key_weight,
    value_weight,
    query_gain,
    key_gain,
    lengths,
    page_table,
):
    row_count = hidden.shape[0]
    head_dim = query_gain.shape[0]
    query_cols = query_weight.shape[1]
    key_cols = key_weight.shape[1]
    kv_heads = key_cols // head_dim
    group_size = query_cols // key_cols
    seq_rank = lax.axis_index("seq")
    prompt_ends = jnp.cumsum(lengths)
    tp_rank = lax.axis_index("tp")
    pieces = [hidden]
    for shift in range(1, tp_size):
        pairs = [(i, (i + shift) % tp_size) for i in range(tp_size)]
        pieces.append(lax.ppermute(hidden, "tp", pairs))
    gathered = jnp.concatenate(
        [lax.select_n((tp_rank - u) % tp_size, *pieces) for u in range(tp_size)], axis=1
    )
    widened = gathered.astype(jnp.float32)
    normed = (
        widened
        * lax.rsqrt(jnp.mean(widened * widened, axis=-1, keepdims=True) + epsilon)
        * norm_gain
    ).astype(jnp.bfloat16)
    server_block = jnp.concatenate([query_weight, key_weight, value_weight], axis=1).astype(
        jnp.bfloat16
    )
    full_block = lax.all_gather(server_block, "seq", axis=0, tiled=True)
    normed_perm = normed
    projected_kv = jnp.dot(normed_perm, full_block[:, query_cols:], preferred_element_type=jnp.float32)
    slot_index = seq_rank * row_count + jnp.arange(row_count, dtype=jnp.int32)
    segment_id, position = position_of(slot_index, prompt_ends, lengths)
    key_rows = rotate(
        head_norm(projected_kv[:, :key_cols].reshape(row_count, kv_heads, head_dim), key_gain),
        position,
    )
    key_rows = key_rows.reshape(row_count, key_cols).astype(jnp.bfloat16)
    values = projected_kv[:, key_cols:].astype(jnp.bfloat16)
    local_kv = jnp.concatenate([key_rows, values], axis=1)
    windows = gather_rows(local_kv, chips)
    projected_q = jnp.dot(normed_perm, full_block[:, :query_cols], preferred_element_type=jnp.float32)
    queries = rotate(
        head_norm(projected_q.reshape(row_count, query_cols // head_dim, head_dim), query_gain),
        position,
    )
    queries = queries.reshape(row_count, query_cols).astype(jnp.bfloat16)
    block_q = 128
    block_k = 512
    row_start = slot_index - position
    firsts = row_start[::block_q]
    lasts = row_start[block_q - 1 :: block_q]
    meta = jnp.stack([slot_index[::block_q], firsts, lasts], axis=1).reshape(-1).astype(jnp.int32)
    state = None
    for number, (window, where) in enumerate(windows):
        state = flash(
            meta, where, queries, window, row_start.reshape(row_count, 1).astype(jnp.int32), state,
            kv_heads, group_size, head_dim, block_q, block_k, number == len(windows) - 1,
        )
    attention = state
    pages_dev = row_count // PAGE
    owned_pages = seq_rank * pages_dev + jnp.arange(pages_dev, dtype=jnp.int32)
    page_count = page_table.shape[0]
    source_block = jnp.sum(
        jnp.where(
            page_table[None, :] == owned_pages[:, None],
            jnp.arange(page_count, dtype=jnp.int32)[None, :],
            0,
        ),
        axis=1,
    )
    source_rank = source_block // pages_dev
    offset = (source_block % pages_dev) * PAGE
    pages = None
    for window, where in windows:
        stored = jnp.maximum(where[source_rank], 0) * row_count + offset
        taken = jnp.stack([lax.dynamic_slice_in_dim(window, stored[p], PAGE, 0) for p in range(pages_dev)])
        if pages is None:
            pages = taken
        else:
            pages = jnp.where((where[source_rank] >= 0)[:, None, None], taken, pages)
    key_cache = pages[:, :, :key_cols].reshape(pages_dev, PAGE, kv_heads, head_dim).transpose(0, 2, 1, 3)
    value_cache = pages[:, :, key_cols:].reshape(pages_dev, PAGE, kv_heads, head_dim).transpose(0, 2, 1, 3)
    return (attention, key_cache, value_cache)


def solution(mesh):
    seq_size = mesh.shape["seq"]
    tp_size = mesh.shape["tp"]
    chips = seq_size // 2
    return jax.shard_map(
        partial(shards, chips, tp_size),
        mesh=mesh,
        in_specs=(
            P("seq", "tp"),
            P(),
            P("seq", "tp"),
            P("seq", "tp"),
            P("seq", "tp"),
            P(),
            P(),
            P(),
            P(),
        ),
        out_specs=(P("seq", "tp"), P("seq", "tp", None, None), P("seq", "tp", None, None)),
        check_vma=False,
    )
```

```python
import math
from functools import partial

import jax
import jax.numpy as jnp
from jax import lax
from jax.sharding import Mesh, PartitionSpec as P
from jax.experimental import pallas as pl
from jax.experimental.pallas import tpu as pltpu

PAGE = 128


epsilon = 1e-06
excluded = -1e30


def segment_of(slot_index, prompt_ends):
    return jnp.sum((slot_index[..., None] >= prompt_ends).astype(jnp.int32), axis=-1)


def position_of(slot_index, prompt_ends, lengths):
    segment_id = segment_of(slot_index, prompt_ends)
    prompt_starts = prompt_ends - lengths
    labels = jnp.arange(lengths.shape[0], dtype=jnp.int32)
    picked = jnp.sum(jnp.where(segment_id[..., None] == labels, prompt_starts, 0), axis=-1)
    return (segment_id, slot_index - picked)


def head_norm(vectors, gain):
    mean_sq = jnp.mean(vectors * vectors, axis=-1, keepdims=True)
    return vectors * lax.rsqrt(mean_sq + epsilon) * gain


def rotate(vectors, position):
    head_dim = vectors.shape[-1]
    half_dim = head_dim // 2
    frequency = 1000000.0 ** (-(jnp.arange(half_dim, dtype=jnp.float32) * 2.0 / head_dim))
    angles = position.astype(jnp.float32)[:, None] * frequency[None, :]
    cosine = jnp.cos(angles)[:, None, :]
    sine_part = jnp.sin(angles)[:, None, :]
    front = vectors[..., :half_dim]
    back_half = vectors[..., half_dim:]
    return jnp.concatenate(
        [front * cosine - back_half * sine_part, back_half * cosine + front * sine_part], axis=-1
    )


def attend(
    query_block,
    query_slots,
    query_segments,
    key_piece,
    value_piece,
    key_slots,
    key_segments,
    kv_heads,
    group_size,
    head_dim,
    running,
):
    running_max, denominator, accumulator = running
    half_rows = query_block.shape[0]
    key_count = key_piece.shape[0]
    scores = jnp.einsum(
        "qkgd,nkd->kgqn",
        query_block.reshape(half_rows, kv_heads, group_size, head_dim),
        key_piece.reshape(key_count, kv_heads, head_dim),
        preferred_element_type=jnp.float32,
    ) * head_dim ** (-0.5)
    allowed = (key_segments[None, :] == query_segments[:, None]) & (
        key_slots[None, :] <= query_slots[:, None]
    )
    masked = jnp.where(allowed, scores, excluded)
    new_max = jnp.maximum(running_max, jnp.max(masked, axis=-1))
    weights = jnp.where(allowed, jnp.exp(scores - new_max[..., None]), 0.0)
    denominator = jnp.sum(weights, axis=-1)
    probs = weights.astype(jnp.bfloat16)
    accumulator = jnp.einsum(
        "kgqn,nkd->kgqd",
        probs,
        value_piece.reshape(key_count, kv_heads, head_dim),
        preferred_element_type=jnp.float32,
    )
    return (new_max, denominator, accumulator)


def flash_kernel(group_size, block_q, block_k, head_dim, rank_rows, first_call, last_call, meta_ref, where_ref, *refs):
    if first_call:
        q_ref, k_ref, v_ref, rs_ref = refs[:4]
        refs = refs[4:]
    else:
        q_ref, k_ref, v_ref, rs_ref, m_in, l_in, acc_in = refs[:7]
        refs = refs[7:]
    if last_call:
        o_ref, m_sc, l_sc, acc_sc = refs
    else:
        m_out, l_out, acc_out, m_sc, l_sc, acc_sc = refs
    i = pl.program_id(1)
    r0 = meta_ref[3 * i]
    s_first = meta_ref[3 * i + 1]
    s_last = meta_ref[3 * i + 2]
    rows = group_size * block_q
    q = q_ref[...]
    qs = jnp.concatenate([q[:, g * head_dim : (g + 1) * head_dim] for g in range(group_size)], axis=0)
    rstart = jnp.concatenate([rs_ref[...]] * group_size, axis=0)
    row_slot = r0 + lax.broadcasted_iota(jnp.int32, (group_size, block_q, 1), 1).reshape(rows, 1)
    if first_call:
        m_sc[...] = jnp.full(m_sc.shape, excluded, jnp.float32)
        l_sc[...] = jnp.zeros(l_sc.shape, jnp.float32)
        acc_sc[...] = jnp.zeros(acc_sc.shape, jnp.float32)
    else:
        m_sc[...] = jnp.broadcast_to(m_in[...], m_sc.shape)
        l_sc[...] = jnp.broadcast_to(l_in[...], l_sc.shape)
        acc_sc[...] = acc_in[...]
    scale = head_dim ** (-0.5) * math.log2(math.e)

    def update(kb, masked):
        first = kb * block_k
        stored = pl.multiple_of(where_ref[first // rank_rows] * rank_rows + first % rank_rows, block_k)
        k = k_ref[pl.ds(stored, block_k), :]
        v = v_ref[pl.ds(stored, block_k), :]
        s = lax.dot_general(qs, k, (((1,), (1,)), ((), ())), preferred_element_type=jnp.float32)
        if masked:
            cols = first + lax.broadcasted_iota(jnp.int32, (rows, block_k), 1)
            allowed = (cols >= rstart) & (cols <= row_slot)
            s_max = jnp.max(jnp.where(allowed, s, excluded), axis=1, keepdims=True)
        else:
            s_max = jnp.max(s, axis=1, keepdims=True)
        m_prev = m_sc[...]
        m_next = jnp.maximum(m_prev, s_max)
        alpha = jnp.exp2((m_prev - m_next) * scale)
        p = jnp.exp2((s - m_next[:, :1]) * scale)
        if masked:
            p = jnp.where(allowed, p, 0.0)
        l_sc[...] = alpha * l_sc[...] + jnp.sum(p, axis=1, keepdims=True)
        pv = jnp.dot(p.astype(jnp.bfloat16), v, preferred_element_type=jnp.float32)
        acc_sc[...] = acc_sc[...] * alpha + pv
        m_sc[...] = m_next

    def body(kb, carry):
        lo = kb * block_k
        full = (lo >= s_last) & (lo + block_k - 1 <= r0)
        present = where_ref[lo // rank_rows] >= 0

        @pl.when(full & present)
        def _():
            update(kb, False)

        @pl.when(jnp.logical_not(full) & present)
        def _():
            update(kb, True)

        return carry

    lax.fori_loop(s_first // block_k, (r0 + block_q - 1) // block_k + 1, body, 0)
    if last_call:
        res = acc_sc[...] / l_sc[...]
        o_ref[...] = jnp.concatenate(
            [res[g * block_q : (g + 1) * block_q] for g in range(group_size)], axis=1
        ).astype(o_ref.dtype)
    else:
        m_out[...] = m_sc[:, :1]
        l_out[...] = l_sc[:, :1]
        acc_out[...] = acc_sc[...]


def flash(meta, where, queries, both, row_start, state, kv_heads, group_size, head_dim, block_q, block_k, last_call):
    row_count = queries.shape[0]
    key_count = both.shape[0]
    n_qb = row_count // block_q
    rows = group_size * block_q
    first_call = state is None
    kernel = partial(flash_kernel, group_size, block_q, block_k, head_dim, row_count, first_call, last_call)
    in_specs = [
        pl.BlockSpec((block_q, group_size * head_dim), lambda h, i, meta, where: (i, h)),
        pl.BlockSpec((key_count, head_dim), lambda h, i, meta, where: (0, h)),
        pl.BlockSpec((key_count, head_dim), lambda h, i, meta, where: (0, kv_heads + h)),
        pl.BlockSpec((block_q, 1), lambda h, i, meta, where: (i, 0)),
    ]
    state_specs = [
        pl.BlockSpec((rows, 1), lambda h, i, meta, where: (h * n_qb + i, 0)),
        pl.BlockSpec((rows, 1), lambda h, i, meta, where: (h * n_qb + i, 0)),
        pl.BlockSpec((rows, head_dim), lambda h, i, meta, where: (h * n_qb + i, 0)),
    ]
    state_shapes = [
        jax.ShapeDtypeStruct((kv_heads * n_qb * rows, 1), jnp.float32),
        jax.ShapeDtypeStruct((kv_heads * n_qb * rows, 1), jnp.float32),
        jax.ShapeDtypeStruct((kv_heads * n_qb * rows, head_dim), jnp.float32),
    ]
    operands = [meta, where, queries, both, both, row_start]
    if not first_call:
        in_specs = in_specs + state_specs
        operands = operands + list(state)
    if last_call:
        out_specs = pl.BlockSpec((block_q, group_size * head_dim), lambda h, i, meta, where: (i, h))
        out_shape = jax.ShapeDtypeStruct(queries.shape, queries.dtype)
    else:
        out_specs = state_specs
        out_shape = state_shapes
    grid_spec = pltpu.PrefetchScalarGridSpec(
        num_scalar_prefetch=2,
        grid=(kv_heads, n_qb),
        in_specs=in_specs,
        out_specs=out_specs,
        scratch_shapes=[
            pltpu.VMEM((rows, head_dim), jnp.float32),
            pltpu.VMEM((rows, head_dim), jnp.float32),
            pltpu.VMEM((rows, head_dim), jnp.float32),
        ],
    )
    flops = 2 * kv_heads * rows * n_qb * 1024 * head_dim
    return pl.pallas_call(
        kernel,
        grid_spec=grid_spec,
        out_shape=out_shape,
        compiler_params=pltpu.CompilerParams(dimension_semantics=("arbitrary", "arbitrary")),
        cost_estimate=pl.CostEstimate(
            flops=flops, transcendentals=flops // (4 * head_dim), bytes_accessed=2 * queries.size * 2 + both.size * 2
        ),
    )(*operands)


def gather_rows(x, chips):
    seq_size = 2 * chips
    me = lax.axis_index("seq")
    ranks = jnp.arange(seq_size, dtype=jnp.int32)
    if chips != 4:
        return [(lax.all_gather(x, "seq", axis=0, tiled=True), ranks, list(range(seq_size)))]

    def swap(value, bit):
        return lax.ppermute(value, "seq", [(i, i ^ bit) for i in range(seq_size)])

    from_partner = swap(x, 1)
    from_x = swap(x, 2)
    from_y = swap(x, 4)
    forward = jnp.where(me % 2 == 0, from_y, from_x)
    from_diagonal = lax.ppermute(
        forward, "seq", [(i, i ^ 2) if i % 2 == 0 else (i, i ^ 4) for i in range(seq_size)]
    )
    early = jnp.concatenate([x, from_partner, from_x, from_y], axis=0)
    late = jnp.concatenate([swap(from_x, 1), swap(from_y, 1), from_diagonal, swap(from_diagonal, 1)], axis=0)
    mask = jnp.bitwise_xor(ranks, me)
    early_at = jnp.array([0, 1, 2, -1, 3, -1, -1, -1], jnp.int32)[mask]
    late_at = jnp.array([-1, -1, -1, 0, -1, 1, 2, 3], jnp.int32)[mask]
    return [(early, early_at, [me ^ m for m in (0, 1, 2, 4)]), (late, late_at, [me ^ m for m in (3, 5, 6, 7)])]


def shards(
    chips,
    tp_size,
    hidden,
    norm_gain,
    query_weight,
    key_weight,
    value_weight,
    query_gain,
    key_gain,
    lengths,
    page_table,
):
    row_count = hidden.shape[0]
    head_dim = query_gain.shape[0]
    query_cols = query_weight.shape[1]
    key_cols = key_weight.shape[1]
    kv_heads = key_cols // head_dim
    group_size = query_cols // key_cols
    seq_rank = lax.axis_index("seq")
    prompt_ends = jnp.cumsum(lengths)
    tp_rank = lax.axis_index("tp")
    pieces = [hidden]
    for shift in range(1, tp_size):
        pairs = [(i, (i + shift) % tp_size) for i in range(tp_size)]
        pieces.append(lax.ppermute(hidden, "tp", pairs))
    gathered = jnp.concatenate(
        [lax.select_n((tp_rank - u) % tp_size, *pieces) for u in range(tp_size)], axis=1
    )
    widened = gathered.astype(jnp.float32)
    normed = (
        widened
        * lax.rsqrt(jnp.mean(widened * widened, axis=-1, keepdims=True) + epsilon)
        * norm_gain
    ).astype(jnp.bfloat16)
    server_block = jnp.concatenate([query_weight, key_weight, value_weight], axis=1).astype(
        jnp.bfloat16
    )
    weight_rows = server_block.shape[0]
    weight_windows = gather_rows(server_block, chips)
    normed_windows = [
        jnp.concatenate(
            [lax.dynamic_slice_in_dim(normed, rank * weight_rows, weight_rows, axis=1) for rank in order], axis=1
        )
        for _, _, order in weight_windows
    ]

    def project(first_col, last_col):
        total = None
        for (block, _, _), part in zip(weight_windows, normed_windows):
            term = jnp.dot(part, block[:, first_col:last_col], preferred_element_type=jnp.float32)
            total = term if total is None else total + term
        return total

    projected_kv = project(query_cols, query_cols + 2 * key_cols)
    slot_index = seq_rank * row_count + jnp.arange(row_count, dtype=jnp.int32)
    segment_id, position = position_of(slot_index, prompt_ends, lengths)
    key_rows = rotate(
        head_norm(projected_kv[:, :key_cols].reshape(row_count, kv_heads, head_dim), key_gain),
        position,
    )
    key_rows = key_rows.reshape(row_count, key_cols).astype(jnp.bfloat16)
    values = projected_kv[:, key_cols:].astype(jnp.bfloat16)
    local_kv = jnp.concatenate([key_rows, values], axis=1)
    windows = gather_rows(local_kv, chips)
    projected_q = project(0, query_cols)
    queries = rotate(
        head_norm(projected_q.reshape(row_count, query_cols // head_dim, head_dim), query_gain),
        position,
    )
    queries = queries.reshape(row_count, query_cols).astype(jnp.bfloat16)
    block_q = 128
    block_k = 512
    row_start = slot_index - position
    firsts = row_start[::block_q]
    lasts = row_start[block_q - 1 :: block_q]
    meta = jnp.stack([slot_index[::block_q], firsts, lasts], axis=1).reshape(-1).astype(jnp.int32)
    state = None
    for number, (window, where, _) in enumerate(windows):
        state = flash(
            meta, where, queries, window, row_start.reshape(row_count, 1).astype(jnp.int32), state,
            kv_heads, group_size, head_dim, block_q, block_k, number == len(windows) - 1,
        )
    attention = state
    pages_dev = row_count // PAGE
    owned_pages = seq_rank * pages_dev + jnp.arange(pages_dev, dtype=jnp.int32)
    page_count = page_table.shape[0]
    source_block = jnp.sum(
        jnp.where(
            page_table[None, :] == owned_pages[:, None],
            jnp.arange(page_count, dtype=jnp.int32)[None, :],
            0,
        ),
        axis=1,
    )
    source_rank = source_block // pages_dev
    offset = (source_block % pages_dev) * PAGE
    pages = None
    for window, where, _ in windows:
        stored = jnp.maximum(where[source_rank], 0) * row_count + offset
        taken = jnp.stack([lax.dynamic_slice_in_dim(window, stored[p], PAGE, 0) for p in range(pages_dev)])
        if pages is None:
            pages = taken
        else:
            pages = jnp.where((where[source_rank] >= 0)[:, None, None], taken, pages)
    key_cache = pages[:, :, :key_cols].reshape(pages_dev, PAGE, kv_heads, head_dim).transpose(0, 2, 1, 3)
    value_cache = pages[:, :, key_cols:].reshape(pages_dev, PAGE, kv_heads, head_dim).transpose(0, 2, 1, 3)
    return (attention, key_cache, value_cache)


def solution(mesh):
    seq_size = mesh.shape["seq"]
    tp_size = mesh.shape["tp"]
    chips = seq_size // 2
    return jax.shard_map(
        partial(shards, chips, tp_size),
        mesh=mesh,
        in_specs=(
            P("seq", "tp"),
            P(),
            P("seq", "tp"),
            P("seq", "tp"),
            P("seq", "tp"),
            P(),
            P(),
            P(),
            P(),
        ),
        out_specs=(P("seq", "tp"), P("seq", "tp", None, None), P("seq", "tp", None, None)),
        check_vma=False,
    )
```

```python
import math
from functools import partial

import jax
import jax.numpy as jnp
from jax import lax
from jax.sharding import Mesh, PartitionSpec as P
from jax.experimental import pallas as pl
from jax.experimental.pallas import tpu as pltpu

PAGE = 128


epsilon = 1e-06
excluded = -1e30


def segment_of(slot_index, prompt_ends):
    return jnp.sum((slot_index[..., None] >= prompt_ends).astype(jnp.int32), axis=-1)


def position_of(slot_index, prompt_ends, lengths):
    segment_id = segment_of(slot_index, prompt_ends)
    prompt_starts = prompt_ends - lengths
    labels = jnp.arange(lengths.shape[0], dtype=jnp.int32)
    picked = jnp.sum(jnp.where(segment_id[..., None] == labels, prompt_starts, 0), axis=-1)
    return (segment_id, slot_index - picked)


def head_norm(vectors, gain):
    mean_sq = jnp.mean(vectors * vectors, axis=-1, keepdims=True)
    return vectors * lax.rsqrt(mean_sq + epsilon) * gain


def rotate(vectors, position):
    head_dim = vectors.shape[-1]
    half_dim = head_dim // 2
    frequency = 1000000.0 ** (-(jnp.arange(half_dim, dtype=jnp.float32) * 2.0 / head_dim))
    angles = position.astype(jnp.float32)[:, None] * frequency[None, :]
    cosine = jnp.cos(angles)[:, None, :]
    sine_part = jnp.sin(angles)[:, None, :]
    front = vectors[..., :half_dim]
    back_half = vectors[..., half_dim:]
    return jnp.concatenate(
        [front * cosine - back_half * sine_part, back_half * cosine + front * sine_part], axis=-1
    )


def attend(
    query_block,
    query_slots,
    query_segments,
    key_piece,
    value_piece,
    key_slots,
    key_segments,
    kv_heads,
    group_size,
    head_dim,
    running,
):
    running_max, denominator, accumulator = running
    half_rows = query_block.shape[0]
    key_count = key_piece.shape[0]
    scores = jnp.einsum(
        "qkgd,nkd->kgqn",
        query_block.reshape(half_rows, kv_heads, group_size, head_dim),
        key_piece.reshape(key_count, kv_heads, head_dim),
        preferred_element_type=jnp.float32,
    ) * head_dim ** (-0.5)
    allowed = (key_segments[None, :] == query_segments[:, None]) & (
        key_slots[None, :] <= query_slots[:, None]
    )
    masked = jnp.where(allowed, scores, excluded)
    new_max = jnp.maximum(running_max, jnp.max(masked, axis=-1))
    weights = jnp.where(allowed, jnp.exp(scores - new_max[..., None]), 0.0)
    denominator = jnp.sum(weights, axis=-1)
    probs = weights.astype(jnp.bfloat16)
    accumulator = jnp.einsum(
        "kgqn,nkd->kgqd",
        probs,
        value_piece.reshape(key_count, kv_heads, head_dim),
        preferred_element_type=jnp.float32,
    )
    return (new_max, denominator, accumulator)


def flash_kernel(group_size, block_q, block_k, head_dim, rank_rows, first_call, last_call, meta_ref, where_ref, *refs):
    if first_call:
        q_ref, k_ref, v_ref, rs_ref = refs[:4]
        refs = refs[4:]
    else:
        q_ref, k_ref, v_ref, rs_ref, m_in, l_in, acc_in = refs[:7]
        refs = refs[7:]
    if last_call:
        o_ref, m_sc, l_sc, acc_sc = refs
    else:
        m_out, l_out, acc_out, m_sc, l_sc, acc_sc = refs
    i = pl.program_id(1)
    r0 = meta_ref[3 * i]
    s_first = meta_ref[3 * i + 1]
    s_last = meta_ref[3 * i + 2]
    rows = group_size * block_q
    q = q_ref[...]
    qs = jnp.concatenate([q[:, g * head_dim : (g + 1) * head_dim] for g in range(group_size)], axis=0)
    rstart = jnp.concatenate([rs_ref[...]] * group_size, axis=0)
    row_slot = r0 + lax.broadcasted_iota(jnp.int32, (group_size, block_q, 1), 1).reshape(rows, 1)
    if first_call:
        m_sc[...] = jnp.full(m_sc.shape, excluded, jnp.float32)
        l_sc[...] = jnp.zeros(l_sc.shape, jnp.float32)
        acc_sc[...] = jnp.zeros(acc_sc.shape, jnp.float32)
    else:
        m_sc[...] = jnp.broadcast_to(m_in[...], m_sc.shape)
        l_sc[...] = jnp.broadcast_to(l_in[...], l_sc.shape)
        acc_sc[...] = acc_in[...]
    scale = head_dim ** (-0.5) * math.log2(math.e)

    def update(kb, masked):
        first = kb * block_k
        stored = pl.multiple_of(where_ref[first // rank_rows] * rank_rows + first % rank_rows, block_k)
        k = k_ref[pl.ds(stored, block_k), :]
        v = v_ref[pl.ds(stored, block_k), :]
        s = lax.dot_general(qs, k, (((1,), (1,)), ((), ())), preferred_element_type=jnp.float32)
        if masked:
            cols = first + lax.broadcasted_iota(jnp.int32, (rows, block_k), 1)
            allowed = (cols >= rstart) & (cols <= row_slot)
            s = jnp.where(allowed, s, 2.0 * excluded)
        s_max = jnp.max(s, axis=1, keepdims=True)
        m_prev = m_sc[...]
        m_next = jnp.maximum(m_prev, s_max)
        alpha = jnp.exp2((m_prev - m_next) * scale)
        p = jnp.exp2((s - m_next[:, :1]) * scale)
        l_sc[...] = alpha * l_sc[...] + jnp.sum(p, axis=1, keepdims=True)
        pv = jnp.dot(p.astype(jnp.bfloat16), v, preferred_element_type=jnp.float32)
        acc_sc[...] = acc_sc[...] * alpha + pv
        m_sc[...] = m_next

    def body(kb, carry):
        lo = kb * block_k
        full = (lo >= s_last) & (lo + block_k - 1 <= r0)
        present = where_ref[lo // rank_rows] >= 0

        @pl.when(full & present)
        def _():
            update(kb, False)

        @pl.when(jnp.logical_not(full) & present)
        def _():
            update(kb, True)

        return carry

    lax.fori_loop(s_first // block_k, (r0 + block_q - 1) // block_k + 1, body, 0)
    if last_call:
        res = acc_sc[...] / l_sc[...]
        o_ref[...] = jnp.concatenate(
            [res[g * block_q : (g + 1) * block_q] for g in range(group_size)], axis=1
        ).astype(o_ref.dtype)
    else:
        m_out[...] = m_sc[:, :1]
        l_out[...] = l_sc[:, :1]
        acc_out[...] = acc_sc[...]


def flash(meta, where, queries, both, row_start, state, kv_heads, group_size, head_dim, block_q, block_k, last_call):
    row_count = queries.shape[0]
    key_count = both.shape[0]
    n_qb = row_count // block_q
    rows = group_size * block_q
    first_call = state is None
    kernel = partial(flash_kernel, group_size, block_q, block_k, head_dim, row_count, first_call, last_call)
    in_specs = [
        pl.BlockSpec((block_q, group_size * head_dim), lambda h, i, meta, where: (i, h)),
        pl.BlockSpec((key_count, head_dim), lambda h, i, meta, where: (0, h)),
        pl.BlockSpec((key_count, head_dim), lambda h, i, meta, where: (0, kv_heads + h)),
        pl.BlockSpec((block_q, 1), lambda h, i, meta, where: (i, 0)),
    ]
    state_specs = [
        pl.BlockSpec((rows, 1), lambda h, i, meta, where: (h * n_qb + i, 0)),
        pl.BlockSpec((rows, 1), lambda h, i, meta, where: (h * n_qb + i, 0)),
        pl.BlockSpec((rows, head_dim), lambda h, i, meta, where: (h * n_qb + i, 0)),
    ]
    state_shapes = [
        jax.ShapeDtypeStruct((kv_heads * n_qb * rows, 1), jnp.float32),
        jax.ShapeDtypeStruct((kv_heads * n_qb * rows, 1), jnp.float32),
        jax.ShapeDtypeStruct((kv_heads * n_qb * rows, head_dim), jnp.float32),
    ]
    operands = [meta, where, queries, both, both, row_start]
    if not first_call:
        in_specs = in_specs + state_specs
        operands = operands + list(state)
    if last_call:
        out_specs = pl.BlockSpec((block_q, group_size * head_dim), lambda h, i, meta, where: (i, h))
        out_shape = jax.ShapeDtypeStruct(queries.shape, queries.dtype)
    else:
        out_specs = state_specs
        out_shape = state_shapes
    grid_spec = pltpu.PrefetchScalarGridSpec(
        num_scalar_prefetch=2,
        grid=(kv_heads, n_qb),
        in_specs=in_specs,
        out_specs=out_specs,
        scratch_shapes=[
            pltpu.VMEM((rows, head_dim), jnp.float32),
            pltpu.VMEM((rows, head_dim), jnp.float32),
            pltpu.VMEM((rows, head_dim), jnp.float32),
        ],
    )
    flops = 2 * kv_heads * rows * n_qb * 1024 * head_dim
    return pl.pallas_call(
        kernel,
        grid_spec=grid_spec,
        out_shape=out_shape,
        compiler_params=pltpu.CompilerParams(dimension_semantics=("arbitrary", "arbitrary")),
        cost_estimate=pl.CostEstimate(
            flops=flops, transcendentals=flops // (4 * head_dim), bytes_accessed=2 * queries.size * 2 + both.size * 2
        ),
    )(*operands)


def gather_rows(x, chips):
    seq_size = 2 * chips
    me = lax.axis_index("seq")
    ranks = jnp.arange(seq_size, dtype=jnp.int32)
    if chips != 4:
        return [(lax.all_gather(x, "seq", axis=0, tiled=True), ranks)]

    def swap(value, bit):
        return lax.ppermute(value, "seq", [(i, i ^ bit) for i in range(seq_size)])

    from_partner = swap(x, 1)
    from_x = swap(x, 2)
    from_y = swap(x, 4)
    forward = jnp.where(me % 2 == 0, from_y, from_x)
    from_diagonal = lax.ppermute(
        forward, "seq", [(i, i ^ 2) if i % 2 == 0 else (i, i ^ 4) for i in range(seq_size)]
    )
    early = jnp.concatenate([x, from_partner, from_x, from_y], axis=0)
    late = jnp.concatenate([swap(from_x, 1), swap(from_y, 1), from_diagonal, swap(from_diagonal, 1)], axis=0)
    mask = jnp.bitwise_xor(ranks, me)
    early_at = jnp.array([0, 1, 2, -1, 3, -1, -1, -1], jnp.int32)[mask]
    late_at = jnp.array([-1, -1, -1, 0, -1, 1, 2, 3], jnp.int32)[mask]
    return [(early, early_at), (late, late_at)]


def shards(
    chips,
    tp_size,
    hidden,
    norm_gain,
    query_weight,
    key_weight,
    value_weight,
    query_gain,
    key_gain,
    lengths,
    page_table,
):
    row_count = hidden.shape[0]
    head_dim = query_gain.shape[0]
    query_cols = query_weight.shape[1]
    key_cols = key_weight.shape[1]
    kv_heads = key_cols // head_dim
    group_size = query_cols // key_cols
    seq_rank = lax.axis_index("seq")
    prompt_ends = jnp.cumsum(lengths)
    tp_rank = lax.axis_index("tp")
    pieces = [hidden]
    for shift in range(1, tp_size):
        pairs = [(i, (i + shift) % tp_size) for i in range(tp_size)]
        pieces.append(lax.ppermute(hidden, "tp", pairs))
    gathered = jnp.concatenate(
        [lax.select_n((tp_rank - u) % tp_size, *pieces) for u in range(tp_size)], axis=1
    )
    widened = gathered.astype(jnp.float32)
    normed = (
        widened
        * lax.rsqrt(jnp.mean(widened * widened, axis=-1, keepdims=True) + epsilon)
        * norm_gain
    ).astype(jnp.bfloat16)
    server_block = jnp.concatenate([query_weight, key_weight, value_weight], axis=1).astype(
        jnp.bfloat16
    )
    full_block = lax.all_gather(server_block, "seq", axis=0, tiled=True)
    normed_perm = normed
    projected_kv = jnp.dot(normed_perm, full_block[:, query_cols:], preferred_element_type=jnp.float32)
    slot_index = seq_rank * row_count + jnp.arange(row_count, dtype=jnp.int32)
    segment_id, position = position_of(slot_index, prompt_ends, lengths)
    key_rows = rotate(
        head_norm(projected_kv[:, :key_cols].reshape(row_count, kv_heads, head_dim), key_gain),
        position,
    )
    key_rows = key_rows.reshape(row_count, key_cols).astype(jnp.bfloat16)
    values = projected_kv[:, key_cols:].astype(jnp.bfloat16)
    local_kv = jnp.concatenate([key_rows, values], axis=1)
    windows = gather_rows(local_kv, chips)
    projected_q = jnp.dot(normed_perm, full_block[:, :query_cols], preferred_element_type=jnp.float32)
    queries = rotate(
        head_norm(projected_q.reshape(row_count, query_cols // head_dim, head_dim), query_gain),
        position,
    )
    queries = queries.reshape(row_count, query_cols).astype(jnp.bfloat16)
    block_q = 128
    block_k = 512
    row_start = slot_index - position
    firsts = row_start[::block_q]
    lasts = row_start[block_q - 1 :: block_q]
    meta = jnp.stack([slot_index[::block_q], firsts, lasts], axis=1).reshape(-1).astype(jnp.int32)
    state = None
    for number, (window, where) in enumerate(windows):
        state = flash(
            meta, where, queries, window, row_start.reshape(row_count, 1).astype(jnp.int32), state,
            kv_heads, group_size, head_dim, block_q, block_k, number == len(windows) - 1,
        )
    attention = state
    pages_dev = row_count // PAGE
    owned_pages = seq_rank * pages_dev + jnp.arange(pages_dev, dtype=jnp.int32)
    page_count = page_table.shape[0]
    source_block = jnp.sum(
        jnp.where(
            page_table[None, :] == owned_pages[:, None],
            jnp.arange(page_count, dtype=jnp.int32)[None, :],
            0,
        ),
        axis=1,
    )
    source_rank = source_block // pages_dev
    offset = (source_block % pages_dev) * PAGE
    pages = None
    for window, where in windows:
        stored = jnp.maximum(where[source_rank], 0) * row_count + offset
        taken = jnp.stack([lax.dynamic_slice_in_dim(window, stored[p], PAGE, 0) for p in range(pages_dev)])
        if pages is None:
            pages = taken
        else:
            pages = jnp.where((where[source_rank] >= 0)[:, None, None], taken, pages)
    key_cache = pages[:, :, :key_cols].reshape(pages_dev, PAGE, kv_heads, head_dim).transpose(0, 2, 1, 3)
    value_cache = pages[:, :, key_cols:].reshape(pages_dev, PAGE, kv_heads, head_dim).transpose(0, 2, 1, 3)
    return (attention, key_cache, value_cache)


def solution(mesh):
    seq_size = mesh.shape["seq"]
    tp_size = mesh.shape["tp"]
    chips = seq_size // 2
    return jax.shard_map(
        partial(shards, chips, tp_size),
        mesh=mesh,
        in_specs=(
            P("seq", "tp"),
            P(),
            P("seq", "tp"),
            P("seq", "tp"),
            P("seq", "tp"),
            P(),
            P(),
            P(),
            P(),
        ),
        out_specs=(P("seq", "tp"), P("seq", "tp", None, None), P("seq", "tp", None, None)),
        check_vma=False,
    )
```

```python
import math
from functools import partial

import jax
import jax.numpy as jnp
from jax import lax
from jax.sharding import Mesh, PartitionSpec as P
from jax.experimental import pallas as pl
from jax.experimental.pallas import tpu as pltpu

PAGE = 128


epsilon = 1e-06
excluded = -1e30


def segment_of(slot_index, prompt_ends):
    return jnp.sum((slot_index[..., None] >= prompt_ends).astype(jnp.int32), axis=-1)


def position_of(slot_index, prompt_ends, lengths):
    segment_id = segment_of(slot_index, prompt_ends)
    prompt_starts = prompt_ends - lengths
    labels = jnp.arange(lengths.shape[0], dtype=jnp.int32)
    picked = jnp.sum(jnp.where(segment_id[..., None] == labels, prompt_starts, 0), axis=-1)
    return (segment_id, slot_index - picked)


def head_norm(vectors, gain):
    mean_sq = jnp.mean(vectors * vectors, axis=-1, keepdims=True)
    return vectors * lax.rsqrt(mean_sq + epsilon) * gain


def rotate(vectors, position):
    head_dim = vectors.shape[-1]
    half_dim = head_dim // 2
    frequency = 1000000.0 ** (-(jnp.arange(half_dim, dtype=jnp.float32) * 2.0 / head_dim))
    angles = position.astype(jnp.float32)[:, None] * frequency[None, :]
    cosine = jnp.cos(angles)[:, None, :]
    sine_part = jnp.sin(angles)[:, None, :]
    front = vectors[..., :half_dim]
    back_half = vectors[..., half_dim:]
    return jnp.concatenate(
        [front * cosine - back_half * sine_part, back_half * cosine + front * sine_part], axis=-1
    )


def attend(
    query_block,
    query_slots,
    query_segments,
    key_piece,
    value_piece,
    key_slots,
    key_segments,
    kv_heads,
    group_size,
    head_dim,
    running,
):
    running_max, denominator, accumulator = running
    half_rows = query_block.shape[0]
    key_count = key_piece.shape[0]
    scores = jnp.einsum(
        "qkgd,nkd->kgqn",
        query_block.reshape(half_rows, kv_heads, group_size, head_dim),
        key_piece.reshape(key_count, kv_heads, head_dim),
        preferred_element_type=jnp.float32,
    ) * head_dim ** (-0.5)
    allowed = (key_segments[None, :] == query_segments[:, None]) & (
        key_slots[None, :] <= query_slots[:, None]
    )
    masked = jnp.where(allowed, scores, excluded)
    new_max = jnp.maximum(running_max, jnp.max(masked, axis=-1))
    weights = jnp.where(allowed, jnp.exp(scores - new_max[..., None]), 0.0)
    denominator = jnp.sum(weights, axis=-1)
    probs = weights.astype(jnp.bfloat16)
    accumulator = jnp.einsum(
        "kgqn,nkd->kgqd",
        probs,
        value_piece.reshape(key_count, kv_heads, head_dim),
        preferred_element_type=jnp.float32,
    )
    return (new_max, denominator, accumulator)


def flash_kernel(group_size, block_q, block_k, head_dim, chips, rank_rows, meta_ref, where_ref, q_ref, k_ref, v_ref, rs_ref, o_ref, m_sc, l_sc, acc_sc):
    i = pl.program_id(1)
    r0 = meta_ref[3 * i]
    s_first = meta_ref[3 * i + 1]
    s_last = meta_ref[3 * i + 2]
    rows = group_size * block_q
    q = q_ref[...]
    qs = jnp.concatenate([q[:, g * head_dim : (g + 1) * head_dim] for g in range(group_size)], axis=0)
    rstart = jnp.concatenate([rs_ref[...]] * group_size, axis=0)
    row_slot = r0 + lax.broadcasted_iota(jnp.int32, (group_size, block_q, 1), 1).reshape(rows, 1)
    m_sc[...] = jnp.full(m_sc.shape, excluded, jnp.float32)
    l_sc[...] = jnp.zeros(l_sc.shape, jnp.float32)
    acc_sc[...] = jnp.zeros(acc_sc.shape, jnp.float32)
    scale = head_dim ** (-0.5) * math.log2(math.e)

    def update(kb, masked):
        first = kb * block_k
        stored = pl.multiple_of(where_ref[first // rank_rows] * rank_rows + first % rank_rows, block_k)
        k = k_ref[pl.ds(stored, block_k), :]
        v = v_ref[pl.ds(stored, block_k), :]
        s = lax.dot_general(qs, k, (((1,), (1,)), ((), ())), preferred_element_type=jnp.float32)
        if masked:
            cols = first + lax.broadcasted_iota(jnp.int32, (rows, block_k), 1)
            allowed = (cols >= rstart) & (cols <= row_slot)
            s = jnp.where(allowed, s, 2.0 * excluded)
        s_max = jnp.max(s, axis=1, keepdims=True)
        m_prev = m_sc[...]
        m_next = jnp.maximum(m_prev, s_max)
        alpha = jnp.exp2((m_prev - m_next) * scale)
        p = jnp.exp2((s - m_next[:, :1]) * scale)
        l_sc[...] = alpha * l_sc[...] + jnp.sum(p, axis=1, keepdims=True)
        pv = jnp.dot(p.astype(jnp.bfloat16), v, preferred_element_type=jnp.float32)
        acc_sc[...] = acc_sc[...] * alpha + pv
        m_sc[...] = m_next

    def body(kb, carry):
        lo = kb * block_k
        full = (lo >= s_last) & (lo + block_k - 1 <= r0)

        @pl.when(full)
        def _():
            update(kb, False)

        @pl.when(jnp.logical_not(full))
        def _():
            update(kb, True)

        return carry

    lax.fori_loop(s_first // block_k, (r0 + block_q - 1) // block_k + 1, body, 0)
    res = acc_sc[...] / l_sc[...]
    o_ref[...] = jnp.concatenate(
        [res[g * block_q : (g + 1) * block_q] for g in range(group_size)], axis=1
    ).astype(o_ref.dtype)


def flash(meta, where, queries, both, row_start, kv_heads, group_size, head_dim, block_q, block_k, chips):
    row_count = queries.shape[0]
    key_count = both.shape[0]
    n_qb = row_count // block_q
    rows = group_size * block_q
    kernel = partial(flash_kernel, group_size, block_q, block_k, head_dim, chips, row_count)
    grid_spec = pltpu.PrefetchScalarGridSpec(
        num_scalar_prefetch=2,
        grid=(kv_heads, n_qb),
        in_specs=[
            pl.BlockSpec((block_q, group_size * head_dim), lambda h, i, meta, where: (i, h)),
            pl.BlockSpec((key_count, head_dim), lambda h, i, meta, where: (0, h)),
            pl.BlockSpec((key_count, head_dim), lambda h, i, meta, where: (0, kv_heads + h)),
            pl.BlockSpec((block_q, 1), lambda h, i, meta, where: (i, 0)),
        ],
        out_specs=pl.BlockSpec((block_q, group_size * head_dim), lambda h, i, meta, where: (i, h)),
        scratch_shapes=[
            pltpu.VMEM((rows, head_dim), jnp.float32),
            pltpu.VMEM((rows, head_dim), jnp.float32),
            pltpu.VMEM((rows, head_dim), jnp.float32),
        ],
    )
    flops = 4 * kv_heads * rows * n_qb * 1536 * head_dim
    return pl.pallas_call(
        kernel,
        grid_spec=grid_spec,
        out_shape=jax.ShapeDtypeStruct(queries.shape, queries.dtype),
        compiler_params=pltpu.CompilerParams(dimension_semantics=("arbitrary", "arbitrary")),
        cost_estimate=pl.CostEstimate(
            flops=flops, transcendentals=flops // (4 * head_dim), bytes_accessed=2 * queries.size * 2 + both.size * 2
        ),
    )(meta, where, queries, both, both, row_start)


def gather_rows(x, chips):
    seq_size = 2 * chips
    me = lax.axis_index("seq")
    if chips != 4:
        return lax.all_gather(x, "seq", axis=0, tiled=True), jnp.arange(seq_size, dtype=jnp.int32)

    def swap(value, bit):
        return lax.ppermute(value, "seq", [(i, i ^ bit) for i in range(seq_size)])

    from_partner = swap(x, 1)
    from_x = swap(x, 2)
    from_y = swap(x, 4)
    forward = jnp.where(me % 2 == 0, from_y, from_x)
    from_diagonal = lax.ppermute(
        forward, "seq", [(i, i ^ 2) if i % 2 == 0 else (i, i ^ 4) for i in range(seq_size)]
    )
    by_mask = [
        x,
        from_partner,
        from_x,
        swap(from_x, 1),
        from_y,
        swap(from_y, 1),
        from_diagonal,
        swap(from_diagonal, 1),
    ]
    where = jnp.bitwise_xor(jnp.arange(seq_size, dtype=jnp.int32), me)
    return jnp.concatenate(by_mask, axis=0), where


def shards(
    chips,
    tp_size,
    hidden,
    norm_gain,
    query_weight,
    key_weight,
    value_weight,
    query_gain,
    key_gain,
    lengths,
    page_table,
):
    row_count = hidden.shape[0]
    head_dim = query_gain.shape[0]
    query_cols = query_weight.shape[1]
    key_cols = key_weight.shape[1]
    kv_heads = key_cols // head_dim
    group_size = query_cols // key_cols
    seq_rank = lax.axis_index("seq")
    prompt_ends = jnp.cumsum(lengths)
    tp_rank = lax.axis_index("tp")
    pieces = [hidden]
    for shift in range(1, tp_size):
        pairs = [(i, (i + shift) % tp_size) for i in range(tp_size)]
        pieces.append(lax.ppermute(hidden, "tp", pairs))
    gathered = jnp.concatenate(
        [lax.select_n((tp_rank - u) % tp_size, *pieces) for u in range(tp_size)], axis=1
    )
    widened = gathered.astype(jnp.float32)
    normed = (
        widened
        * lax.rsqrt(jnp.mean(widened * widened, axis=-1, keepdims=True) + epsilon)
        * norm_gain
    ).astype(jnp.bfloat16)
    server_block = jnp.concatenate([query_weight, key_weight, value_weight], axis=1).astype(
        jnp.bfloat16
    )
    full_block = lax.all_gather(server_block, "seq", axis=0, tiled=True)
    normed_perm = normed
    projected_kv = jnp.dot(normed_perm, full_block[:, query_cols:], preferred_element_type=jnp.float32)
    slot_index = seq_rank * row_count + jnp.arange(row_count, dtype=jnp.int32)
    segment_id, position = position_of(slot_index, prompt_ends, lengths)
    key_rows = rotate(
        head_norm(projected_kv[:, :key_cols].reshape(row_count, kv_heads, head_dim), key_gain),
        position,
    )
    key_rows = key_rows.reshape(row_count, key_cols).astype(jnp.bfloat16)
    values = projected_kv[:, key_cols:].astype(jnp.bfloat16)
    local_kv = jnp.concatenate([key_rows, values], axis=1)
    both_piece, where = gather_rows(local_kv, chips)
    projected_q = jnp.dot(normed_perm, full_block[:, :query_cols], preferred_element_type=jnp.float32)
    queries = rotate(
        head_norm(projected_q.reshape(row_count, query_cols // head_dim, head_dim), query_gain),
        position,
    )
    queries = queries.reshape(row_count, query_cols).astype(jnp.bfloat16)
    block_q = 128
    block_k = 512
    row_start = slot_index - position
    firsts = row_start[::block_q]
    lasts = row_start[block_q - 1 :: block_q]
    meta = jnp.stack([slot_index[::block_q], firsts, lasts], axis=1).reshape(-1).astype(jnp.int32)
    attention = flash(
        meta, where, queries, both_piece, row_start.reshape(row_count, 1).astype(jnp.int32),
        kv_heads, group_size, head_dim, block_q, block_k, chips,
    )
    pages_dev = row_count // PAGE
    owned_pages = seq_rank * pages_dev + jnp.arange(pages_dev, dtype=jnp.int32)
    page_count = page_table.shape[0]
    source_block = jnp.sum(
        jnp.where(
            page_table[None, :] == owned_pages[:, None],
            jnp.arange(page_count, dtype=jnp.int32)[None, :],
            0,
        ),
        axis=1,
    )
    stored = where[source_block // pages_dev] * row_count + (source_block % pages_dev) * PAGE
    pages = jnp.stack([lax.dynamic_slice_in_dim(both_piece, stored[p], PAGE, 0) for p in range(pages_dev)])
    key_cache = pages[:, :, :key_cols].reshape(pages_dev, PAGE, kv_heads, head_dim).transpose(0, 2, 1, 3)
    value_cache = pages[:, :, key_cols:].reshape(pages_dev, PAGE, kv_heads, head_dim).transpose(0, 2, 1, 3)
    return (attention, key_cache, value_cache)


def solution(mesh):
    seq_size = mesh.shape["seq"]
    tp_size = mesh.shape["tp"]
    chips = seq_size // 2
    return jax.shard_map(
        partial(shards, chips, tp_size),
        mesh=mesh,
        in_specs=(
            P("seq", "tp"),
            P(),
            P("seq", "tp"),
            P("seq", "tp"),
            P("seq", "tp"),
            P(),
            P(),
            P(),
            P(),
        ),
        out_specs=(P("seq", "tp"), P("seq", "tp", None, None), P("seq", "tp", None, None)),
        check_vma=False,
    )
```

```python
import math
from functools import partial

import jax
import jax.numpy as jnp
from jax import lax
from jax.sharding import Mesh, PartitionSpec as P
from jax.experimental import pallas as pl
from jax.experimental.pallas import tpu as pltpu

PAGE = 128


epsilon = 1e-06
excluded = -1e30


def segment_of(slot_index, prompt_ends):
    return jnp.sum((slot_index[..., None] >= prompt_ends).astype(jnp.int32), axis=-1)


def position_of(slot_index, prompt_ends, lengths):
    segment_id = segment_of(slot_index, prompt_ends)
    prompt_starts = prompt_ends - lengths
    labels = jnp.arange(lengths.shape[0], dtype=jnp.int32)
    picked = jnp.sum(jnp.where(segment_id[..., None] == labels, prompt_starts, 0), axis=-1)
    return (segment_id, slot_index - picked)


def head_norm(vectors, gain):
    mean_sq = jnp.mean(vectors * vectors, axis=-1, keepdims=True)
    return vectors * lax.rsqrt(mean_sq + epsilon) * gain


def rotate(vectors, position):
    head_dim = vectors.shape[-1]
    half_dim = head_dim // 2
    frequency = 1000000.0 ** (-(jnp.arange(half_dim, dtype=jnp.float32) * 2.0 / head_dim))
    angles = position.astype(jnp.float32)[:, None] * frequency[None, :]
    cosine = jnp.cos(angles)[:, None, :]
    sine_part = jnp.sin(angles)[:, None, :]
    front = vectors[..., :half_dim]
    back_half = vectors[..., half_dim:]
    return jnp.concatenate(
        [front * cosine - back_half * sine_part, back_half * cosine + front * sine_part], axis=-1
    )


def attend(
    query_block,
    query_slots,
    query_segments,
    key_piece,
    value_piece,
    key_slots,
    key_segments,
    kv_heads,
    group_size,
    head_dim,
    running,
):
    running_max, denominator, accumulator = running
    half_rows = query_block.shape[0]
    key_count = key_piece.shape[0]
    scores = jnp.einsum(
        "qkgd,nkd->kgqn",
        query_block.reshape(half_rows, kv_heads, group_size, head_dim),
        key_piece.reshape(key_count, kv_heads, head_dim),
        preferred_element_type=jnp.float32,
    ) * head_dim ** (-0.5)
    allowed = (key_segments[None, :] == query_segments[:, None]) & (
        key_slots[None, :] <= query_slots[:, None]
    )
    masked = jnp.where(allowed, scores, excluded)
    new_max = jnp.maximum(running_max, jnp.max(masked, axis=-1))
    weights = jnp.where(allowed, jnp.exp(scores - new_max[..., None]), 0.0)
    denominator = jnp.sum(weights, axis=-1)
    probs = weights.astype(jnp.bfloat16)
    accumulator = jnp.einsum(
        "kgqn,nkd->kgqd",
        probs,
        value_piece.reshape(key_count, kv_heads, head_dim),
        preferred_element_type=jnp.float32,
    )
    return (new_max, denominator, accumulator)


def flash_kernel(group_size, block_q, block_k, head_dim, chips, rank_rows, meta_ref, where_ref, q_ref, k_ref, v_ref, rs_ref, o_ref, m_sc, l_sc, acc_sc):
    i = pl.program_id(1)
    r0 = meta_ref[3 * i]
    s_first = meta_ref[3 * i + 1]
    s_last = meta_ref[3 * i + 2]
    rows = group_size * block_q
    q = q_ref[...]
    qs = jnp.concatenate([q[:, g * head_dim : (g + 1) * head_dim] for g in range(group_size)], axis=0)
    rstart = jnp.concatenate([rs_ref[...]] * group_size, axis=0)
    row_slot = r0 + lax.broadcasted_iota(jnp.int32, (group_size, block_q, 1), 1).reshape(rows, 1)
    m_sc[...] = jnp.full(m_sc.shape, excluded, jnp.float32)
    l_sc[...] = jnp.zeros(l_sc.shape, jnp.float32)
    acc_sc[...] = jnp.zeros(acc_sc.shape, jnp.float32)
    scale = head_dim ** (-0.5) * math.log2(math.e)

    def update(kb, masked):
        first = kb * block_k
        stored = pl.multiple_of(where_ref[first // rank_rows] * rank_rows + first % rank_rows, block_k)
        k = k_ref[pl.ds(stored, block_k), :]
        v = v_ref[pl.ds(stored, block_k), :]
        s = lax.dot_general(qs, k, (((1,), (1,)), ((), ())), preferred_element_type=jnp.float32)
        if masked:
            cols = first + lax.broadcasted_iota(jnp.int32, (rows, block_k), 1)
            allowed = (cols >= rstart) & (cols <= row_slot)
            s = jnp.where(allowed, s, 2.0 * excluded)
        s_max = jnp.max(s, axis=1, keepdims=True)
        m_prev = m_sc[...]
        m_next = jnp.maximum(m_prev, s_max)
        alpha = jnp.exp2((m_prev - m_next) * scale)
        p = jnp.exp2((s - m_next[:, :1]) * scale)
        l_sc[...] = alpha * l_sc[...] + jnp.sum(p, axis=1, keepdims=True)
        pv = jnp.dot(p.astype(jnp.bfloat16), v, preferred_element_type=jnp.float32)
        acc_sc[...] = acc_sc[...] * alpha + pv
        m_sc[...] = m_next

    def body(kb, carry):
        lo = kb * block_k
        full = (lo >= s_last) & (lo + block_k - 1 <= r0)

        @pl.when(full)
        def _():
            update(kb, False)

        @pl.when(jnp.logical_not(full))
        def _():
            update(kb, True)

        return carry

    lax.fori_loop(s_first // block_k, (r0 + block_q - 1) // block_k + 1, body, 0)
    res = acc_sc[...] / l_sc[...]
    o_ref[...] = jnp.concatenate(
        [res[g * block_q : (g + 1) * block_q] for g in range(group_size)], axis=1
    ).astype(o_ref.dtype)


def flash(meta, where, queries, both, row_start, kv_heads, group_size, head_dim, block_q, block_k, chips):
    row_count = queries.shape[0]
    key_count = both.shape[0]
    n_qb = row_count // block_q
    rows = group_size * block_q
    kernel = partial(flash_kernel, group_size, block_q, block_k, head_dim, chips, row_count)
    grid_spec = pltpu.PrefetchScalarGridSpec(
        num_scalar_prefetch=2,
        grid=(kv_heads, n_qb),
        in_specs=[
            pl.BlockSpec((block_q, group_size * head_dim), lambda h, i, meta, where: (i, h)),
            pl.BlockSpec((key_count, head_dim), lambda h, i, meta, where: (0, h)),
            pl.BlockSpec((key_count, head_dim), lambda h, i, meta, where: (0, kv_heads + h)),
            pl.BlockSpec((block_q, 1), lambda h, i, meta, where: (i, 0)),
        ],
        out_specs=pl.BlockSpec((block_q, group_size * head_dim), lambda h, i, meta, where: (i, h)),
        scratch_shapes=[
            pltpu.VMEM((rows, head_dim), jnp.float32),
            pltpu.VMEM((rows, head_dim), jnp.float32),
            pltpu.VMEM((rows, head_dim), jnp.float32),
        ],
    )
    flops = 4 * kv_heads * rows * n_qb * 1536 * head_dim
    return pl.pallas_call(
        kernel,
        grid_spec=grid_spec,
        out_shape=jax.ShapeDtypeStruct(queries.shape, queries.dtype),
        compiler_params=pltpu.CompilerParams(dimension_semantics=("arbitrary", "arbitrary")),
        cost_estimate=pl.CostEstimate(
            flops=flops, transcendentals=flops // (4 * head_dim), bytes_accessed=2 * queries.size * 2 + both.size * 2
        ),
    )(meta, where, queries, both, both, row_start)


def gather_rows(x, chips):
    seq_size = 2 * chips
    me = lax.axis_index("seq")
    if chips != 4:
        return lax.all_gather(x, "seq", axis=0, tiled=True), jnp.arange(seq_size, dtype=jnp.int32)

    def swap(value, bit):
        return lax.ppermute(value, "seq", [(i, i ^ bit) for i in range(seq_size)])

    from_partner = swap(x, 1)
    from_x = swap(x, 2)
    from_y = swap(x, 4)
    forward = jnp.where(me % 2 == 0, from_y, from_x)
    from_diagonal = lax.ppermute(
        forward, "seq", [(i, i ^ 2) if i % 2 == 0 else (i, i ^ 4) for i in range(seq_size)]
    )
    by_mask = [
        x,
        from_partner,
        from_x,
        swap(from_x, 1),
        from_y,
        swap(from_y, 1),
        from_diagonal,
        swap(from_diagonal, 1),
    ]
    where = jnp.bitwise_xor(jnp.arange(seq_size, dtype=jnp.int32), me)
    return jnp.concatenate(by_mask, axis=0), where


def shards(
    chips,
    tp_size,
    hidden,
    norm_gain,
    query_weight,
    key_weight,
    value_weight,
    query_gain,
    key_gain,
    lengths,
    page_table,
):
    row_count = hidden.shape[0]
    head_dim = query_gain.shape[0]
    query_cols = query_weight.shape[1]
    key_cols = key_weight.shape[1]
    kv_heads = key_cols // head_dim
    group_size = query_cols // key_cols
    seq_rank = lax.axis_index("seq")
    prompt_ends = jnp.cumsum(lengths)
    tp_rank = lax.axis_index("tp")
    pieces = [hidden]
    for shift in range(1, tp_size):
        pairs = [(i, (i + shift) % tp_size) for i in range(tp_size)]
        pieces.append(lax.ppermute(hidden, "tp", pairs))
    gathered = jnp.concatenate(
        [lax.select_n((tp_rank - u) % tp_size, *pieces) for u in range(tp_size)], axis=1
    )
    widened = gathered.astype(jnp.float32)
    normed = (
        widened
        * lax.rsqrt(jnp.mean(widened * widened, axis=-1, keepdims=True) + epsilon)
        * norm_gain
    ).astype(jnp.bfloat16)
    server_block = jnp.concatenate([query_weight, key_weight, value_weight], axis=1).astype(
        jnp.bfloat16
    )
    full_block = lax.all_gather(server_block, "seq", axis=0, tiled=True)
    normed_perm = normed
    projected_kv = jnp.dot(normed_perm, full_block[:, query_cols:], preferred_element_type=jnp.float32)
    slot_index = seq_rank * row_count + jnp.arange(row_count, dtype=jnp.int32)
    segment_id, position = position_of(slot_index, prompt_ends, lengths)
    key_rows = rotate(
        head_norm(projected_kv[:, :key_cols].reshape(row_count, kv_heads, head_dim), key_gain),
        position,
    )
    key_rows = key_rows.reshape(row_count, key_cols).astype(jnp.bfloat16)
    values = projected_kv[:, key_cols:].astype(jnp.bfloat16)
    local_kv = jnp.concatenate([key_rows, values], axis=1)
    both_piece, where = gather_rows(local_kv, chips)
    projected_q = jnp.dot(normed_perm, full_block[:, :query_cols], preferred_element_type=jnp.float32)
    queries = rotate(
        head_norm(projected_q.reshape(row_count, query_cols // head_dim, head_dim), query_gain),
        position,
    )
    queries = queries.reshape(row_count, query_cols).astype(jnp.bfloat16)
    block_q = 256
    block_k = 512
    row_start = slot_index - position
    firsts = row_start[::block_q]
    lasts = row_start[block_q - 1 :: block_q]
    meta = jnp.stack([slot_index[::block_q], firsts, lasts], axis=1).reshape(-1).astype(jnp.int32)
    attention = flash(
        meta, where, queries, both_piece, row_start.reshape(row_count, 1).astype(jnp.int32),
        kv_heads, group_size, head_dim, block_q, block_k, chips,
    )
    pages_dev = row_count // PAGE
    owned_pages = seq_rank * pages_dev + jnp.arange(pages_dev, dtype=jnp.int32)
    page_count = page_table.shape[0]
    source_block = jnp.sum(
        jnp.where(
            page_table[None, :] == owned_pages[:, None],
            jnp.arange(page_count, dtype=jnp.int32)[None, :],
            0,
        ),
        axis=1,
    )
    stored = where[source_block // pages_dev] * row_count + (source_block % pages_dev) * PAGE
    pages = jnp.stack([lax.dynamic_slice_in_dim(both_piece, stored[p], PAGE, 0) for p in range(pages_dev)])
    key_cache = pages[:, :, :key_cols].reshape(pages_dev, PAGE, kv_heads, head_dim).transpose(0, 2, 1, 3)
    value_cache = pages[:, :, key_cols:].reshape(pages_dev, PAGE, kv_heads, head_dim).transpose(0, 2, 1, 3)
    return (attention, key_cache, value_cache)


def solution(mesh):
    seq_size = mesh.shape["seq"]
    tp_size = mesh.shape["tp"]
    chips = seq_size // 2
    return jax.shard_map(
        partial(shards, chips, tp_size),
        mesh=mesh,
        in_specs=(
            P("seq", "tp"),
            P(),
            P("seq", "tp"),
            P("seq", "tp"),
            P("seq", "tp"),
            P(),
            P(),
            P(),
            P(),
        ),
        out_specs=(P("seq", "tp"), P("seq", "tp", None, None), P("seq", "tp", None, None)),
        check_vma=False,
    )
```

```python
import math
from functools import partial

import jax
import jax.numpy as jnp
from jax import lax
from jax.sharding import Mesh, PartitionSpec as P
from jax.experimental import pallas as pl
from jax.experimental.pallas import tpu as pltpu

PAGE = 128


epsilon = 1e-06
excluded = -1e30


def segment_of(slot_index, prompt_ends):
    return jnp.sum((slot_index[..., None] >= prompt_ends).astype(jnp.int32), axis=-1)


def position_of(slot_index, prompt_ends, lengths):
    segment_id = segment_of(slot_index, prompt_ends)
    prompt_starts = prompt_ends - lengths
    labels = jnp.arange(lengths.shape[0], dtype=jnp.int32)
    picked = jnp.sum(jnp.where(segment_id[..., None] == labels, prompt_starts, 0), axis=-1)
    return (segment_id, slot_index - picked)


def head_norm(vectors, gain):
    mean_sq = jnp.mean(vectors * vectors, axis=-1, keepdims=True)
    return vectors * lax.rsqrt(mean_sq + epsilon) * gain


def rotate(vectors, position):
    head_dim = vectors.shape[-1]
    half_dim = head_dim // 2
    frequency = 1000000.0 ** (-(jnp.arange(half_dim, dtype=jnp.float32) * 2.0 / head_dim))
    angles = position.astype(jnp.float32)[:, None] * frequency[None, :]
    cosine = jnp.cos(angles)[:, None, :]
    sine_part = jnp.sin(angles)[:, None, :]
    front = vectors[..., :half_dim]
    back_half = vectors[..., half_dim:]
    return jnp.concatenate(
        [front * cosine - back_half * sine_part, back_half * cosine + front * sine_part], axis=-1
    )


def attend(
    query_block,
    query_slots,
    query_segments,
    key_piece,
    value_piece,
    key_slots,
    key_segments,
    kv_heads,
    group_size,
    head_dim,
    running,
):
    running_max, denominator, accumulator = running
    half_rows = query_block.shape[0]
    key_count = key_piece.shape[0]
    scores = jnp.einsum(
        "qkgd,nkd->kgqn",
        query_block.reshape(half_rows, kv_heads, group_size, head_dim),
        key_piece.reshape(key_count, kv_heads, head_dim),
        preferred_element_type=jnp.float32,
    ) * head_dim ** (-0.5)
    allowed = (key_segments[None, :] == query_segments[:, None]) & (
        key_slots[None, :] <= query_slots[:, None]
    )
    masked = jnp.where(allowed, scores, excluded)
    new_max = jnp.maximum(running_max, jnp.max(masked, axis=-1))
    weights = jnp.where(allowed, jnp.exp(scores - new_max[..., None]), 0.0)
    denominator = jnp.sum(weights, axis=-1)
    probs = weights.astype(jnp.bfloat16)
    accumulator = jnp.einsum(
        "kgqn,nkd->kgqd",
        probs,
        value_piece.reshape(key_count, kv_heads, head_dim),
        preferred_element_type=jnp.float32,
    )
    return (new_max, denominator, accumulator)


def flash_kernel(group_size, block_q, block_k, head_dim, chips, rank_rows, meta_ref, where_ref, q_ref, k_ref, v_ref, rs_ref, o_ref, m_sc, l_sc, acc_sc):
    i = pl.program_id(1)
    r0 = meta_ref[3 * i]
    s_first = meta_ref[3 * i + 1]
    s_last = meta_ref[3 * i + 2]
    rows = group_size * block_q
    q = q_ref[...]
    qs = jnp.concatenate([q[:, g * head_dim : (g + 1) * head_dim] for g in range(group_size)], axis=0)
    rstart = jnp.concatenate([rs_ref[...]] * group_size, axis=0)
    row_slot = r0 + lax.broadcasted_iota(jnp.int32, (group_size, block_q, 1), 1).reshape(rows, 1)
    m_sc[...] = jnp.full(m_sc.shape, excluded, jnp.float32)
    l_sc[...] = jnp.zeros(l_sc.shape, jnp.float32)
    acc_sc[...] = jnp.zeros(acc_sc.shape, jnp.float32)
    scale = head_dim ** (-0.5) * math.log2(math.e)

    def update(kb, masked):
        first = kb * block_k
        stored = pl.multiple_of(where_ref[first // rank_rows] * rank_rows + first % rank_rows, block_k)
        k = k_ref[pl.ds(stored, block_k), :]
        v = v_ref[pl.ds(stored, block_k), :]
        s = lax.dot_general(qs, k, (((1,), (1,)), ((), ())), preferred_element_type=jnp.float32)
        if masked:
            cols = first + lax.broadcasted_iota(jnp.int32, (rows, block_k), 1)
            allowed = (cols >= rstart) & (cols <= row_slot)
            s = jnp.where(allowed, s, 2.0 * excluded)
        s_max = jnp.max(s, axis=1, keepdims=True)
        m_prev = m_sc[...]
        m_next = jnp.maximum(m_prev, s_max)
        alpha = jnp.exp2((m_prev - m_next) * scale)
        p = jnp.exp2((s - m_next[:, :1]) * scale)
        l_sc[...] = alpha * l_sc[...] + jnp.sum(p, axis=1, keepdims=True)
        pv = jnp.dot(p.astype(jnp.bfloat16), v, preferred_element_type=jnp.float32)
        acc_sc[...] = acc_sc[...] * alpha + pv
        m_sc[...] = m_next

    def body(kb, carry):
        lo = kb * block_k
        full = (lo >= s_last) & (lo + block_k - 1 <= r0)

        @pl.when(full)
        def _():
            update(kb, False)

        @pl.when(jnp.logical_not(full))
        def _():
            update(kb, True)

        return carry

    lax.fori_loop(s_first // block_k, (r0 + block_q - 1) // block_k + 1, body, 0)
    res = acc_sc[...] / l_sc[...]
    o_ref[...] = jnp.concatenate(
        [res[g * block_q : (g + 1) * block_q] for g in range(group_size)], axis=1
    ).astype(o_ref.dtype)


def flash(meta, where, queries, both, row_start, kv_heads, group_size, head_dim, block_q, block_k, chips):
    row_count = queries.shape[0]
    key_count = both.shape[0]
    n_qb = row_count // block_q
    rows = group_size * block_q
    kernel = partial(flash_kernel, group_size, block_q, block_k, head_dim, chips, row_count)
    grid_spec = pltpu.PrefetchScalarGridSpec(
        num_scalar_prefetch=2,
        grid=(kv_heads, n_qb),
        in_specs=[
            pl.BlockSpec((block_q, group_size * head_dim), lambda h, i, meta, where: (i, h)),
            pl.BlockSpec((key_count, head_dim), lambda h, i, meta, where: (0, h)),
            pl.BlockSpec((key_count, head_dim), lambda h, i, meta, where: (0, kv_heads + h)),
            pl.BlockSpec((block_q, 1), lambda h, i, meta, where: (i, 0)),
        ],
        out_specs=pl.BlockSpec((block_q, group_size * head_dim), lambda h, i, meta, where: (i, h)),
        scratch_shapes=[
            pltpu.VMEM((rows, head_dim), jnp.float32),
            pltpu.VMEM((rows, head_dim), jnp.float32),
            pltpu.VMEM((rows, head_dim), jnp.float32),
        ],
    )
    flops = 4 * kv_heads * rows * n_qb * 1536 * head_dim
    return pl.pallas_call(
        kernel,
        grid_spec=grid_spec,
        out_shape=jax.ShapeDtypeStruct(queries.shape, queries.dtype),
        compiler_params=pltpu.CompilerParams(dimension_semantics=("arbitrary", "arbitrary")),
        cost_estimate=pl.CostEstimate(
            flops=flops, transcendentals=flops // (4 * head_dim), bytes_accessed=2 * queries.size * 2 + both.size * 2
        ),
    )(meta, where, queries, both, both, row_start)


def regroup_kernel(q_ref, k_ref, v_ref, o_ref):
    q_cols = q_ref.shape[1]
    k_cols = k_ref.shape[1]
    o_ref[:, :q_cols] = q_ref[...].astype(o_ref.dtype)
    o_ref[:, q_cols : q_cols + k_cols] = k_ref[...].astype(o_ref.dtype)
    o_ref[:, q_cols + k_cols :] = v_ref[...].astype(o_ref.dtype)


def regroup(query_weight, key_weight, value_weight):
    rows = query_weight.shape[0]
    cols = query_weight.shape[1] + key_weight.shape[1] + value_weight.shape[1]
    return pl.pallas_call(
        regroup_kernel,
        out_shape=jax.ShapeDtypeStruct((rows, cols), jnp.bfloat16),
        cost_estimate=pl.CostEstimate(flops=0, transcendentals=0, bytes_accessed=rows * cols * 6),
    )(query_weight, key_weight, value_weight)


def gather_rows(x, chips):
    seq_size = 2 * chips
    me = lax.axis_index("seq")
    if chips != 4:
        return lax.all_gather(x, "seq", axis=0, tiled=True), jnp.arange(seq_size, dtype=jnp.int32)

    def swap(value, bit):
        return lax.ppermute(value, "seq", [(i, i ^ bit) for i in range(seq_size)])

    from_partner = swap(x, 1)
    from_x = swap(x, 2)
    from_y = swap(x, 4)
    forward = jnp.where(me % 2 == 0, from_y, from_x)
    from_diagonal = lax.ppermute(
        forward, "seq", [(i, i ^ 2) if i % 2 == 0 else (i, i ^ 4) for i in range(seq_size)]
    )
    by_mask = [
        x,
        from_partner,
        from_x,
        swap(from_x, 1),
        from_y,
        swap(from_y, 1),
        from_diagonal,
        swap(from_diagonal, 1),
    ]
    where = jnp.bitwise_xor(jnp.arange(seq_size, dtype=jnp.int32), me)
    return jnp.concatenate(by_mask, axis=0), where


def shards(
    chips,
    tp_size,
    hidden,
    norm_gain,
    query_weight,
    key_weight,
    value_weight,
    query_gain,
    key_gain,
    lengths,
    page_table,
):
    row_count = hidden.shape[0]
    head_dim = query_gain.shape[0]
    query_cols = query_weight.shape[1]
    key_cols = key_weight.shape[1]
    kv_heads = key_cols // head_dim
    group_size = query_cols // key_cols
    seq_rank = lax.axis_index("seq")
    prompt_ends = jnp.cumsum(lengths)
    tp_rank = lax.axis_index("tp")
    pieces = [hidden]
    for shift in range(1, tp_size):
        pairs = [(i, (i + shift) % tp_size) for i in range(tp_size)]
        pieces.append(lax.ppermute(hidden, "tp", pairs))
    gathered = jnp.concatenate(
        [lax.select_n((tp_rank - u) % tp_size, *pieces) for u in range(tp_size)], axis=1
    )
    widened = gathered.astype(jnp.float32)
    normed = (
        widened
        * lax.rsqrt(jnp.mean(widened * widened, axis=-1, keepdims=True) + epsilon)
        * norm_gain
    ).astype(jnp.bfloat16)
    server_block = regroup(query_weight, key_weight, value_weight)
    full_block = lax.all_gather(server_block, "seq", axis=0, tiled=True)
    normed_perm = normed
    projected_kv = jnp.dot(normed_perm, full_block[:, query_cols:], preferred_element_type=jnp.float32)
    slot_index = seq_rank * row_count + jnp.arange(row_count, dtype=jnp.int32)
    segment_id, position = position_of(slot_index, prompt_ends, lengths)
    key_rows = rotate(
        head_norm(projected_kv[:, :key_cols].reshape(row_count, kv_heads, head_dim), key_gain),
        position,
    )
    key_rows = key_rows.reshape(row_count, key_cols).astype(jnp.bfloat16)
    values = projected_kv[:, key_cols:].astype(jnp.bfloat16)
    local_kv = jnp.concatenate([key_rows, values], axis=1)
    both_piece, where = gather_rows(local_kv, chips)
    projected_q = jnp.dot(normed_perm, full_block[:, :query_cols], preferred_element_type=jnp.float32)
    queries = rotate(
        head_norm(projected_q.reshape(row_count, query_cols // head_dim, head_dim), query_gain),
        position,
    )
    queries = queries.reshape(row_count, query_cols).astype(jnp.bfloat16)
    block_q = 128
    block_k = 512
    row_start = slot_index - position
    firsts = row_start[::block_q]
    lasts = row_start[block_q - 1 :: block_q]
    meta = jnp.stack([slot_index[::block_q], firsts, lasts], axis=1).reshape(-1).astype(jnp.int32)
    attention = flash(
        meta, where, queries, both_piece, row_start.reshape(row_count, 1).astype(jnp.int32),
        kv_heads, group_size, head_dim, block_q, block_k, chips,
    )
    pages_dev = row_count // PAGE
    owned_pages = seq_rank * pages_dev + jnp.arange(pages_dev, dtype=jnp.int32)
    page_count = page_table.shape[0]
    source_block = jnp.sum(
        jnp.where(
            page_table[None, :] == owned_pages[:, None],
            jnp.arange(page_count, dtype=jnp.int32)[None, :],
            0,
        ),
        axis=1,
    )
    stored = where[source_block // pages_dev] * row_count + (source_block % pages_dev) * PAGE
    pages = jnp.stack([lax.dynamic_slice_in_dim(both_piece, stored[p], PAGE, 0) for p in range(pages_dev)])
    key_cache = pages[:, :, :key_cols].reshape(pages_dev, PAGE, kv_heads, head_dim).transpose(0, 2, 1, 3)
    value_cache = pages[:, :, key_cols:].reshape(pages_dev, PAGE, kv_heads, head_dim).transpose(0, 2, 1, 3)
    return (attention, key_cache, value_cache)


def solution(mesh):
    seq_size = mesh.shape["seq"]
    tp_size = mesh.shape["tp"]
    chips = seq_size // 2
    return jax.shard_map(
        partial(shards, chips, tp_size),
        mesh=mesh,
        in_specs=(
            P("seq", "tp"),
            P(),
            P("seq", "tp"),
            P("seq", "tp"),
            P("seq", "tp"),
            P(),
            P(),
            P(),
            P(),
        ),
        out_specs=(P("seq", "tp"), P("seq", "tp", None, None), P("seq", "tp", None, None)),
        check_vma=False,
    )
```

```python
import math
from functools import partial

import jax
import jax.numpy as jnp
from jax import lax
from jax.sharding import Mesh, PartitionSpec as P
from jax.experimental import pallas as pl
from jax.experimental.pallas import tpu as pltpu

PAGE = 128


epsilon = 1e-06
excluded = -1e30


def segment_of(slot_index, prompt_ends):
    return jnp.sum((slot_index[..., None] >= prompt_ends).astype(jnp.int32), axis=-1)


def position_of(slot_index, prompt_ends, lengths):
    segment_id = segment_of(slot_index, prompt_ends)
    prompt_starts = prompt_ends - lengths
    labels = jnp.arange(lengths.shape[0], dtype=jnp.int32)
    picked = jnp.sum(jnp.where(segment_id[..., None] == labels, prompt_starts, 0), axis=-1)
    return (segment_id, slot_index - picked)


def head_norm(vectors, gain):
    mean_sq = jnp.mean(vectors * vectors, axis=-1, keepdims=True)
    return vectors * lax.rsqrt(mean_sq + epsilon) * gain


def rotate(vectors, position):
    head_dim = vectors.shape[-1]
    half_dim = head_dim // 2
    frequency = 1000000.0 ** (-(jnp.arange(half_dim, dtype=jnp.float32) * 2.0 / head_dim))
    angles = position.astype(jnp.float32)[:, None] * frequency[None, :]
    cosine = jnp.cos(angles)[:, None, :]
    sine_part = jnp.sin(angles)[:, None, :]
    front = vectors[..., :half_dim]
    back_half = vectors[..., half_dim:]
    return jnp.concatenate(
        [front * cosine - back_half * sine_part, back_half * cosine + front * sine_part], axis=-1
    )


def attend(
    query_block,
    query_slots,
    query_segments,
    key_piece,
    value_piece,
    key_slots,
    key_segments,
    kv_heads,
    group_size,
    head_dim,
    running,
):
    running_max, denominator, accumulator = running
    half_rows = query_block.shape[0]
    key_count = key_piece.shape[0]
    scores = jnp.einsum(
        "qkgd,nkd->kgqn",
        query_block.reshape(half_rows, kv_heads, group_size, head_dim),
        key_piece.reshape(key_count, kv_heads, head_dim),
        preferred_element_type=jnp.float32,
    ) * head_dim ** (-0.5)
    allowed = (key_segments[None, :] == query_segments[:, None]) & (
        key_slots[None, :] <= query_slots[:, None]
    )
    masked = jnp.where(allowed, scores, excluded)
    new_max = jnp.maximum(running_max, jnp.max(masked, axis=-1))
    weights = jnp.where(allowed, jnp.exp(scores - new_max[..., None]), 0.0)
    denominator = jnp.sum(weights, axis=-1)
    probs = weights.astype(jnp.bfloat16)
    accumulator = jnp.einsum(
        "kgqn,nkd->kgqd",
        probs,
        value_piece.reshape(key_count, kv_heads, head_dim),
        preferred_element_type=jnp.float32,
    )
    return (new_max, denominator, accumulator)


def flash_kernel(group_size, block_q, block_k, head_dim, chips, rank_rows, meta_ref, where_ref, q_ref, k_ref, v_ref, rs_ref, o_ref, m_sc, l_sc, acc_sc):
    i = pl.program_id(1)
    r0 = meta_ref[3 * i]
    s_first = meta_ref[3 * i + 1]
    s_last = meta_ref[3 * i + 2]
    rows = group_size * block_q
    q = q_ref[...]
    qs = jnp.concatenate([q[:, g * head_dim : (g + 1) * head_dim] for g in range(group_size)], axis=0)
    rstart = jnp.concatenate([rs_ref[...]] * group_size, axis=0)
    row_slot = r0 + lax.broadcasted_iota(jnp.int32, (group_size, block_q, 1), 1).reshape(rows, 1)
    m_sc[...] = jnp.full(m_sc.shape, excluded, jnp.float32)
    l_sc[...] = jnp.zeros(l_sc.shape, jnp.float32)
    acc_sc[...] = jnp.zeros(acc_sc.shape, jnp.float32)
    scale = head_dim ** (-0.5) * math.log2(math.e)

    def update(kb, masked):
        first = kb * block_k
        stored = pl.multiple_of(where_ref[first // rank_rows] * rank_rows + first % rank_rows, block_k)
        k = k_ref[pl.ds(stored, block_k), :]
        v = v_ref[pl.ds(stored, block_k), :]
        s = lax.dot_general(qs, k, (((1,), (1,)), ((), ())), preferred_element_type=jnp.float32)
        if masked:
            cols = first + lax.broadcasted_iota(jnp.int32, (rows, block_k), 1)
            if masked == "causal":
                allowed = cols <= row_slot
            elif masked == "start":
                allowed = cols >= rstart
            else:
                allowed = (cols >= rstart) & (cols <= row_slot)
            s = jnp.where(allowed, s, 2.0 * excluded)
        s_max = jnp.max(s, axis=1, keepdims=True)
        m_prev = m_sc[...]
        m_next = jnp.maximum(m_prev, s_max)
        alpha = jnp.exp2((m_prev - m_next) * scale)
        p = jnp.exp2((s - m_next[:, :1]) * scale)
        l_sc[...] = alpha * l_sc[...] + jnp.sum(p, axis=1, keepdims=True)
        pv = jnp.dot(p.astype(jnp.bfloat16), v, preferred_element_type=jnp.float32)
        acc_sc[...] = acc_sc[...] * alpha + pv
        m_sc[...] = m_next

    def body(kb, carry):
        lo = kb * block_k
        after_start = lo >= s_last
        before_diagonal = lo + block_k - 1 <= r0

        @pl.when(after_start & before_diagonal)
        def _():
            update(kb, None)

        @pl.when(after_start & jnp.logical_not(before_diagonal))
        def _():
            update(kb, "causal")

        @pl.when(jnp.logical_not(after_start) & before_diagonal)
        def _():
            update(kb, "start")

        @pl.when(jnp.logical_not(after_start) & jnp.logical_not(before_diagonal))
        def _():
            update(kb, "both")

        return carry

    lax.fori_loop(s_first // block_k, (r0 + block_q - 1) // block_k + 1, body, 0)
    res = acc_sc[...] / l_sc[...]
    o_ref[...] = jnp.concatenate(
        [res[g * block_q : (g + 1) * block_q] for g in range(group_size)], axis=1
    ).astype(o_ref.dtype)


def flash(meta, where, queries, both, row_start, kv_heads, group_size, head_dim, block_q, block_k, chips):
    row_count = queries.shape[0]
    key_count = both.shape[0]
    n_qb = row_count // block_q
    rows = group_size * block_q
    kernel = partial(flash_kernel, group_size, block_q, block_k, head_dim, chips, row_count)
    grid_spec = pltpu.PrefetchScalarGridSpec(
        num_scalar_prefetch=2,
        grid=(kv_heads, n_qb),
        in_specs=[
            pl.BlockSpec((block_q, group_size * head_dim), lambda h, i, meta, where: (i, h)),
            pl.BlockSpec((key_count, head_dim), lambda h, i, meta, where: (0, h)),
            pl.BlockSpec((key_count, head_dim), lambda h, i, meta, where: (0, kv_heads + h)),
            pl.BlockSpec((block_q, 1), lambda h, i, meta, where: (i, 0)),
        ],
        out_specs=pl.BlockSpec((block_q, group_size * head_dim), lambda h, i, meta, where: (i, h)),
        scratch_shapes=[
            pltpu.VMEM((rows, head_dim), jnp.float32),
            pltpu.VMEM((rows, head_dim), jnp.float32),
            pltpu.VMEM((rows, head_dim), jnp.float32),
        ],
    )
    flops = 4 * kv_heads * rows * n_qb * 1536 * head_dim
    return pl.pallas_call(
        kernel,
        grid_spec=grid_spec,
        out_shape=jax.ShapeDtypeStruct(queries.shape, queries.dtype),
        compiler_params=pltpu.CompilerParams(dimension_semantics=("arbitrary", "arbitrary")),
        cost_estimate=pl.CostEstimate(
            flops=flops, transcendentals=flops // (4 * head_dim), bytes_accessed=2 * queries.size * 2 + both.size * 2
        ),
    )(meta, where, queries, both, both, row_start)


def regroup_kernel(q_ref, k_ref, v_ref, o_ref):
    q_cols = q_ref.shape[1]
    k_cols = k_ref.shape[1]
    o_ref[:, :q_cols] = q_ref[...].astype(o_ref.dtype)
    o_ref[:, q_cols : q_cols + k_cols] = k_ref[...].astype(o_ref.dtype)
    o_ref[:, q_cols + k_cols :] = v_ref[...].astype(o_ref.dtype)


def regroup(query_weight, key_weight, value_weight):
    rows = query_weight.shape[0]
    cols = query_weight.shape[1] + key_weight.shape[1] + value_weight.shape[1]
    return pl.pallas_call(
        regroup_kernel,
        out_shape=jax.ShapeDtypeStruct((rows, cols), jnp.bfloat16),
        cost_estimate=pl.CostEstimate(flops=0, transcendentals=0, bytes_accessed=rows * cols * 6),
    )(query_weight, key_weight, value_weight)


def gather_rows(x, chips):
    seq_size = 2 * chips
    me = lax.axis_index("seq")
    if chips != 4:
        return lax.all_gather(x, "seq", axis=0, tiled=True), jnp.arange(seq_size, dtype=jnp.int32)

    def swap(value, bit):
        return lax.ppermute(value, "seq", [(i, i ^ bit) for i in range(seq_size)])

    from_partner = swap(x, 1)
    from_x = swap(x, 2)
    from_y = swap(x, 4)
    forward = jnp.where(me % 2 == 0, from_y, from_x)
    from_diagonal = lax.ppermute(
        forward, "seq", [(i, i ^ 2) if i % 2 == 0 else (i, i ^ 4) for i in range(seq_size)]
    )
    by_mask = [
        x,
        from_partner,
        from_x,
        swap(from_x, 1),
        from_y,
        swap(from_y, 1),
        from_diagonal,
        swap(from_diagonal, 1),
    ]
    where = jnp.bitwise_xor(jnp.arange(seq_size, dtype=jnp.int32), me)
    return jnp.concatenate(by_mask, axis=0), where


def shards(
    chips,
    tp_size,
    hidden,
    norm_gain,
    query_weight,
    key_weight,
    value_weight,
    query_gain,
    key_gain,
    lengths,
    page_table,
):
    row_count = hidden.shape[0]
    head_dim = query_gain.shape[0]
    query_cols = query_weight.shape[1]
    key_cols = key_weight.shape[1]
    kv_heads = key_cols // head_dim
    group_size = query_cols // key_cols
    seq_rank = lax.axis_index("seq")
    prompt_ends = jnp.cumsum(lengths)
    tp_rank = lax.axis_index("tp")
    pieces = [hidden]
    for shift in range(1, tp_size):
        pairs = [(i, (i + shift) % tp_size) for i in range(tp_size)]
        pieces.append(lax.ppermute(hidden, "tp", pairs))
    gathered = jnp.concatenate(
        [lax.select_n((tp_rank - u) % tp_size, *pieces) for u in range(tp_size)], axis=1
    )
    widened = gathered.astype(jnp.float32)
    normed = (
        widened
        * lax.rsqrt(jnp.mean(widened * widened, axis=-1, keepdims=True) + epsilon)
        * norm_gain
    ).astype(jnp.bfloat16)
    server_block = regroup(query_weight, key_weight, value_weight)
    full_block = lax.all_gather(server_block, "seq", axis=0, tiled=True)
    normed_perm = normed
    projected_kv = jnp.dot(normed_perm, full_block[:, query_cols:], preferred_element_type=jnp.float32)
    slot_index = seq_rank * row_count + jnp.arange(row_count, dtype=jnp.int32)
    segment_id, position = position_of(slot_index, prompt_ends, lengths)
    key_rows = rotate(
        head_norm(projected_kv[:, :key_cols].reshape(row_count, kv_heads, head_dim), key_gain),
        position,
    )
    key_rows = key_rows.reshape(row_count, key_cols).astype(jnp.bfloat16)
    values = projected_kv[:, key_cols:].astype(jnp.bfloat16)
    local_kv = jnp.concatenate([key_rows, values], axis=1)
    both_piece, where = gather_rows(local_kv, chips)
    projected_q = jnp.dot(normed_perm, full_block[:, :query_cols], preferred_element_type=jnp.float32)
    queries = rotate(
        head_norm(projected_q.reshape(row_count, query_cols // head_dim, head_dim), query_gain),
        position,
    )
    queries = queries.reshape(row_count, query_cols).astype(jnp.bfloat16)
    block_q = 128
    block_k = 512
    row_start = slot_index - position
    firsts = row_start[::block_q]
    lasts = row_start[block_q - 1 :: block_q]
    meta = jnp.stack([slot_index[::block_q], firsts, lasts], axis=1).reshape(-1).astype(jnp.int32)
    attention = flash(
        meta, where, queries, both_piece, row_start.reshape(row_count, 1).astype(jnp.int32),
        kv_heads, group_size, head_dim, block_q, block_k, chips,
    )
    pages_dev = row_count // PAGE
    owned_pages = seq_rank * pages_dev + jnp.arange(pages_dev, dtype=jnp.int32)
    page_count = page_table.shape[0]
    source_block = jnp.sum(
        jnp.where(
            page_table[None, :] == owned_pages[:, None],
            jnp.arange(page_count, dtype=jnp.int32)[None, :],
            0,
        ),
        axis=1,
    )
    stored = where[source_block // pages_dev] * row_count + (source_block % pages_dev) * PAGE
    pages = jnp.stack([lax.dynamic_slice_in_dim(both_piece, stored[p], PAGE, 0) for p in range(pages_dev)])
    key_cache = pages[:, :, :key_cols].reshape(pages_dev, PAGE, kv_heads, head_dim).transpose(0, 2, 1, 3)
    value_cache = pages[:, :, key_cols:].reshape(pages_dev, PAGE, kv_heads, head_dim).transpose(0, 2, 1, 3)
    return (attention, key_cache, value_cache)


def solution(mesh):
    seq_size = mesh.shape["seq"]
    tp_size = mesh.shape["tp"]
    chips = seq_size // 2
    return jax.shard_map(
        partial(shards, chips, tp_size),
        mesh=mesh,
        in_specs=(
            P("seq", "tp"),
            P(),
            P("seq", "tp"),
            P("seq", "tp"),
            P("seq", "tp"),
            P(),
            P(),
            P(),
            P(),
        ),
        out_specs=(P("seq", "tp"), P("seq", "tp", None, None), P("seq", "tp", None, None)),
        check_vma=False,
    )
```

```python
import math
from functools import partial

import jax
import jax.numpy as jnp
from jax import lax
from jax.sharding import Mesh, PartitionSpec as P
from jax.experimental import pallas as pl
from jax.experimental.pallas import tpu as pltpu

PAGE = 128


epsilon = 1e-06
excluded = -1e30


def segment_of(slot_index, prompt_ends):
    return jnp.sum((slot_index[..., None] >= prompt_ends).astype(jnp.int32), axis=-1)


def position_of(slot_index, prompt_ends, lengths):
    segment_id = segment_of(slot_index, prompt_ends)
    prompt_starts = prompt_ends - lengths
    labels = jnp.arange(lengths.shape[0], dtype=jnp.int32)
    picked = jnp.sum(jnp.where(segment_id[..., None] == labels, prompt_starts, 0), axis=-1)
    return (segment_id, slot_index - picked)


def head_norm(vectors, gain):
    mean_sq = jnp.mean(vectors * vectors, axis=-1, keepdims=True)
    return vectors * lax.rsqrt(mean_sq + epsilon) * gain


def rotate(vectors, position):
    head_dim = vectors.shape[-1]
    half_dim = head_dim // 2
    frequency = 1000000.0 ** (-(jnp.arange(half_dim, dtype=jnp.float32) * 2.0 / head_dim))
    angles = position.astype(jnp.float32)[:, None] * frequency[None, :]
    cosine = jnp.cos(angles)[:, None, :]
    sine_part = jnp.sin(angles)[:, None, :]
    front = vectors[..., :half_dim]
    back_half = vectors[..., half_dim:]
    return jnp.concatenate(
        [front * cosine - back_half * sine_part, back_half * cosine + front * sine_part], axis=-1
    )


def attend(
    query_block,
    query_slots,
    query_segments,
    key_piece,
    value_piece,
    key_slots,
    key_segments,
    kv_heads,
    group_size,
    head_dim,
    running,
):
    running_max, denominator, accumulator = running
    half_rows = query_block.shape[0]
    key_count = key_piece.shape[0]
    scores = jnp.einsum(
        "qkgd,nkd->kgqn",
        query_block.reshape(half_rows, kv_heads, group_size, head_dim),
        key_piece.reshape(key_count, kv_heads, head_dim),
        preferred_element_type=jnp.float32,
    ) * head_dim ** (-0.5)
    allowed = (key_segments[None, :] == query_segments[:, None]) & (
        key_slots[None, :] <= query_slots[:, None]
    )
    masked = jnp.where(allowed, scores, excluded)
    new_max = jnp.maximum(running_max, jnp.max(masked, axis=-1))
    weights = jnp.where(allowed, jnp.exp(scores - new_max[..., None]), 0.0)
    denominator = jnp.sum(weights, axis=-1)
    probs = weights.astype(jnp.bfloat16)
    accumulator = jnp.einsum(
        "kgqn,nkd->kgqd",
        probs,
        value_piece.reshape(key_count, kv_heads, head_dim),
        preferred_element_type=jnp.float32,
    )
    return (new_max, denominator, accumulator)


def flash_kernel(group_size, block_q, block_k, head_dim, chips, rank_rows, meta_ref, where_ref, q_ref, k_ref, v_ref, rs_ref, o_ref, m_sc, l_sc, acc_sc):
    i = pl.program_id(1)
    r0 = meta_ref[3 * i]
    s_first = meta_ref[3 * i + 1]
    s_last = meta_ref[3 * i + 2]
    rows = group_size * block_q
    q = q_ref[...]
    qs = jnp.concatenate([q[:, g * head_dim : (g + 1) * head_dim] for g in range(group_size)], axis=0)
    rstart = jnp.concatenate([rs_ref[...]] * group_size, axis=0)
    row_slot = r0 + lax.broadcasted_iota(jnp.int32, (group_size, block_q, 1), 1).reshape(rows, 1)
    m_sc[...] = jnp.full(m_sc.shape, excluded, jnp.float32)
    l_sc[...] = jnp.zeros(l_sc.shape, jnp.float32)
    acc_sc[...] = jnp.zeros(acc_sc.shape, jnp.float32)
    scale = head_dim ** (-0.5) * math.log2(math.e)

    def update(kb, masked):
        first = kb * block_k
        stored = pl.multiple_of(where_ref[first // rank_rows] * rank_rows + first % rank_rows, block_k)
        k = k_ref[pl.ds(stored, block_k), :]
        v = v_ref[pl.ds(stored, block_k), :]
        s = lax.dot_general(qs, k, (((1,), (1,)), ((), ())), preferred_element_type=jnp.float32)
        if masked:
            cols = first + lax.broadcasted_iota(jnp.int32, (rows, block_k), 1)
            allowed = (cols >= rstart) & (cols <= row_slot)
            s = jnp.where(allowed, s, 2.0 * excluded)
        s_max = jnp.max(s, axis=1, keepdims=True)
        m_prev = m_sc[...]
        m_next = jnp.maximum(m_prev, s_max)
        alpha = jnp.exp2((m_prev - m_next) * scale)
        p = jnp.exp2((s - m_next[:, :1]) * scale)
        l_sc[...] = alpha * l_sc[...] + jnp.sum(p, axis=1, keepdims=True)
        pv = jnp.dot(p.astype(jnp.bfloat16), v, preferred_element_type=jnp.float32)
        acc_sc[...] = acc_sc[...] * alpha + pv
        m_sc[...] = m_next

    def body(kb, carry):
        lo = kb * block_k
        full = (lo >= s_last) & (lo + block_k - 1 <= r0)

        @pl.when(full)
        def _():
            update(kb, False)

        @pl.when(jnp.logical_not(full))
        def _():
            update(kb, True)

        return carry

    lax.fori_loop(s_first // block_k, (r0 + block_q - 1) // block_k + 1, body, 0)
    res = acc_sc[...] / l_sc[...]
    o_ref[...] = jnp.concatenate(
        [res[g * block_q : (g + 1) * block_q] for g in range(group_size)], axis=1
    ).astype(o_ref.dtype)


def flash(meta, where, queries, both, row_start, kv_heads, group_size, head_dim, block_q, block_k, chips):
    row_count = queries.shape[0]
    key_count = both.shape[0]
    n_qb = row_count // block_q
    rows = group_size * block_q
    kernel = partial(flash_kernel, group_size, block_q, block_k, head_dim, chips, row_count)
    grid_spec = pltpu.PrefetchScalarGridSpec(
        num_scalar_prefetch=2,
        grid=(kv_heads, n_qb),
        in_specs=[
            pl.BlockSpec((block_q, group_size * head_dim), lambda h, i, meta, where: (i, h)),
            pl.BlockSpec((key_count, head_dim), lambda h, i, meta, where: (0, h)),
            pl.BlockSpec((key_count, head_dim), lambda h, i, meta, where: (0, kv_heads + h)),
            pl.BlockSpec((block_q, 1), lambda h, i, meta, where: (i, 0)),
        ],
        out_specs=pl.BlockSpec((block_q, group_size * head_dim), lambda h, i, meta, where: (i, h)),
        scratch_shapes=[
            pltpu.VMEM((rows, head_dim), jnp.float32),
            pltpu.VMEM((rows, head_dim), jnp.float32),
            pltpu.VMEM((rows, head_dim), jnp.float32),
        ],
    )
    flops = 4 * kv_heads * rows * n_qb * 1536 * head_dim
    return pl.pallas_call(
        kernel,
        grid_spec=grid_spec,
        out_shape=jax.ShapeDtypeStruct(queries.shape, queries.dtype),
        compiler_params=pltpu.CompilerParams(dimension_semantics=("arbitrary", "arbitrary")),
        cost_estimate=pl.CostEstimate(
            flops=flops, transcendentals=flops // (4 * head_dim), bytes_accessed=2 * queries.size * 2 + both.size * 2
        ),
    )(meta, where, queries, both, both, row_start)


def regroup_kernel(q_ref, k_ref, v_ref, o_ref):
    q_cols = q_ref.shape[1]
    k_cols = k_ref.shape[1]
    o_ref[:, :q_cols] = q_ref[...].astype(o_ref.dtype)
    o_ref[:, q_cols : q_cols + k_cols] = k_ref[...].astype(o_ref.dtype)
    o_ref[:, q_cols + k_cols :] = v_ref[...].astype(o_ref.dtype)


def regroup(query_weight, key_weight, value_weight):
    rows = query_weight.shape[0]
    cols = query_weight.shape[1] + key_weight.shape[1] + value_weight.shape[1]
    return pl.pallas_call(
        regroup_kernel,
        out_shape=jax.ShapeDtypeStruct((rows, cols), jnp.bfloat16),
        cost_estimate=pl.CostEstimate(flops=0, transcendentals=0, bytes_accessed=rows * cols * 6),
    )(query_weight, key_weight, value_weight)


def gather_rows(x, chips):
    seq_size = 2 * chips
    me = lax.axis_index("seq")
    if chips != 4:
        return lax.all_gather(x, "seq", axis=0, tiled=True), jnp.arange(seq_size, dtype=jnp.int32)

    def swap(value, bit):
        return lax.ppermute(value, "seq", [(i, i ^ bit) for i in range(seq_size)])

    from_partner = swap(x, 1)
    from_x = swap(x, 2)
    from_y = swap(x, 4)
    forward = lax.select_n(me % 2, from_y, from_x)
    from_diagonal = lax.ppermute(
        forward, "seq", [(i, i ^ 2) if i % 2 == 0 else (i, i ^ 4) for i in range(seq_size)]
    )
    by_mask = [
        x,
        from_partner,
        from_x,
        swap(from_x, 1),
        from_y,
        swap(from_y, 1),
        from_diagonal,
        swap(from_diagonal, 1),
    ]
    where = jnp.bitwise_xor(jnp.arange(seq_size, dtype=jnp.int32), me)
    return jnp.concatenate(by_mask, axis=0), where


def shards(
    chips,
    tp_size,
    hidden,
    norm_gain,
    query_weight,
    key_weight,
    value_weight,
    query_gain,
    key_gain,
    lengths,
    page_table,
):
    row_count = hidden.shape[0]
    head_dim = query_gain.shape[0]
    query_cols = query_weight.shape[1]
    key_cols = key_weight.shape[1]
    kv_heads = key_cols // head_dim
    group_size = query_cols // key_cols
    seq_rank = lax.axis_index("seq")
    prompt_ends = jnp.cumsum(lengths)
    tp_rank = lax.axis_index("tp")
    pieces = [hidden]
    for shift in range(1, tp_size):
        pairs = [(i, (i + shift) % tp_size) for i in range(tp_size)]
        pieces.append(lax.ppermute(hidden, "tp", pairs))
    gathered = jnp.concatenate(
        [lax.select_n((tp_rank - u) % tp_size, *pieces) for u in range(tp_size)], axis=1
    )
    widened = gathered.astype(jnp.float32)
    normed = (
        widened
        * lax.rsqrt(jnp.mean(widened * widened, axis=-1, keepdims=True) + epsilon)
        * norm_gain
    ).astype(jnp.bfloat16)
    server_block = regroup(query_weight, key_weight, value_weight)
    full_block = lax.all_gather(server_block, "seq", axis=0, tiled=True)
    normed_perm = normed
    projected_kv = jnp.dot(normed_perm, full_block[:, query_cols:], preferred_element_type=jnp.float32)
    slot_index = seq_rank * row_count + jnp.arange(row_count, dtype=jnp.int32)
    segment_id, position = position_of(slot_index, prompt_ends, lengths)
    key_rows = rotate(
        head_norm(projected_kv[:, :key_cols].reshape(row_count, kv_heads, head_dim), key_gain),
        position,
    )
    key_rows = key_rows.reshape(row_count, key_cols).astype(jnp.bfloat16)
    values = projected_kv[:, key_cols:].astype(jnp.bfloat16)
    local_kv = jnp.concatenate([key_rows, values], axis=1)
    both_piece, where = gather_rows(local_kv, chips)
    projected_q = jnp.dot(normed_perm, full_block[:, :query_cols], preferred_element_type=jnp.float32)
    queries = rotate(
        head_norm(projected_q.reshape(row_count, query_cols // head_dim, head_dim), query_gain),
        position,
    )
    queries = queries.reshape(row_count, query_cols).astype(jnp.bfloat16)
    block_q = 128
    block_k = 512
    row_start = slot_index - position
    firsts = row_start[::block_q]
    lasts = row_start[block_q - 1 :: block_q]
    meta = jnp.stack([slot_index[::block_q], firsts, lasts], axis=1).reshape(-1).astype(jnp.int32)
    attention = flash(
        meta, where, queries, both_piece, row_start.reshape(row_count, 1).astype(jnp.int32),
        kv_heads, group_size, head_dim, block_q, block_k, chips,
    )
    pages_dev = row_count // PAGE
    owned_pages = seq_rank * pages_dev + jnp.arange(pages_dev, dtype=jnp.int32)
    page_count = page_table.shape[0]
    source_block = jnp.sum(
        jnp.where(
            page_table[None, :] == owned_pages[:, None],
            jnp.arange(page_count, dtype=jnp.int32)[None, :],
            0,
        ),
        axis=1,
    )
    stored = where[source_block // pages_dev] * row_count + (source_block % pages_dev) * PAGE
    pages = jnp.stack([lax.dynamic_slice_in_dim(both_piece, stored[p], PAGE, 0) for p in range(pages_dev)])
    key_cache = pages[:, :, :key_cols].reshape(pages_dev, PAGE, kv_heads, head_dim).transpose(0, 2, 1, 3)
    value_cache = pages[:, :, key_cols:].reshape(pages_dev, PAGE, kv_heads, head_dim).transpose(0, 2, 1, 3)
    return (attention, key_cache, value_cache)


def solution(mesh):
    seq_size = mesh.shape["seq"]
    tp_size = mesh.shape["tp"]
    chips = seq_size // 2
    return jax.shard_map(
        partial(shards, chips, tp_size),
        mesh=mesh,
        in_specs=(
            P("seq", "tp"),
            P(),
            P("seq", "tp"),
            P("seq", "tp"),
            P("seq", "tp"),
            P(),
            P(),
            P(),
            P(),
        ),
        out_specs=(P("seq", "tp"), P("seq", "tp", None, None), P("seq", "tp", None, None)),
        check_vma=False,
    )
```
